32 devices in a mesh: row: 8 (over z, x), col: 4 (over y, core).
Axes of the slice: x: 2, y: 2, z: 4, core: 2. Of those that a mesh axis runs over, the one named last changes fastest.
Arguments:
- fine_blocks: bfloat16 [32, 16, 64, 576], P('row', 'col'), may hold values from -0.25 to 0.25
- fine_columns: int32 [32, 16, 9], P('row', 'col'), may hold values from 0 to 511, as said below
- fine_counts: int32 [32, 16], P('row', 'col'), may hold values from 1 to 9, as said below
- prolong_blocks: bfloat16 [32, 16, 64, 256], P('row', 'col'), may hold values from -1.1953125 to 1.1953125
- prolong_columns: int32 [32, 16, 4], P('row', 'col'), may hold values from 0 to 31, as said below
- prolong_counts: int32 [32, 16], P('row', 'col'), may hold values from 1 to 4, as said below
Outputs:
- galerkin: bfloat16 [8, 4, 64, 3136], P('row', 'col')
The draws below stay inside these ranges and needn't reach their ends.
Inputs may be any that keep to these rules, and one draw needn't show every extreme that they name: `fine_columns`: entry 0 of patch (x, y) is the patch itself; entries 1 to 8 are distinct directions among the eight patches at offsets of at most one along both dimensions, in an order drawn per patch, with coordinates clamped to the grid. `fine_counts`: the patch at the low corner of each 4 x 4 tile uses all 9 blocks. `prolong_columns`: entry 0 of patch (x, y) is its own aggregate (x // 4, y // 4); the other entries are distinct aggregates inside the grid at offsets of at most one from it along both dimensions. `prolong_counts`: the patch at the low corner of each 4 x 4 tile uses all 4 blocks.
All inputs are finite; a program needn't handle non-finite values.
Results may differ from the reference program's by a relative error of at most 0.0049.
Values may be sent and summed in bfloat16 or wider, within the bound.
No kernel may reach another device: no remote copies, remote signals or barrier semaphores. Data moves between devices by JAX's collectives and lax.ppermute only.
A program may use at most 128 MiB of HBM per device.

```python
import jax
import jax.numpy as jnp
from jax import lax

B = 64
KA = 9
KP = 4
AG = 4
PX = 4
PY = 4
FX = 32
FY = 16
CXG = 8
CYG = 4


neighbour_rows = (-1, -1, -1, 0, 0, 1, 1, 1)


neighbour_cols = (-1, 0, 1, -1, 1, -1, 0, 1)


def draw_fine_columns(key, part):
    grid_rows = jnp.arange(FX, dtype=jnp.int32)[:, None, None]
    grid_cols = jnp.arange(FY, dtype=jnp.int32)[None, :, None]
    scores = jax.random.randint(key, (FX, FY, 8), 0, 1 << 20, dtype=jnp.int32) * 8 + jnp.arange(8, dtype=jnp.int32)
    order = jnp.argsort(scores, axis=-1)[..., :KA - 1]
    target_row = jnp.clip(grid_rows + jnp.take(jnp.array(neighbour_rows, jnp.int32), order), 0, FX - 1)
    target_col = jnp.clip(grid_cols + jnp.take(jnp.array(neighbour_cols, jnp.int32), order), 0, FY - 1)
    itself = grid_rows * FY + grid_cols + jnp.zeros((FX, FY, 1), jnp.int32)
    return jnp.concatenate([itself, target_row * FY + target_col], axis=-1).astype(jnp.int32)


def corner_mask():
    return (jnp.arange(FX)[:, None] % PX == 0) & (jnp.arange(FY)[None, :] % PY == 0)


def draw_fine_counts(key, part):
    first_key, second_key = jax.random.split(key)
    level = jax.random.randint(first_key, (FX // PX, FY // PY), 1, KA + 1, dtype=jnp.int32)
    lowest = jnp.repeat(jnp.repeat(level, PX, axis=0), PY, axis=1)
    counts = jax.random.randint(second_key, (FX, FY), lowest, KA + 1, dtype=jnp.int32)
    return jnp.where(corner_mask(), KA, counts).astype(jnp.int32)


def draw_prolong_columns(key, part):
    agg_row = (jnp.arange(FX, dtype=jnp.int32) // AG)[:, None, None]
    agg_col = (jnp.arange(FY, dtype=jnp.int32) // AG)[None, :, None]
    step_rows = jnp.array(neighbour_rows, jnp.int32)
    step_cols = jnp.array(neighbour_cols, jnp.int32)
    reach_row = agg_row + step_rows
    reach_col = agg_col + step_cols
    inside = (reach_row >= 0) & (reach_row < CXG) & (reach_col >= 0) & (reach_col < CYG)
    scores = jax.random.randint(key, (FX, FY, 8), 0, 1 << 20, dtype=jnp.int32) * 8 + jnp.arange(8, dtype=jnp.int32)
    scores = scores + jnp.where(inside, 0, 1 << 24)
    order = jnp.argsort(scores, axis=-1)[..., :KP - 1]
    target_row = agg_row + jnp.take(step_rows, order)
    target_col = agg_col + jnp.take(step_cols, order)
    itself = agg_row * CYG + agg_col + jnp.zeros((FX, FY, 1), jnp.int32)
    return jnp.concatenate([itself, target_row * CYG + target_col], axis=-1).astype(jnp.int32)


def draw_prolong_counts(key, part):
    counts = jax.random.randint(key, (FX, FY), 1, KP + 1, dtype=jnp.int32)
    return jnp.where(corner_mask(), KP, counts).astype(jnp.int32)


def shard_levels(key, dims, shards, smallest, top_value):
    loudness, own = 1.0, jax.random.fold_in(key, 6)
    for axis_at, blocks in shards:
        draws = jnp.exp(jax.random.uniform(jax.random.fold_in(own, axis_at), (blocks,), jnp.float32, smallest / len(shards), top_value / len(shards)))
        loudness = loudness * jnp.repeat(draws, dims[axis_at] // blocks).reshape([-1 if axis == axis_at else 1 for axis in range(len(dims))])
    return loudness


def normal_values(own_key, shape, width, reach, cuts=(), held_as=jnp.bfloat16):
    drawn = jax.random.normal(own_key, shape, jnp.float32) * width
    if len(cuts) > 0:
        drawn = shard_levels(own_key, shape, cuts, -0.22, 0.18) * drawn
    return jnp.clip(drawn, min=-reach, max=reach).astype(held_as)


def setup_inputs(seed: int = 0) -> dict:
    seeds = jax.random.split(jax.random.key(seed), 7)
    return {
        "fine_blocks": normal_values(seeds[0], (FX, FY, B, KA * B), (KA * B) ** -0.5, 0.25, ((0, 8), (1, 4))),
        "fine_columns": draw_fine_columns(jax.random.fold_in(seeds[6], 71), 0),
        "fine_counts": draw_fine_counts(jax.random.fold_in(seeds[6], 71), 0),
        "prolong_blocks": normal_values(seeds[3], (FX, FY, B, KP * B), 0.2, 1.1953125, ((0, 8), (1, 4))),
        "prolong_columns": draw_prolong_columns(jax.random.fold_in(seeds[6], 71), 0),
        "prolong_counts": draw_prolong_counts(jax.random.fold_in(seeds[6], 71), 0),
    }


def regroup(values):
    rest = values.shape[2:]
    return values.reshape((AG, CYG, AG) + rest).swapaxes(0, 1).reshape((CYG, AG * AG) + rest)


def int_starts(values):
    return tuple(jnp.asarray(value, jnp.int32) for value in values)


def reference(fine_blocks, fine_columns, fine_counts, prolong_blocks, prolong_columns, prolong_counts):
    blocks = jnp.arange(KA, dtype=jnp.int32)
    entries = jnp.arange(KP, dtype=jnp.int32)
    fine_grid = jnp.where((blocks[None, None, :] < fine_counts[:, :, None])[:, :, None, :, None],
                          fine_blocks.reshape(FX, FY, B, KA, B), jnp.zeros((), jnp.bfloat16))
    prolong = jnp.where((entries[None, None, :] < prolong_counts[:, :, None])[:, :, None, :, None],
                        prolong_blocks.reshape(FX, FY, B, KP, B), jnp.zeros((), jnp.bfloat16))
    prolong_flat = prolong.reshape(FX * FY, B, KP, B)
    codes_flat = prolong_columns.reshape(FX * FY, KP)
    window = jnp.arange(25, dtype=jnp.int32)
    nearby = jnp.arange(9, dtype=jnp.int32)
    columns_of = jnp.arange(CYG, dtype=jnp.int32)

    def one_row(partial_value, agg_row):
        first_patch = agg_row * AG
        local_a = regroup(lax.dynamic_slice_in_dim(fine_grid, first_patch, AG, 0))
        targets = regroup(lax.dynamic_slice_in_dim(fine_columns, first_patch, AG, 0))
        near_p = jnp.take(prolong_flat, targets, axis=0)
        near_codes = jnp.take(codes_flat, targets, axis=0)
        term_blocks = jnp.einsum("gnakb,gnkbqc->gnkqac", local_a.astype(jnp.float32), near_p.astype(jnp.float32),
                                 precision=lax.Precision.HIGHEST)
        window_slot = (near_codes // CYG - agg_row + 2) * 5 + near_codes % CYG - columns_of[:, None, None, None] + 2
        select = (window_slot[..., None] == window).astype(jnp.float32)
        product = jnp.einsum("gnkqj,gnkqac->gnjac", select, term_blocks,
                             precision=lax.Precision.HIGHEST).astype(jnp.bfloat16)
        own_p = regroup(lax.dynamic_slice_in_dim(prolong, first_patch, AG, 0))
        own_codes = regroup(lax.dynamic_slice_in_dim(prolong_columns, first_patch, AG, 0))
        home_slot = (own_codes // CYG - agg_row + 1) * 3 + own_codes % CYG - columns_of[:, None, None] + 1
        spread = (home_slot[..., None] == nearby).astype(jnp.float32)
        dense_p = jnp.einsum("gnpi,gnbpc->gnibc", spread, own_p.astype(jnp.float32),
                             precision=lax.Precision.HIGHEST).astype(jnp.bfloat16)
        contrib = jnp.einsum("gniba,gnjbc->giajc", dense_p.astype(jnp.float32), product.astype(jnp.float32),
                             precision=lax.Precision.HIGHEST).reshape(CYG, 3, 3, B, 5, 5, B)
        for downward in range(3):
            for sideways in range(3):
                corner_at = int_starts((agg_row + downward, sideways, 0, 2 - downward, 2 - sideways, 0))
                current = lax.dynamic_slice(partial_value, corner_at, (1, CYG, B, 5, 5, B))
                partial_value = lax.dynamic_update_slice(partial_value, current + contrib[:, downward, sideways][None], corner_at)
        return partial_value, None

    partial_value = jnp.zeros((CXG + 2, CYG + 2, B, 7, 7, B), jnp.float32)
    partial_value, unused = lax.scan(one_row, partial_value, jnp.arange(CXG, dtype=jnp.int32))
    return partial_value[1:CXG + 1, 1:CYG + 1].reshape(CXG, CYG, B, 49 * B).astype(jnp.bfloat16)
```

```python
import jax
import jax.numpy as jnp
from jax import lax
from jax.experimental import pallas as pl
from jax.experimental.pallas import tpu as pltpu
from jax.sharding import PartitionSpec as P

B = 64
KA = 9
KP = 4
AG = 4

NEAR = 3
WIN = 5
HOME = 3
OUTW = 7
TRASH = WIN * WIN


def shifted(value, by_row, by_col):
    rows = lax.axis_size("row")
    cols = lax.axis_size("col")
    pairs = []
    for r in range(rows):
        for c in range(cols):
            tr, tc = r + by_row, c + by_col
            if 0 <= tr < rows and 0 <= tc < cols:
                pairs.append((r * cols + c, tr * cols + tc))
    return lax.ppermute(value, ("row", "col"), pairs)


def galerkin_kernel(pos_ref, slot_ref, a_ref, p_ref, dpt_ref, out_ref, acc_ref, prod_ref):
    patches = a_ref.shape[0]

    def one_patch(i, carry):
        acc_ref[...] = jnp.zeros(acc_ref.shape, jnp.float32)
        for k in range(KA):
            pos = pos_ref[i * KA + k]
            a_blk = a_ref[i, :, k * B:(k + 1) * B]
            term = jnp.dot(a_blk, p_ref[pos], preferred_element_type=jnp.float32)
            for q in range(KP):
                s = slot_ref[(i * KA + k) * KP + q]
                acc_ref[s] = acc_ref[s] + term[:, q * B:(q + 1) * B]
        row = pl.multiple_of(i * B, B)
        for w in range(WIN * WIN):
            prod_ref[pl.ds(row, B), w * B:(w + 1) * B] = acc_ref[w].astype(jnp.bfloat16)
        return carry

    lax.fori_loop(0, patches, one_patch, 0)
    out_ref[...] = jnp.dot(dpt_ref[...], prod_ref[...], preferred_element_type=jnp.float32)


def per_device(
    fine_blocks, fine_columns, fine_counts, prolong_blocks, prolong_columns, prolong_counts
):
    tile_rows, tile_cols = fine_counts.shape
    assert tile_rows == AG and tile_cols == AG
    patches = tile_rows * tile_cols
    grid_cols = tile_cols * lax.axis_size("col")
    coarse_grid_cols = lax.axis_size("col")
    row_index = lax.axis_index("row")
    col_index = lax.axis_index("col")

    entries = jnp.arange(KP, dtype=jnp.int32)
    kept = (entries[None, None, :] < prolong_counts[:, :, None])[:, :, None, :, None]
    prolong = jnp.where(
        kept, prolong_blocks.reshape(tile_rows, tile_cols, B, KP, B), jnp.zeros((), jnp.bfloat16)
    ).reshape(tile_rows, tile_cols, B, KP * B)

    hr, hc = tile_rows + 2, tile_cols + 2
    near_p = jnp.zeros((hr, hc, B, KP * B), jnp.bfloat16)
    near_codes = jnp.zeros((hr, hc, KP), jnp.int32)
    near_p = near_p.at[1:hr - 1, 1:hc - 1].set(prolong)
    near_codes = near_codes.at[1:hr - 1, 1:hc - 1].set(prolong_columns)
    for dr in (-1, 0, 1):
        for dc in (-1, 0, 1):
            if dr == 0 and dc == 0:
                continue
            rs = slice(0, tile_rows) if dr == 0 else (slice(0, 1) if dr == 1 else slice(tile_rows - 1, tile_rows))
            cs = slice(0, tile_cols) if dc == 0 else (slice(0, 1) if dc == 1 else slice(tile_cols - 1, tile_cols))
            got_p, got_c = shifted((prolong[rs, cs], prolong_columns[rs, cs]), -dr, -dc)
            drs = slice(1, hr - 1) if dr == 0 else (slice(hr - 1, hr) if dr == 1 else slice(0, 1))
            dcs = slice(1, hc - 1) if dc == 0 else (slice(hc - 1, hc) if dc == 1 else slice(0, 1))
            near_p = near_p.at[drs, dcs].set(got_p)
            near_codes = near_codes.at[drs, dcs].set(got_c)
    near_p = near_p.reshape(hr * hc, B, KP * B)
    near_codes = near_codes.reshape(hr * hc, KP)

    first_row = row_index * tile_rows
    first_col = col_index * tile_cols
    targets = fine_columns.reshape(patches, KA)
    pos = (targets // grid_cols - first_row + 1) * hc + targets % grid_cols - first_col + 1
    pos = jnp.clip(pos, 0, hr * hc - 1)
    codes = near_codes[pos]
    srow = jnp.clip(codes // coarse_grid_cols - row_index + 2, 0, WIN - 1)
    scol = jnp.clip(codes % coarse_grid_cols - col_index + 2, 0, WIN - 1)
    slot = srow * WIN + scol
    blocks = jnp.arange(KA, dtype=jnp.int32)
    used = blocks[None, :] < fine_counts.reshape(patches)[:, None]
    slot = jnp.where(used[:, :, None], slot, TRASH)

    own_codes = prolong_columns.reshape(patches, KP)
    hrow = jnp.clip(own_codes // coarse_grid_cols - row_index + 1, 0, HOME - 1)
    hcol = jnp.clip(own_codes % coarse_grid_cols - col_index + 1, 0, HOME - 1)
    home = hrow * HOME + hcol
    spread = (home[..., None] == jnp.arange(HOME * HOME, dtype=jnp.int32)).astype(jnp.bfloat16)
    dpt = jnp.einsum(
        "iph,ibpa->haib", spread, prolong.reshape(patches, B, KP, B),
        preferred_element_type=jnp.float32,
    ).astype(jnp.bfloat16).reshape(HOME * HOME * B, patches * B)

    smem = pltpu.MemorySpace.SMEM if hasattr(pltpu, "MemorySpace") else pltpu.SMEM
    contrib = pl.pallas_call(
        galerkin_kernel,
        out_shape=jax.ShapeDtypeStruct((HOME * HOME * B, WIN * WIN * B), jnp.float32),
        in_specs=[
            pl.BlockSpec(memory_space=smem),
            pl.BlockSpec(memory_space=smem),
            pl.BlockSpec(memory_space=pltpu.VMEM),
            pl.BlockSpec(memory_space=pltpu.VMEM),
            pl.BlockSpec(memory_space=pltpu.VMEM),
        ],
        out_specs=pl.BlockSpec(memory_space=pltpu.VMEM),
        scratch_shapes=[
            pltpu.VMEM((TRASH + 1, B, B), jnp.float32),
            pltpu.VMEM((patches * B, WIN * WIN * B), jnp.bfloat16),
        ],
    )(
        pos.reshape(-1).astype(jnp.int32),
        slot.reshape(-1).astype(jnp.int32),
        fine_blocks.reshape(patches, B, KA * B),
        near_p,
        dpt,
    )
    contrib = contrib.reshape(HOME, HOME, B, WIN, WIN, B)

    total = jnp.zeros((B, OUTW, OUTW, B), jnp.float32)
    for dr in (-1, 0, 1):
        for dc in (-1, 0, 1):
            block = contrib[dr + 1, dc + 1]
            if dr != 0 or dc != 0:
                block = shifted(block, dr, dc)
            total = total + jnp.pad(
                block, ((0, 0), (1 - dr, 1 + dr), (1 - dc, 1 + dc), (0, 0))
            )
    return total.astype(jnp.bfloat16).reshape(1, 1, B, OUTW * OUTW * B)


def solution(mesh):
    in_specs = (
        P("row", "col", None, None),
        P("row", "col", None),
        P("row", "col"),
        P("row", "col", None, None),
        P("row", "col", None),
        P("row", "col"),
    )
    out_specs = P("row", "col", None, None)
    return jax.shard_map(
        per_device, mesh=mesh, in_specs=in_specs, out_specs=out_specs, check_vma=False
    )
```

```python
import jax
import jax.numpy as jnp
from jax import lax
from jax.experimental import pallas as pl
from jax.experimental.pallas import tpu as pltpu
from jax.sharding import PartitionSpec as P

B = 64
KA = 9
KP = 4
AG = 4

NEAR = 3
WIN = 5
HOME = 3
OUTW = 7
TRASH = WIN * WIN
SEND = jnp.float32


def shifted(value, by_row, by_col):
    rows = lax.axis_size("row")
    cols = lax.axis_size("col")
    pairs = []
    for r in range(rows):
        for c in range(cols):
            tr, tc = r + by_row, c + by_col
            if 0 <= tr < rows and 0 <= tc < cols:
                pairs.append((r * cols + c, tr * cols + tc))
    return lax.ppermute(value, ("row", "col"), pairs)


def galerkin_kernel(pos_ref, slot_ref, a_ref, p_ref, dpt_ref, keep_ref, send_ref, acc_ref, prod_ref):
    patches = a_ref.shape[0]

    def one_patch(i, carry):
        acc_ref[...] = jnp.zeros(acc_ref.shape, jnp.float32)
        for k in range(KA):
            pos = pos_ref[i * KA + k]
            a_blk = a_ref[i, :, k * B:(k + 1) * B]
            term = jnp.dot(a_blk, p_ref[pos], preferred_element_type=jnp.float32)
            for q in range(KP):
                s = slot_ref[(i * KA + k) * KP + q]
                acc_ref[s] = acc_ref[s] + term[:, q * B:(q + 1) * B]
        row = pl.multiple_of(i * B, B)
        for w in range(WIN * WIN):
            prod_ref[pl.ds(row, B), w * B:(w + 1) * B] = acc_ref[w].astype(jnp.bfloat16)
        return carry

    lax.fori_loop(0, patches, one_patch, 0)
    rows = HOME * B
    keep_ref[...] = jnp.dot(dpt_ref[rows:2 * rows], prod_ref[...], preferred_element_type=jnp.float32)
    for side, start in ((0, 0), (1, 2 * rows)):
        send_ref[side] = jnp.dot(
            dpt_ref[start:start + rows], prod_ref[...], preferred_element_type=jnp.float32
        ).astype(send_ref.dtype)


def fold_cols_kernel(keep_ref, left_ref, right_ref, keep_out, send_out):
    for d in range(HOME):
        for sx in range(WIN):
            for t in range(OUTW):
                parts = []
                if 1 <= t <= WIN:
                    u = t - 1
                    parts.append(keep_ref[d, :, (sx * WIN + u) * B:(sx * WIN + u + 1) * B])
                if t <= WIN - 1:
                    parts.append(left_ref[d, :, (sx * WIN + t) * B:(sx * WIN + t + 1) * B].astype(jnp.float32))
                if t >= 2:
                    u = t - 2
                    parts.append(right_ref[d, :, (sx * WIN + u) * B:(sx * WIN + u + 1) * B].astype(jnp.float32))
                total = parts[0]
                for extra in parts[1:]:
                    total = total + extra
                lo = (sx * OUTW + t) * B
                if d == 1:
                    keep_out[:, lo:lo + B] = total
                else:
                    send_out[d // 2, :, lo:lo + B] = total.astype(send_out.dtype)


def fold_rows_kernel(keep_ref, up_ref, down_ref, out_ref):
    band = OUTW * B
    for s in range(OUTW):
        parts = []
        if 1 <= s <= WIN:
            parts.append(keep_ref[:, (s - 1) * band:s * band])
        if s <= WIN - 1:
            parts.append(up_ref[:, s * band:(s + 1) * band].astype(jnp.float32))
        if s >= 2:
            parts.append(down_ref[:, (s - 2) * band:(s - 1) * band].astype(jnp.float32))
        total = parts[0]
        for extra in parts[1:]:
            total = total + extra
        out_ref[:, s * band:(s + 1) * band] = total.astype(out_ref.dtype)


def per_device(
    fine_blocks, fine_columns, fine_counts, prolong_blocks, prolong_columns, prolong_counts
):
    tile_rows, tile_cols = fine_counts.shape
    assert tile_rows == AG and tile_cols == AG
    patches = tile_rows * tile_cols
    grid_cols = tile_cols * lax.axis_size("col")
    coarse_grid_cols = lax.axis_size("col")
    row_index = lax.axis_index("row")
    col_index = lax.axis_index("col")

    entries = jnp.arange(KP, dtype=jnp.int32)
    kept = (entries[None, None, :] < prolong_counts[:, :, None])[:, :, None, :, None]
    prolong = jnp.where(
        kept, prolong_blocks.reshape(tile_rows, tile_cols, B, KP, B), jnp.zeros((), jnp.bfloat16)
    ).reshape(tile_rows, tile_cols, B, KP * B)

    hr, hc = tile_rows + 2, tile_cols + 2
    from_above = shifted(prolong[tile_rows - 1:], 1, 0)
    from_below = shifted(prolong[:1], -1, 0)
    tall = jnp.concatenate([from_above, prolong, from_below], axis=0)
    from_left = shifted(tall[:, tile_cols - 1:], 0, 1)
    from_right = shifted(tall[:, :1], 0, -1)
    near_p = jnp.concatenate([from_left, tall, from_right], axis=1).reshape(hr * hc, B, KP * B)

    all_codes = lax.all_gather(prolong_columns, ("row", "col"), axis=0, tiled=False)
    rows_n, cols_n = lax.axis_size("row"), lax.axis_size("col")
    all_codes = all_codes.reshape(rows_n, cols_n, tile_rows, tile_cols, KP)
    all_codes = all_codes.transpose(0, 2, 1, 3, 4).reshape(rows_n * tile_rows * cols_n * tile_cols, KP)

    first_row = row_index * tile_rows
    first_col = col_index * tile_cols
    targets = fine_columns.reshape(patches, KA)
    pos = (targets // grid_cols - first_row + 1) * hc + targets % grid_cols - first_col + 1
    pos = jnp.clip(pos, 0, hr * hc - 1)
    codes = all_codes[jnp.clip(targets, 0, all_codes.shape[0] - 1)]
    srow = jnp.clip(codes // coarse_grid_cols - row_index + 2, 0, WIN - 1)
    scol = jnp.clip(codes % coarse_grid_cols - col_index + 2, 0, WIN - 1)
    slot = srow * WIN + scol
    blocks = jnp.arange(KA, dtype=jnp.int32)
    used = blocks[None, :] < fine_counts.reshape(patches)[:, None]
    slot = jnp.where(used[:, :, None], slot, TRASH)

    own_codes = prolong_columns.reshape(patches, KP)
    hrow = jnp.clip(own_codes // coarse_grid_cols - row_index + 1, 0, HOME - 1)
    hcol = jnp.clip(own_codes % coarse_grid_cols - col_index + 1, 0, HOME - 1)
    home = hcol * HOME + hrow
    spread = (home[..., None] == jnp.arange(HOME * HOME, dtype=jnp.int32)).astype(jnp.bfloat16)
    dpt = jnp.einsum(
        "iph,ibpa->haib", spread, prolong.reshape(patches, B, KP, B),
        preferred_element_type=jnp.float32,
    ).astype(jnp.bfloat16).reshape(HOME * HOME * B, patches * B)

    smem = pltpu.MemorySpace.SMEM
    vmem = pltpu.MemorySpace.VMEM
    width = WIN * WIN * B
    keep, send = pl.pallas_call(
        galerkin_kernel,
        out_shape=(
            jax.ShapeDtypeStruct((HOME * B, width), jnp.float32),
            jax.ShapeDtypeStruct((2, HOME * B, width), SEND),
        ),
        in_specs=[
            pl.BlockSpec(memory_space=smem),
            pl.BlockSpec(memory_space=smem),
            pl.BlockSpec(memory_space=vmem),
            pl.BlockSpec(memory_space=vmem),
            pl.BlockSpec(memory_space=vmem),
        ],
        out_specs=(pl.BlockSpec(memory_space=vmem), pl.BlockSpec(memory_space=vmem)),
        scratch_shapes=[
            pltpu.VMEM((TRASH + 1, B, B), jnp.float32),
            pltpu.VMEM((patches * B, width), jnp.bfloat16),
        ],
    )(
        pos.reshape(-1).astype(jnp.int32),
        slot.reshape(-1).astype(jnp.int32),
        fine_blocks.reshape(patches, B, KA * B),
        near_p,
        dpt,
    )
    left_in = shifted(send[1].reshape(HOME, B, width), 0, 1)
    right_in = shifted(send[0].reshape(HOME, B, width), 0, -1)
    band = WIN * OUTW * B
    keep2, send2 = pl.pallas_call(
        fold_cols_kernel,
        out_shape=(
            jax.ShapeDtypeStruct((B, band), jnp.float32),
            jax.ShapeDtypeStruct((2, B, band), SEND),
        ),
        in_specs=[pl.BlockSpec(memory_space=vmem)] * 3,
        out_specs=(pl.BlockSpec(memory_space=vmem), pl.BlockSpec(memory_space=vmem)),
    )(keep.reshape(HOME, B, width), left_in, right_in)
    up_in = shifted(send2[1], 1, 0)
    down_in = shifted(send2[0], -1, 0)
    out = pl.pallas_call(
        fold_rows_kernel,
        out_shape=jax.ShapeDtypeStruct((B, OUTW * OUTW * B), jnp.bfloat16),
        in_specs=[pl.BlockSpec(memory_space=vmem)] * 3,
        out_specs=pl.BlockSpec(memory_space=vmem),
    )(keep2, up_in, down_in)
    return out.reshape(1, 1, B, OUTW * OUTW * B)


def solution(mesh):
    in_specs = (
        P("row", "col", None, None),
        P("row", "col", None),
        P("row", "col"),
        P("row", "col", None, None),
        P("row", "col", None),
        P("row", "col"),
    )
    out_specs = P("row", "col", None, None)
    return jax.shard_map(
        per_device, mesh=mesh, in_specs=in_specs, out_specs=out_specs, check_vma=False
    )
```

```python
import jax
import jax.numpy as jnp
from jax import lax
from jax.experimental import pallas as pl
from jax.experimental.pallas import tpu as pltpu
from jax.sharding import PartitionSpec as P

B = 64
KA = 9
KP = 4
AG = 4

NEAR = 3
WIN = 5
HOME = 3
OUTW = 7
TRASH = WIN * WIN
SEND = jnp.float32


def shifted(value, by_row, by_col):
    rows = lax.axis_size("row")
    cols = lax.axis_size("col")
    pairs = []
    for r in range(rows):
        for c in range(cols):
            tr, tc = r + by_row, c + by_col
            if 0 <= tr < rows and 0 <= tc < cols:
                pairs.append((r * cols + c, tr * cols + tc))
    return lax.ppermute(value, ("row", "col"), pairs)


def galerkin_kernel(pos_ref, slot_ref, home_ref, a_ref, p_ref, own_ref, keep_ref, send_ref,
                    acc_ref, prod_ref, dp_ref):
    patches = a_ref.shape[0]

    def one_patch(i, carry):
        acc_ref[...] = jnp.zeros(acc_ref.shape, jnp.float32)
        for k in range(KA):
            pos = pos_ref[i * KA + k]
            a_blk = a_ref[i, :, k * B:(k + 1) * B]
            term = jnp.dot(a_blk, p_ref[pos], preferred_element_type=jnp.float32)
            for q in range(KP):
                s = slot_ref[(i * KA + k) * KP + q]
                acc_ref[s] = acc_ref[s] + term[:, q * B:(q + 1) * B]
        row = pl.multiple_of(i * B, B)
        for w in range(WIN * WIN):
            prod_ref[pl.ds(row, B), w * B:(w + 1) * B] = acc_ref[w].astype(jnp.bfloat16)
        for p in range(KP):
            h = home_ref[i * KP + p]
            dp_ref[h, pl.ds(row, B), :] = dp_ref[h, pl.ds(row, B), :] + own_ref[i, :, p * B:(p + 1) * B].astype(jnp.float32)
        return carry

    dp_ref[...] = jnp.zeros(dp_ref.shape, jnp.float32)
    lax.fori_loop(0, patches, one_patch, 0)
    prod = prod_ref[...]
    dims = (((0,), (0,)), ((), ()))

    def coarse_terms(h):
        return lax.dot_general(dp_ref[h].astype(jnp.bfloat16), prod, dims, preferred_element_type=jnp.float32)

    for dr in range(HOME):
        keep_ref[dr] = coarse_terms(HOME + dr)
        send_ref[0, dr] = coarse_terms(dr).astype(send_ref.dtype)
        send_ref[1, dr] = coarse_terms(2 * HOME + dr).astype(send_ref.dtype)


def fold_cols_kernel(keep_ref, left_ref, right_ref, keep_out, send_out):
    for d in range(HOME):
        for sx in range(WIN):
            for t in range(OUTW):
                parts = []
                if 1 <= t <= WIN:
                    u = t - 1
                    parts.append(keep_ref[d, :, (sx * WIN + u) * B:(sx * WIN + u + 1) * B])
                if t <= WIN - 1:
                    parts.append(left_ref[d, :, (sx * WIN + t) * B:(sx * WIN + t + 1) * B].astype(jnp.float32))
                if t >= 2:
                    u = t - 2
                    parts.append(right_ref[d, :, (sx * WIN + u) * B:(sx * WIN + u + 1) * B].astype(jnp.float32))
                total = parts[0]
                for extra in parts[1:]:
                    total = total + extra
                lo = (sx * OUTW + t) * B
                if d == 1:
                    keep_out[:, lo:lo + B] = total
                else:
                    send_out[d // 2, :, lo:lo + B] = total.astype(send_out.dtype)


def fold_rows_kernel(keep_ref, up_ref, down_ref, out_ref):
    band = OUTW * B
    for s in range(OUTW):
        parts = []
        if 1 <= s <= WIN:
            parts.append(keep_ref[:, (s - 1) * band:s * band])
        if s <= WIN - 1:
            parts.append(up_ref[:, s * band:(s + 1) * band].astype(jnp.float32))
        if s >= 2:
            parts.append(down_ref[:, (s - 2) * band:(s - 1) * band].astype(jnp.float32))
        total = parts[0]
        for extra in parts[1:]:
            total = total + extra
        out_ref[:, s * band:(s + 1) * band] = total.astype(out_ref.dtype)


def per_device(
    fine_blocks, fine_columns, fine_counts, prolong_blocks, prolong_columns, prolong_counts
):
    tile_rows, tile_cols = fine_counts.shape
    assert tile_rows == AG and tile_cols == AG
    patches = tile_rows * tile_cols
    grid_cols = tile_cols * lax.axis_size("col")
    coarse_grid_cols = lax.axis_size("col")
    row_index = lax.axis_index("row")
    col_index = lax.axis_index("col")

    entries = jnp.arange(KP, dtype=jnp.int32)
    kept = (entries[None, None, :] < prolong_counts[:, :, None])[:, :, None, :, None]
    prolong = jnp.where(
        kept, prolong_blocks.reshape(tile_rows, tile_cols, B, KP, B), jnp.zeros((), jnp.bfloat16)
    ).reshape(tile_rows, tile_cols, B, KP * B)

    own_codes = prolong_columns.reshape(patches, KP)
    hrow = jnp.clip(own_codes // coarse_grid_cols - row_index + 1, 0, HOME - 1)
    hcol = jnp.clip(own_codes % coarse_grid_cols - col_index + 1, 0, HOME - 1)
    rel = (hrow * HOME + hcol).reshape(tile_rows, tile_cols, KP)

    def payload(p_part, rel_part):
        count = p_part.shape[0]
        flat = p_part.reshape(count * B, KP * B)
        extra = jnp.zeros((16, KP * B), jnp.bfloat16)
        extra = extra.at[0, :count * KP].set(rel_part.reshape(-1).astype(jnp.bfloat16))
        return jnp.concatenate([flat, extra], axis=0)

    def unpack(got, count):
        p_part = got[:count * B].reshape(count, B, KP * B)
        rel_part = got[count * B, :count * KP].astype(jnp.int32).reshape(count, KP)
        return p_part, rel_part

    hr, hc = tile_rows + 2, tile_cols + 2
    above, above_rel = unpack(shifted(payload(prolong[tile_rows - 1], rel[tile_rows - 1]), 1, 0), tile_cols)
    below, below_rel = unpack(shifted(payload(prolong[0], rel[0]), -1, 0), tile_cols)
    tall = jnp.concatenate([above[None], prolong, below[None]], axis=0)
    tall_rel = jnp.concatenate([above_rel[None], rel, below_rel[None]], axis=0)
    left, left_rel = unpack(shifted(payload(tall[:, tile_cols - 1], tall_rel[:, tile_cols - 1]), 0, 1), hr)
    right, right_rel = unpack(shifted(payload(tall[:, 0], tall_rel[:, 0]), 0, -1), hr)
    near_p = jnp.concatenate([left[:, None], tall, right[:, None]], axis=1).reshape(hr * hc, B, KP * B)
    near_rel = jnp.concatenate([left_rel[:, None], tall_rel, right_rel[:, None]], axis=1)

    off_r = (jnp.arange(hr, dtype=jnp.int32) + tile_rows - 1) // tile_rows - 1
    off_c = (jnp.arange(hc, dtype=jnp.int32) + tile_cols - 1) // tile_cols - 1
    near_slot = (near_rel // HOME + off_r[:, None, None] + 1) * WIN + near_rel % HOME + off_c[None, :, None] + 1
    near_slot = near_slot.reshape(hr * hc, KP)

    first_row = row_index * tile_rows
    first_col = col_index * tile_cols
    targets = fine_columns.reshape(patches, KA)
    pos = (targets // grid_cols - first_row + 1) * hc + targets % grid_cols - first_col + 1
    pos = jnp.clip(pos, 0, hr * hc - 1)
    slot = near_slot[pos]
    blocks = jnp.arange(KA, dtype=jnp.int32)
    used = blocks[None, :] < fine_counts.reshape(patches)[:, None]
    slot = jnp.where(used[:, :, None], slot, TRASH)
    home = hcol * HOME + hrow

    smem = pltpu.MemorySpace.SMEM
    vmem = pltpu.MemorySpace.VMEM
    width = WIN * WIN * B
    keep, send = pl.pallas_call(
        galerkin_kernel,
        out_shape=(
            jax.ShapeDtypeStruct((HOME, B, width), jnp.float32),
            jax.ShapeDtypeStruct((2, HOME, B, width), SEND),
        ),
        in_specs=[
            pl.BlockSpec(memory_space=smem),
            pl.BlockSpec(memory_space=smem),
            pl.BlockSpec(memory_space=smem),
            pl.BlockSpec(memory_space=vmem),
            pl.BlockSpec(memory_space=vmem),
            pl.BlockSpec(memory_space=vmem),
        ],
        out_specs=(pl.BlockSpec(memory_space=vmem), pl.BlockSpec(memory_space=vmem)),
        scratch_shapes=[
            pltpu.VMEM((TRASH + 1, B, B), jnp.float32),
            pltpu.VMEM((patches * B, width), jnp.bfloat16),
            pltpu.VMEM((HOME * HOME, patches * B, B), jnp.float32),
        ],
    )(
        pos.reshape(-1).astype(jnp.int32),
        slot.reshape(-1).astype(jnp.int32),
        home.reshape(-1).astype(jnp.int32),
        fine_blocks.reshape(patches, B, KA * B),
        near_p,
        prolong.reshape(patches, B, KP * B),
    )
    left_in = shifted(send[1], 0, 1)
    right_in = shifted(send[0], 0, -1)
    band = WIN * OUTW * B
    keep2, send2 = pl.pallas_call(
        fold_cols_kernel,
        out_shape=(
            jax.ShapeDtypeStruct((B, band), jnp.float32),
            jax.ShapeDtypeStruct((2, B, band), SEND),
        ),
        in_specs=[pl.BlockSpec(memory_space=vmem)] * 3,
        out_specs=(pl.BlockSpec(memory_space=vmem), pl.BlockSpec(memory_space=vmem)),
    )(keep, left_in, right_in)
    up_in = shifted(send2[1], 1, 0)
    down_in = shifted(send2[0], -1, 0)
    out = pl.pallas_call(
        fold_rows_kernel,
        out_shape=jax.ShapeDtypeStruct((B, OUTW * OUTW * B), jnp.bfloat16),
        in_specs=[pl.BlockSpec(memory_space=vmem)] * 3,
        out_specs=pl.BlockSpec(memory_space=vmem),
    )(keep2, up_in, down_in)
    return out.reshape(1, 1, B, OUTW * OUTW * B)


def solution(mesh):
    in_specs = (
        P("row", "col", None, None),
        P("row", "col", None),
        P("row", "col"),
        P("row", "col", None, None),
        P("row", "col", None),
        P("row", "col"),
    )
    out_specs = P("row", "col", None, None)
    return jax.shard_map(
        per_device, mesh=mesh, in_specs=in_specs, out_specs=out_specs, check_vma=False
    )
```

```python
import jax
import jax.numpy as jnp
from jax import lax
from jax.experimental import pallas as pl
from jax.experimental.pallas import tpu as pltpu
from jax.sharding import PartitionSpec as P

B = 64
KA = 9
KP = 4
AG = 4

NEAR = 3
WIN = 5
HOME = 3
OUTW = 7
TRASH = WIN * WIN
SEND = jnp.bfloat16


def shifted(value, by_row, by_col):
    rows = lax.axis_size("row")
    cols = lax.axis_size("col")
    pairs = []
    for r in range(rows):
        for c in range(cols):
            tr, tc = r + by_row, c + by_col
            if 0 <= tr < rows and 0 <= tc < cols:
                pairs.append((r * cols + c, tr * cols + tc))
    return lax.ppermute(value, ("row", "col"), pairs)


def galerkin_kernel(pos_ref, slot_ref, home_ref, a_ref, p_ref, own_ref, keep_ref, send_ref,
                    acc_ref, prod_ref, dp_ref):
    patches = a_ref.shape[0]

    def one_patch(i, carry):
        acc_ref[...] = jnp.zeros(acc_ref.shape, jnp.float32)
        for k in range(KA):
            pos = pos_ref[i * KA + k]
            a_blk = a_ref[i, :, k * B:(k + 1) * B]
            term = jnp.dot(a_blk, p_ref[pos], preferred_element_type=jnp.float32)
            for q in range(KP):
                s = slot_ref[(i * KA + k) * KP + q]
                acc_ref[s] = acc_ref[s] + term[:, q * B:(q + 1) * B]
        row = pl.multiple_of(i * B, B)
        for w in range(WIN * WIN):
            prod_ref[pl.ds(row, B), w * B:(w + 1) * B] = acc_ref[w].astype(jnp.bfloat16)
        for p in range(KP):
            h = home_ref[i * KP + p]
            dp_ref[h, pl.ds(row, B), :] = dp_ref[h, pl.ds(row, B), :] + own_ref[i, :, p * B:(p + 1) * B].astype(jnp.float32)
        return carry

    dp_ref[...] = jnp.zeros(dp_ref.shape, jnp.float32)
    lax.fori_loop(0, patches, one_patch, 0)
    prod = prod_ref[...]
    dims = (((0,), (0,)), ((), ()))

    def coarse_terms(h):
        return lax.dot_general(dp_ref[h].astype(jnp.bfloat16), prod, dims, preferred_element_type=jnp.float32)

    for dr in range(HOME):
        keep_ref[dr] = coarse_terms(HOME + dr)
        send_ref[0, dr] = coarse_terms(dr).astype(send_ref.dtype)
        send_ref[1, dr] = coarse_terms(2 * HOME + dr).astype(send_ref.dtype)


def fold_cols_kernel(keep_ref, left_ref, right_ref, keep_out, send_out):
    for d in range(HOME):
        for sx in range(WIN):
            for t in range(OUTW):
                parts = []
                if 1 <= t <= WIN:
                    u = t - 1
                    parts.append(keep_ref[d, :, (sx * WIN + u) * B:(sx * WIN + u + 1) * B])
                if t <= WIN - 1:
                    parts.append(left_ref[d, :, (sx * WIN + t) * B:(sx * WIN + t + 1) * B].astype(jnp.float32))
                if t >= 2:
                    u = t - 2
                    parts.append(right_ref[d, :, (sx * WIN + u) * B:(sx * WIN + u + 1) * B].astype(jnp.float32))
                total = parts[0]
                for extra in parts[1:]:
                    total = total + extra
                lo = (sx * OUTW + t) * B
                if d == 1:
                    keep_out[:, lo:lo + B] = total
                else:
                    send_out[d // 2, :, lo:lo + B] = total.astype(send_out.dtype)


def fold_rows_kernel(keep_ref, up_ref, down_ref, out_ref):
    band = OUTW * B
    for s in range(OUTW):
        parts = []
        if 1 <= s <= WIN:
            parts.append(keep_ref[:, (s - 1) * band:s * band])
        if s <= WIN - 1:
            parts.append(up_ref[:, s * band:(s + 1) * band].astype(jnp.float32))
        if s >= 2:
            parts.append(down_ref[:, (s - 2) * band:(s - 1) * band].astype(jnp.float32))
        total = parts[0]
        for extra in parts[1:]:
            total = total + extra
        out_ref[:, s * band:(s + 1) * band] = total.astype(out_ref.dtype)


def per_device(
    fine_blocks, fine_columns, fine_counts, prolong_blocks, prolong_columns, prolong_counts
):
    tile_rows, tile_cols = fine_counts.shape
    assert tile_rows == AG and tile_cols == AG
    patches = tile_rows * tile_cols
    grid_cols = tile_cols * lax.axis_size("col")
    coarse_grid_cols = lax.axis_size("col")
    row_index = lax.axis_index("row")
    col_index = lax.axis_index("col")

    entries = jnp.arange(KP, dtype=jnp.int32)
    kept = (entries[None, None, :] < prolong_counts[:, :, None])[:, :, None, :, None]
    prolong = jnp.where(
        kept, prolong_blocks.reshape(tile_rows, tile_cols, B, KP, B), jnp.zeros((), jnp.bfloat16)
    ).reshape(tile_rows, tile_cols, B, KP * B)

    own_codes = prolong_columns.reshape(patches, KP)
    hrow = jnp.clip(own_codes // coarse_grid_cols - row_index + 1, 0, HOME - 1)
    hcol = jnp.clip(own_codes % coarse_grid_cols - col_index + 1, 0, HOME - 1)
    rel = (hrow * HOME + hcol).reshape(tile_rows, tile_cols, KP)

    def payload(p_part, rel_part):
        count = p_part.shape[0]
        flat = p_part.reshape(count * B, KP * B)
        extra = jnp.zeros((16, KP * B), jnp.bfloat16)
        extra = extra.at[0, :count * KP].set(rel_part.reshape(-1).astype(jnp.bfloat16))
        return jnp.concatenate([flat, extra], axis=0)

    def unpack(got, count):
        p_part = got[:count * B].reshape(count, B, KP * B)
        rel_part = got[count * B, :count * KP].astype(jnp.int32).reshape(count, KP)
        return p_part, rel_part

    hr, hc = tile_rows + 2, tile_cols + 2
    above, above_rel = unpack(shifted(payload(prolong[tile_rows - 1], rel[tile_rows - 1]), 1, 0), tile_cols)
    below, below_rel = unpack(shifted(payload(prolong[0], rel[0]), -1, 0), tile_cols)
    tall = jnp.concatenate([above[None], prolong, below[None]], axis=0)
    tall_rel = jnp.concatenate([above_rel[None], rel, below_rel[None]], axis=0)
    left, left_rel = unpack(shifted(payload(tall[:, tile_cols - 1], tall_rel[:, tile_cols - 1]), 0, 1), hr)
    right, right_rel = unpack(shifted(payload(tall[:, 0], tall_rel[:, 0]), 0, -1), hr)
    near_p = jnp.concatenate([left[:, None], tall, right[:, None]], axis=1).reshape(hr * hc, B, KP * B)
    near_rel = jnp.concatenate([left_rel[:, None], tall_rel, right_rel[:, None]], axis=1)

    off_r = (jnp.arange(hr, dtype=jnp.int32) + tile_rows - 1) // tile_rows - 1
    off_c = (jnp.arange(hc, dtype=jnp.int32) + tile_cols - 1) // tile_cols - 1
    near_slot = (near_rel // HOME + off_r[:, None, None] + 1) * WIN + near_rel % HOME + off_c[None, :, None] + 1
    near_slot = near_slot.reshape(hr * hc, KP)

    first_row = row_index * tile_rows
    first_col = col_index * tile_cols
    targets = fine_columns.reshape(patches, KA)
    pos = (targets // grid_cols - first_row + 1) * hc + targets % grid_cols - first_col + 1
    pos = jnp.clip(pos, 0, hr * hc - 1)
    slot = near_slot[pos]
    blocks = jnp.arange(KA, dtype=jnp.int32)
    used = blocks[None, :] < fine_counts.reshape(patches)[:, None]
    slot = jnp.where(used[:, :, None], slot, TRASH)
    home = hcol * HOME + hrow

    smem = pltpu.MemorySpace.SMEM
    vmem = pltpu.MemorySpace.VMEM
    width = WIN * WIN * B
    keep, send = pl.pallas_call(
        galerkin_kernel,
        out_shape=(
            jax.ShapeDtypeStruct((HOME, B, width), jnp.float32),
            jax.ShapeDtypeStruct((2, HOME, B, width), SEND),
        ),
        in_specs=[
            pl.BlockSpec(memory_space=smem),
            pl.BlockSpec(memory_space=smem),
            pl.BlockSpec(memory_space=smem),
            pl.BlockSpec(memory_space=vmem),
            pl.BlockSpec(memory_space=vmem),
            pl.BlockSpec(memory_space=vmem),
        ],
        out_specs=(pl.BlockSpec(memory_space=vmem), pl.BlockSpec(memory_space=vmem)),
        scratch_shapes=[
            pltpu.VMEM((TRASH + 1, B, B), jnp.float32),
            pltpu.VMEM((patches * B, width), jnp.bfloat16),
            pltpu.VMEM((HOME * HOME, patches * B, B), jnp.float32),
        ],
    )(
        pos.reshape(-1).astype(jnp.int32),
        slot.reshape(-1).astype(jnp.int32),
        home.reshape(-1).astype(jnp.int32),
        fine_blocks.reshape(patches, B, KA * B),
        near_p,
        prolong.reshape(patches, B, KP * B),
    )
    left_in = shifted(send[1], 0, 1)
    right_in = shifted(send[0], 0, -1)
    band = WIN * OUTW * B
    keep2, send2 = pl.pallas_call(
        fold_cols_kernel,
        out_shape=(
            jax.ShapeDtypeStruct((B, band), jnp.float32),
            jax.ShapeDtypeStruct((2, B, band), SEND),
        ),
        in_specs=[pl.BlockSpec(memory_space=vmem)] * 3,
        out_specs=(pl.BlockSpec(memory_space=vmem), pl.BlockSpec(memory_space=vmem)),
    )(keep, left_in, right_in)
    up_in = shifted(send2[1], 1, 0)
    down_in = shifted(send2[0], -1, 0)
    out = pl.pallas_call(
        fold_rows_kernel,
        out_shape=jax.ShapeDtypeStruct((B, OUTW * OUTW * B), jnp.bfloat16),
        in_specs=[pl.BlockSpec(memory_space=vmem)] * 3,
        out_specs=pl.BlockSpec(memory_space=vmem),
    )(keep2, up_in, down_in)
    return out.reshape(1, 1, B, OUTW * OUTW * B)


def solution(mesh):
    in_specs = (
        P("row", "col", None, None),
        P("row", "col", None),
        P("row", "col"),
        P("row", "col", None, None),
        P("row", "col", None),
        P("row", "col"),
    )
    out_specs = P("row", "col", None, None)
    return jax.shard_map(
        per_device, mesh=mesh, in_specs=in_specs, out_specs=out_specs, check_vma=False
    )
```

```python
import jax
import jax.numpy as jnp
from jax import lax
from jax.experimental import pallas as pl
from jax.experimental.pallas import tpu as pltpu
from jax.sharding import PartitionSpec as P

B = 64
KA = 9
KP = 4
AG = 4

NEAR = 3
WIN = 5
HOME = 3
OUTW = 7
TRASH = WIN * WIN
SEND = jnp.bfloat16


def shifted(value, by_row, by_col):
    rows = lax.axis_size("row")
    cols = lax.axis_size("col")
    pairs = []
    for r in range(rows):
        for c in range(cols):
            tr, tc = r + by_row, c + by_col
            if 0 <= tr < rows and 0 <= tc < cols:
                pairs.append((r * cols + c, tr * cols + tc))
    return lax.ppermute(value, ("row", "col"), pairs)


def galerkin_kernel(pos_ref, slot_ref, home_ref, a_ref, p_ref, own_ref, keep_ref, send_ref,
                    acc_ref, prod_ref, dp_ref):
    patches = a_ref.shape[0]

    def one_patch(i, carry):
        acc_ref[...] = jnp.zeros(acc_ref.shape, jnp.float32)
        for k in range(KA):
            pos = pos_ref[i * KA + k]
            a_blk = a_ref[i, :, k * B:(k + 1) * B]
            term = jnp.dot(a_blk, p_ref[pos], preferred_element_type=jnp.float32)
            for q in range(KP):
                s = slot_ref[(i * KA + k) * KP + q]
                acc_ref[s] = acc_ref[s] + term[:, q * B:(q + 1) * B]
        row = pl.multiple_of(i * B, B)
        for w in range(WIN * WIN):
            prod_ref[pl.ds(row, B), w * B:(w + 1) * B] = acc_ref[w].astype(jnp.bfloat16)
        for p in range(KP):
            h = home_ref[i * KP + p]
            dp_ref[h, pl.ds(row, B), :] = dp_ref[h, pl.ds(row, B), :] + own_ref[i, :, p * B:(p + 1) * B].astype(jnp.float32)
        return carry

    dp_ref[...] = jnp.zeros(dp_ref.shape, jnp.float32)
    lax.fori_loop(0, patches, one_patch, 0)
    prod = prod_ref[...]
    dims = (((0,), (0,)), ((), ()))

    def coarse_terms(h):
        return lax.dot_general(dp_ref[h].astype(jnp.bfloat16), prod, dims, preferred_element_type=jnp.float32)

    for dr in range(HOME):
        keep_ref[dr] = coarse_terms(HOME + dr)
        send_ref[0, dr] = coarse_terms(dr).astype(send_ref.dtype)
        send_ref[1, dr] = coarse_terms(2 * HOME + dr).astype(send_ref.dtype)


def fold_cols_kernel(keep_ref, left_ref, right_ref, keep_out, send_out):
    src_w = WIN * B
    dst_w = OUTW * B
    for d in range(HOME):
        out = keep_out if d == 1 else send_out.at[d // 2]
        for sx in range(WIN):
            lo = sx * dst_w
            s0 = sx * src_w
            own = keep_ref[d, :, s0:s0 + src_w]
            left = left_ref[d, :, s0:s0 + src_w].astype(jnp.float32)
            right = right_ref[d, :, s0:s0 + src_w].astype(jnp.float32)
            first = left[:, :B]
            mid = left[:, B:2 * B] + own[:, :B]
            core = left[:, 2 * B:] + own[:, B:src_w - B] + right[:, :src_w - 2 * B]
            tail = own[:, src_w - B:] + right[:, src_w - 2 * B:src_w - B]
            last = right[:, src_w - B:]
            out[:, lo:lo + B] = first.astype(out.dtype)
            out[:, lo + B:lo + 2 * B] = mid.astype(out.dtype)
            out[:, lo + 2 * B:lo + 5 * B] = core.astype(out.dtype)
            out[:, lo + 5 * B:lo + 6 * B] = tail.astype(out.dtype)
            out[:, lo + 6 * B:lo + 7 * B] = last.astype(out.dtype)


def fold_rows_kernel(keep_ref, up_ref, down_ref, out_ref):
    band = OUTW * B
    for s in range(OUTW):
        parts = []
        if 1 <= s <= WIN:
            parts.append(keep_ref[:, (s - 1) * band:s * band])
        if s <= WIN - 1:
            parts.append(up_ref[:, s * band:(s + 1) * band].astype(jnp.float32))
        if s >= 2:
            parts.append(down_ref[:, (s - 2) * band:(s - 1) * band].astype(jnp.float32))
        total = parts[0]
        for extra in parts[1:]:
            total = total + extra
        out_ref[:, s * band:(s + 1) * band] = total.astype(out_ref.dtype)


def per_device(
    fine_blocks, fine_columns, fine_counts, prolong_blocks, prolong_columns, prolong_counts
):
    tile_rows, tile_cols = fine_counts.shape
    assert tile_rows == AG and tile_cols == AG
    patches = tile_rows * tile_cols
    grid_cols = tile_cols * lax.axis_size("col")
    coarse_grid_cols = lax.axis_size("col")
    row_index = lax.axis_index("row")
    col_index = lax.axis_index("col")

    prolong = prolong_blocks
    entries = jnp.arange(KP, dtype=jnp.int32)
    kept = entries[None, None, :] < prolong_counts[:, :, None]

    own_codes = prolong_columns.reshape(patches, KP)
    hrow = jnp.clip(own_codes // coarse_grid_cols - row_index + 1, 0, HOME - 1)
    hcol = jnp.clip(own_codes % coarse_grid_cols - col_index + 1, 0, HOME - 1)
    rel = jnp.where(kept, (hrow * HOME + hcol).reshape(tile_rows, tile_cols, KP), HOME * HOME)

    def payload(p_part, rel_part):
        count = p_part.shape[0]
        flat = p_part.reshape(count * B, KP * B)
        extra = jnp.zeros((16, KP * B), jnp.bfloat16)
        extra = extra.at[0, :count * KP].set(rel_part.reshape(-1).astype(jnp.bfloat16))
        return jnp.concatenate([flat, extra], axis=0)

    def unpack(got, count):
        p_part = got[:count * B].reshape(count, B, KP * B)
        rel_part = got[count * B, :count * KP].astype(jnp.int32).reshape(count, KP)
        return p_part, rel_part

    hr, hc = tile_rows + 2, tile_cols + 2
    above, above_rel = unpack(shifted(payload(prolong[tile_rows - 1], rel[tile_rows - 1]), 1, 0), tile_cols)
    below, below_rel = unpack(shifted(payload(prolong[0], rel[0]), -1, 0), tile_cols)
    tall = jnp.concatenate([above[None], prolong, below[None]], axis=0)
    tall_rel = jnp.concatenate([above_rel[None], rel, below_rel[None]], axis=0)
    left, left_rel = unpack(shifted(payload(tall[:, tile_cols - 1], tall_rel[:, tile_cols - 1]), 0, 1), hr)
    right, right_rel = unpack(shifted(payload(tall[:, 0], tall_rel[:, 0]), 0, -1), hr)
    near_p = jnp.concatenate([left[:, None], tall, right[:, None]], axis=1).reshape(hr * hc, B, KP * B)
    near_rel = jnp.concatenate([left_rel[:, None], tall_rel, right_rel[:, None]], axis=1)

    off_r = (jnp.arange(hr, dtype=jnp.int32) + tile_rows - 1) // tile_rows - 1
    off_c = (jnp.arange(hc, dtype=jnp.int32) + tile_cols - 1) // tile_cols - 1
    near_slot = (near_rel // HOME + off_r[:, None, None] + 1) * WIN + near_rel % HOME + off_c[None, :, None] + 1
    near_slot = jnp.where(near_rel < HOME * HOME, near_slot, TRASH).reshape(hr * hc, KP)

    first_row = row_index * tile_rows
    first_col = col_index * tile_cols
    targets = fine_columns.reshape(patches, KA)
    pos = (targets // grid_cols - first_row + 1) * hc + targets % grid_cols - first_col + 1
    pos = jnp.clip(pos, 0, hr * hc - 1)
    slot = near_slot[pos]
    blocks = jnp.arange(KA, dtype=jnp.int32)
    used = blocks[None, :] < fine_counts.reshape(patches)[:, None]
    slot = jnp.where(used[:, :, None], slot, TRASH)
    home = jnp.where(kept.reshape(patches, KP), hcol * HOME + hrow, HOME * HOME)

    smem = pltpu.MemorySpace.SMEM
    vmem = pltpu.MemorySpace.VMEM
    width = WIN * WIN * B
    keep, send = pl.pallas_call(
        galerkin_kernel,
        out_shape=(
            jax.ShapeDtypeStruct((HOME, B, width), jnp.float32),
            jax.ShapeDtypeStruct((2, HOME, B, width), SEND),
        ),
        in_specs=[
            pl.BlockSpec(memory_space=smem),
            pl.BlockSpec(memory_space=smem),
            pl.BlockSpec(memory_space=smem),
            pl.BlockSpec(memory_space=vmem),
            pl.BlockSpec(memory_space=vmem),
            pl.BlockSpec(memory_space=vmem),
        ],
        out_specs=(pl.BlockSpec(memory_space=vmem), pl.BlockSpec(memory_space=vmem)),
        scratch_shapes=[
            pltpu.VMEM((TRASH + 1, B, B), jnp.float32),
            pltpu.VMEM((patches * B, width), jnp.bfloat16),
            pltpu.VMEM((HOME * HOME + 1, patches * B, B), jnp.float32),
        ],
    )(
        pos.reshape(-1).astype(jnp.int32),
        slot.reshape(-1).astype(jnp.int32),
        home.reshape(-1).astype(jnp.int32),
        fine_blocks.reshape(patches, B, KA * B),
        near_p,
        prolong.reshape(patches, B, KP * B),
    )
    left_in = shifted(send[1], 0, 1)
    right_in = shifted(send[0], 0, -1)
    band = WIN * OUTW * B
    keep2, send2 = pl.pallas_call(
        fold_cols_kernel,
        out_shape=(
            jax.ShapeDtypeStruct((B, band), jnp.float32),
            jax.ShapeDtypeStruct((2, B, band), SEND),
        ),
        in_specs=[pl.BlockSpec(memory_space=vmem)] * 3,
        out_specs=(pl.BlockSpec(memory_space=vmem), pl.BlockSpec(memory_space=vmem)),
    )(keep, left_in, right_in)
    up_in = shifted(send2[1], 1, 0)
    down_in = shifted(send2[0], -1, 0)
    out = pl.pallas_call(
        fold_rows_kernel,
        out_shape=jax.ShapeDtypeStruct((B, OUTW * OUTW * B), jnp.bfloat16),
        in_specs=[pl.BlockSpec(memory_space=vmem)] * 3,
        out_specs=pl.BlockSpec(memory_space=vmem),
    )(keep2, up_in, down_in)
    return out.reshape(1, 1, B, OUTW * OUTW * B)


def solution(mesh):
    in_specs = (
        P("row", "col", None, None),
        P("row", "col", None),
        P("row", "col"),
        P("row", "col", None, None),
        P("row", "col", None),
        P("row", "col"),
    )
    out_specs = P("row", "col", None, None)
    return jax.shard_map(
        per_device, mesh=mesh, in_specs=in_specs, out_specs=out_specs, check_vma=False
    )
```

```python
import jax
import jax.numpy as jnp
from jax import lax
from jax.experimental import pallas as pl
from jax.experimental.pallas import tpu as pltpu
from jax.sharding import PartitionSpec as P

B = 64
KA = 9
KP = 4
AG = 4

NEAR = 3
WIN = 5
HOME = 3
OUTW = 7
TRASH = WIN * WIN
SEND = jnp.bfloat16


def shifted(value, by_row, by_col):
    rows = lax.axis_size("row")
    cols = lax.axis_size("col")
    pairs = []
    for r in range(rows):
        for c in range(cols):
            tr, tc = r + by_row, c + by_col
            if 0 <= tr < rows and 0 <= tc < cols:
                pairs.append((r * cols + c, tr * cols + tc))
    return lax.ppermute(value, ("row", "col"), pairs)


def galerkin_kernel(pos_ref, slot_ref, home_ref, a_ref, p_ref, own_ref, keep_ref, right_ref, left_ref,
                    acc_ref, prod_ref, dpt_ref):
    patches = a_ref.shape[0]

    def one_patch(i, carry):
        acc_ref[...] = jnp.zeros(acc_ref.shape, jnp.float32)
        for k in range(KA):
            pos = pos_ref[i * KA + k]
            a_blk = a_ref[i, :, k * B:(k + 1) * B]
            term = jnp.dot(a_blk, p_ref[pos], preferred_element_type=jnp.float32)
            for q in range(KP):
                s = slot_ref[(i * KA + k) * KP + q]
                acc_ref[s] = acc_ref[s] + term[:, q * B:(q + 1) * B]
        row = pl.multiple_of(i * B, B)
        for w in range(WIN * WIN):
            prod_ref[pl.ds(row, B), w * B:(w + 1) * B] = acc_ref[w].astype(jnp.bfloat16)
        return carry

    lax.fori_loop(0, patches, one_patch, 0)

    dpt_ref[...] = jnp.zeros(dpt_ref.shape, jnp.float32)
    for i in range(patches):
        flipped = own_ref[i].astype(jnp.float32).T
        for p in range(KP):
            start = pl.multiple_of(home_ref[i * KP + p] * B, B)
            dpt_ref[pl.ds(start, B), i * B:(i + 1) * B] += flipped[p * B:(p + 1) * B, :]

    prod = prod_ref[...]
    group = HOME * B
    for out, at in ((right_ref, 0), (keep_ref, 1), (left_ref, 2)):
        terms = jnp.dot(dpt_ref[at * group:(at + 1) * group].astype(jnp.bfloat16), prod,
                        preferred_element_type=jnp.float32)
        out[...] = terms.reshape(out.shape).astype(out.dtype)


def fold_cols_kernel(keep_ref, left_ref, right_ref, keep_out, send_out):
    src_w = WIN * B
    dst_w = OUTW * B
    for d in range(HOME):
        out = keep_out if d == 1 else send_out.at[d // 2]
        for sx in range(WIN):
            lo = sx * dst_w
            s0 = sx * src_w
            own = keep_ref[d, :, s0:s0 + src_w]
            left = left_ref[d, :, s0:s0 + src_w].astype(jnp.float32)
            right = right_ref[d, :, s0:s0 + src_w].astype(jnp.float32)
            first = left[:, :B]
            mid = left[:, B:2 * B] + own[:, :B]
            core = left[:, 2 * B:] + own[:, B:src_w - B] + right[:, :src_w - 2 * B]
            tail = own[:, src_w - B:] + right[:, src_w - 2 * B:src_w - B]
            last = right[:, src_w - B:]
            out[:, lo:lo + B] = first.astype(out.dtype)
            out[:, lo + B:lo + 2 * B] = mid.astype(out.dtype)
            out[:, lo + 2 * B:lo + 5 * B] = core.astype(out.dtype)
            out[:, lo + 5 * B:lo + 6 * B] = tail.astype(out.dtype)
            out[:, lo + 6 * B:lo + 7 * B] = last.astype(out.dtype)


def fold_rows_kernel(keep_ref, up_ref, down_ref, out_ref):
    band = OUTW * B
    for s in range(OUTW):
        parts = []
        if 1 <= s <= WIN:
            parts.append(keep_ref[:, (s - 1) * band:s * band])
        if s <= WIN - 1:
            parts.append(up_ref[:, s * band:(s + 1) * band].astype(jnp.float32))
        if s >= 2:
            parts.append(down_ref[:, (s - 2) * band:(s - 1) * band].astype(jnp.float32))
        total = parts[0]
        for extra in parts[1:]:
            total = total + extra
        out_ref[:, s * band:(s + 1) * band] = total.astype(out_ref.dtype)


def per_device(
    fine_blocks, fine_columns, fine_counts, prolong_blocks, prolong_columns, prolong_counts
):
    tile_rows, tile_cols = fine_counts.shape
    assert tile_rows == AG and tile_cols == AG
    patches = tile_rows * tile_cols
    grid_cols = tile_cols * lax.axis_size("col")
    coarse_grid_cols = lax.axis_size("col")
    row_index = lax.axis_index("row")
    col_index = lax.axis_index("col")

    prolong = prolong_blocks
    entries = jnp.arange(KP, dtype=jnp.int32)
    kept = entries[None, None, :] < prolong_counts[:, :, None]

    own_codes = prolong_columns.reshape(patches, KP)
    hrow = jnp.clip(own_codes // coarse_grid_cols - row_index + 1, 0, HOME - 1)
    hcol = jnp.clip(own_codes % coarse_grid_cols - col_index + 1, 0, HOME - 1)
    rel = jnp.where(kept, (hrow * HOME + hcol).reshape(tile_rows, tile_cols, KP), HOME * HOME)

    def payload(p_part, rel_part):
        count = p_part.shape[0]
        flat = p_part.reshape(count * B, KP * B)
        extra = jnp.zeros((16, KP * B), jnp.bfloat16)
        extra = extra.at[0, :count * KP].set(rel_part.reshape(-1).astype(jnp.bfloat16))
        return jnp.concatenate([flat, extra], axis=0)

    def unpack(got, count):
        p_part = got[:count * B].reshape(count, B, KP * B)
        rel_part = got[count * B, :count * KP].astype(jnp.int32).reshape(count, KP)
        return p_part, rel_part

    hr, hc = tile_rows + 2, tile_cols + 2
    above, above_rel = unpack(shifted(payload(prolong[tile_rows - 1], rel[tile_rows - 1]), 1, 0), tile_cols)
    below, below_rel = unpack(shifted(payload(prolong[0], rel[0]), -1, 0), tile_cols)
    tall = jnp.concatenate([above[None], prolong, below[None]], axis=0)
    tall_rel = jnp.concatenate([above_rel[None], rel, below_rel[None]], axis=0)
    left, left_rel = unpack(shifted(payload(tall[:, tile_cols - 1], tall_rel[:, tile_cols - 1]), 0, 1), hr)
    right, right_rel = unpack(shifted(payload(tall[:, 0], tall_rel[:, 0]), 0, -1), hr)
    near_p = jnp.concatenate([left[:, None], tall, right[:, None]], axis=1).reshape(hr * hc, B, KP * B)
    near_rel = jnp.concatenate([left_rel[:, None], tall_rel, right_rel[:, None]], axis=1)

    off_r = (jnp.arange(hr, dtype=jnp.int32) + tile_rows - 1) // tile_rows - 1
    off_c = (jnp.arange(hc, dtype=jnp.int32) + tile_cols - 1) // tile_cols - 1
    near_slot = (near_rel // HOME + off_r[:, None, None] + 1) * WIN + near_rel % HOME + off_c[None, :, None] + 1
    near_slot = jnp.where(near_rel < HOME * HOME, near_slot, TRASH).reshape(hr * hc, KP)

    first_row = row_index * tile_rows
    first_col = col_index * tile_cols
    targets = fine_columns.reshape(patches, KA)
    pos = (targets // grid_cols - first_row + 1) * hc + targets % grid_cols - first_col + 1
    pos = jnp.clip(pos, 0, hr * hc - 1)
    slot = near_slot[pos]
    blocks = jnp.arange(KA, dtype=jnp.int32)
    used = blocks[None, :] < fine_counts.reshape(patches)[:, None]
    slot = jnp.where(used[:, :, None], slot, TRASH)
    home = jnp.where(kept.reshape(patches, KP), hcol * HOME + hrow, HOME * HOME)

    smem = pltpu.MemorySpace.SMEM
    vmem = pltpu.MemorySpace.VMEM
    width = WIN * WIN * B
    keep, to_right, to_left = pl.pallas_call(
        galerkin_kernel,
        out_shape=(
            jax.ShapeDtypeStruct((HOME, B, width), jnp.float32),
            jax.ShapeDtypeStruct((HOME, B, width), SEND),
            jax.ShapeDtypeStruct((HOME, B, width), SEND),
        ),
        in_specs=[
            pl.BlockSpec(memory_space=smem),
            pl.BlockSpec(memory_space=smem),
            pl.BlockSpec(memory_space=smem),
            pl.BlockSpec(memory_space=vmem),
            pl.BlockSpec(memory_space=vmem),
            pl.BlockSpec(memory_space=vmem),
        ],
        out_specs=(pl.BlockSpec(memory_space=vmem),) * 3,
        scratch_shapes=[
            pltpu.VMEM((TRASH + 1, B, B), jnp.float32),
            pltpu.VMEM((patches * B, width), jnp.bfloat16),
            pltpu.VMEM(((HOME * HOME + 1) * B, patches * B), jnp.float32),
        ],
    )(
        pos.reshape(-1).astype(jnp.int32),
        slot.reshape(-1).astype(jnp.int32),
        home.reshape(-1).astype(jnp.int32),
        fine_blocks.reshape(patches, B, KA * B),
        near_p,
        prolong.reshape(patches, B, KP * B),
    )
    left_in = shifted(to_left, 0, 1)
    right_in = shifted(to_right, 0, -1)
    band = WIN * OUTW * B
    keep2, send2 = pl.pallas_call(
        fold_cols_kernel,
        out_shape=(
            jax.ShapeDtypeStruct((B, band), jnp.float32),
            jax.ShapeDtypeStruct((2, B, band), SEND),
        ),
        in_specs=[pl.BlockSpec(memory_space=vmem)] * 3,
        out_specs=(pl.BlockSpec(memory_space=vmem), pl.BlockSpec(memory_space=vmem)),
    )(keep, left_in, right_in)
    up_in = shifted(send2[1], 1, 0)
    down_in = shifted(send2[0], -1, 0)
    out = pl.pallas_call(
        fold_rows_kernel,
        out_shape=jax.ShapeDtypeStruct((B, OUTW * OUTW * B), jnp.bfloat16),
        in_specs=[pl.BlockSpec(memory_space=vmem)] * 3,
        out_specs=pl.BlockSpec(memory_space=vmem),
    )(keep2, up_in, down_in)
    return out.reshape(1, 1, B, OUTW * OUTW * B)


def solution(mesh):
    in_specs = (
        P("row", "col", None, None),
        P("row", "col", None),
        P("row", "col"),
        P("row", "col", None, None),
        P("row", "col", None),
        P("row", "col"),
    )
    out_specs = P("row", "col", None, None)
    return jax.shard_map(
        per_device, mesh=mesh, in_specs=in_specs, out_specs=out_specs, check_vma=False
    )
```

```python
import jax
import jax.numpy as jnp
from jax import lax
from jax.experimental import pallas as pl
from jax.experimental.pallas import tpu as pltpu
from jax.sharding import PartitionSpec as P

B = 64
KA = 9
KP = 4
AG = 4

NEAR = 3
WIN = 5
HOME = 3
OUTW = 7
TRASH = WIN * WIN
SEND = jnp.bfloat16


def shifted(value, by_row, by_col):
    rows = lax.axis_size("row")
    cols = lax.axis_size("col")
    pairs = []
    for r in range(rows):
        for c in range(cols):
            tr, tc = r + by_row, c + by_col
            if 0 <= tr < rows and 0 <= tc < cols:
                pairs.append((r * cols + c, tr * cols + tc))
    return lax.ppermute(value, ("row", "col"), pairs)


def galerkin_kernel(pos_ref, nslot_ref, count_ref, home_ref, a_ref, own_ref, above_ref, below_ref,
                    left_ref, right_ref, keep_ref, to_right_ref, to_left_ref,
                    acc_ref, prod_ref, dpt_ref, p_ref):
    patches = a_ref.shape[0]
    rows, cols = AG, AG
    hc = cols + 2
    for x in range(rows):
        for y in range(cols):
            p_ref[(x + 1) * hc + y + 1] = own_ref[x * cols + y]
    for y in range(cols):
        p_ref[y + 1] = above_ref[y * B:(y + 1) * B]
        p_ref[(rows + 1) * hc + y + 1] = below_ref[y * B:(y + 1) * B]
    for x in range(rows + 2):
        p_ref[x * hc] = left_ref[x * B:(x + 1) * B]
        p_ref[x * hc + hc - 1] = right_ref[x * B:(x + 1) * B]

    def one_patch(i, carry):
        acc_ref[...] = jnp.zeros(acc_ref.shape, jnp.float32)
        count = count_ref[i]
        for k in range(KA):
            pos = pos_ref[i * KA + k]
            a_blk = a_ref[i, :, k * B:(k + 1) * B]
            term = jnp.dot(a_blk, p_ref[pos], preferred_element_type=jnp.float32)
            for q in range(KP):
                s = jnp.where(k < count, nslot_ref[pos * KP + q], TRASH)
                acc_ref[s] = acc_ref[s] + term[:, q * B:(q + 1) * B]
        row = pl.multiple_of(i * B, B)
        for w in range(WIN * WIN):
            prod_ref[pl.ds(row, B), w * B:(w + 1) * B] = acc_ref[w].astype(jnp.bfloat16)
        return carry

    lax.fori_loop(0, patches, one_patch, 0)

    dpt_ref[...] = jnp.zeros(dpt_ref.shape, jnp.float32)
    for i in range(patches):
        flipped = own_ref[i].astype(jnp.float32).T
        for p in range(KP):
            start = pl.multiple_of(home_ref[i * KP + p] * B, B)
            dpt_ref[pl.ds(start, B), i * B:(i + 1) * B] += flipped[p * B:(p + 1) * B, :]

    prod = prod_ref[...]
    group = HOME * B
    for out, at in ((to_right_ref, 0), (keep_ref, 1), (to_left_ref, 2)):
        terms = jnp.dot(dpt_ref[at * group:(at + 1) * group].astype(jnp.bfloat16), prod,
                        preferred_element_type=jnp.float32)
        out[...] = terms.reshape(out.shape).astype(out.dtype)


def fold_cols_kernel(keep_ref, left_ref, right_ref, keep_out, minus_out, plus_out):
    src_w = WIN * B
    dst_w = OUTW * B
    for d in range(HOME):
        out = (minus_out, keep_out, plus_out)[d]
        for sx in range(WIN):
            lo = sx * dst_w
            s0 = sx * src_w
            own = keep_ref[d, :, s0:s0 + src_w]
            left = left_ref[d, :, s0:s0 + src_w].astype(jnp.float32)
            right = right_ref[d, :, s0:s0 + src_w].astype(jnp.float32)
            first = left[:, :B]
            mid = left[:, B:2 * B] + own[:, :B]
            core = left[:, 2 * B:] + own[:, B:src_w - B] + right[:, :src_w - 2 * B]
            tail = own[:, src_w - B:] + right[:, src_w - 2 * B:src_w - B]
            last = right[:, src_w - B:]
            out[:, lo:lo + B] = first.astype(out.dtype)
            out[:, lo + B:lo + 2 * B] = mid.astype(out.dtype)
            out[:, lo + 2 * B:lo + 5 * B] = core.astype(out.dtype)
            out[:, lo + 5 * B:lo + 6 * B] = tail.astype(out.dtype)
            out[:, lo + 6 * B:lo + 7 * B] = last.astype(out.dtype)


def fold_rows_kernel(keep_ref, up_ref, down_ref, out_ref):
    band = OUTW * B
    for s in range(OUTW):
        parts = []
        if 1 <= s <= WIN:
            parts.append(keep_ref[:, (s - 1) * band:s * band])
        if s <= WIN - 1:
            parts.append(up_ref[:, s * band:(s + 1) * band].astype(jnp.float32))
        if s >= 2:
            parts.append(down_ref[:, (s - 2) * band:(s - 1) * band].astype(jnp.float32))
        total = parts[0]
        for extra in parts[1:]:
            total = total + extra
        out_ref[:, s * band:(s + 1) * band] = total.astype(out_ref.dtype)


def per_device(
    fine_blocks, fine_columns, fine_counts, prolong_blocks, prolong_columns, prolong_counts
):
    tile_rows, tile_cols = fine_counts.shape
    assert tile_rows == AG and tile_cols == AG
    patches = tile_rows * tile_cols
    grid_cols = tile_cols * lax.axis_size("col")
    coarse_grid_cols = lax.axis_size("col")
    row_index = lax.axis_index("row")
    col_index = lax.axis_index("col")

    prolong = prolong_blocks
    entries = jnp.arange(KP, dtype=jnp.int32)
    kept = entries[None, None, :] < prolong_counts[:, :, None]

    own_codes = prolong_columns.reshape(patches, KP)
    hrow = jnp.clip(own_codes // coarse_grid_cols - row_index + 1, 0, HOME - 1)
    hcol = jnp.clip(own_codes % coarse_grid_cols - col_index + 1, 0, HOME - 1)
    rel = jnp.where(kept, (hrow * HOME + hcol).reshape(tile_rows, tile_cols, KP), HOME * HOME)

    def payload(p_part, rel_part):
        count = p_part.shape[0]
        flat = p_part.reshape(count * B, KP * B)
        extra = jnp.zeros((16, KP * B), jnp.bfloat16)
        extra = extra.at[0, :count * KP].set(rel_part.reshape(-1).astype(jnp.bfloat16))
        return jnp.concatenate([flat, extra], axis=0)

    def unpack(got, count):
        p_part = got[:count * B].reshape(count, B, KP * B)
        rel_part = got[count * B, :count * KP].astype(jnp.int32).reshape(count, KP)
        return p_part, rel_part

    hr, hc = tile_rows + 2, tile_cols + 2
    above_in = shifted(payload(prolong[tile_rows - 1], rel[tile_rows - 1]), 1, 0)
    below_in = shifted(payload(prolong[0], rel[0]), -1, 0)
    above, above_rel = unpack(above_in, tile_cols)
    below, below_rel = unpack(below_in, tile_cols)
    tall = jnp.concatenate([above[None], prolong, below[None]], axis=0)
    tall_rel = jnp.concatenate([above_rel[None], rel, below_rel[None]], axis=0)
    left_in = shifted(payload(tall[:, tile_cols - 1], tall_rel[:, tile_cols - 1]), 0, 1)
    right_in = shifted(payload(tall[:, 0], tall_rel[:, 0]), 0, -1)
    left_rel = unpack(left_in, hr)[1]
    right_rel = unpack(right_in, hr)[1]
    near_rel = jnp.concatenate([left_rel[:, None], tall_rel, right_rel[:, None]], axis=1)

    off_r = (jnp.arange(hr, dtype=jnp.int32) + tile_rows - 1) // tile_rows - 1
    off_c = (jnp.arange(hc, dtype=jnp.int32) + tile_cols - 1) // tile_cols - 1
    near_slot = (near_rel // HOME + off_r[:, None, None] + 1) * WIN + near_rel % HOME + off_c[None, :, None] + 1
    near_slot = jnp.where(near_rel < HOME * HOME, near_slot, TRASH).reshape(hr * hc * KP)

    first_row = row_index * tile_rows
    first_col = col_index * tile_cols
    targets = fine_columns.reshape(patches, KA)
    pos = (targets // grid_cols - first_row + 1) * hc + targets % grid_cols - first_col + 1
    pos = jnp.clip(pos, 0, hr * hc - 1)
    home = jnp.where(kept.reshape(patches, KP), hcol * HOME + hrow, HOME * HOME)

    smem = pltpu.MemorySpace.SMEM
    vmem = pltpu.MemorySpace.VMEM
    width = WIN * WIN * B
    keep, to_right, to_left = pl.pallas_call(
        galerkin_kernel,
        out_shape=(
            jax.ShapeDtypeStruct((HOME, B, width), jnp.float32),
            jax.ShapeDtypeStruct((HOME, B, width), SEND),
            jax.ShapeDtypeStruct((HOME, B, width), SEND),
        ),
        in_specs=[pl.BlockSpec(memory_space=smem)] * 4 + [pl.BlockSpec(memory_space=vmem)] * 6,
        out_specs=(pl.BlockSpec(memory_space=vmem),) * 3,
        scratch_shapes=[
            pltpu.VMEM((TRASH + 1, B, B), jnp.float32),
            pltpu.VMEM((patches * B, width), jnp.bfloat16),
            pltpu.VMEM(((HOME * HOME + 1) * B, patches * B), jnp.float32),
            pltpu.VMEM((hr * hc, B, KP * B), jnp.bfloat16),
        ],
    )(
        pos.reshape(-1).astype(jnp.int32),
        near_slot.astype(jnp.int32),
        fine_counts.reshape(-1).astype(jnp.int32),
        home.reshape(-1).astype(jnp.int32),
        fine_blocks.reshape(patches, B, KA * B),
        prolong.reshape(patches, B, KP * B),
        above_in,
        below_in,
        left_in,
        right_in,
    )
    from_left = shifted(to_left, 0, 1)
    from_right = shifted(to_right, 0, -1)
    band = WIN * OUTW * B
    keep2, minus, plus = pl.pallas_call(
        fold_cols_kernel,
        out_shape=(
            jax.ShapeDtypeStruct((B, band), jnp.float32),
            jax.ShapeDtypeStruct((B, band), SEND),
            jax.ShapeDtypeStruct((B, band), SEND),
        ),
        in_specs=[pl.BlockSpec(memory_space=vmem)] * 3,
        out_specs=(pl.BlockSpec(memory_space=vmem),) * 3,
    )(keep, from_left, from_right)
    up_in = shifted(plus, 1, 0)
    down_in = shifted(minus, -1, 0)
    out = pl.pallas_call(
        fold_rows_kernel,
        out_shape=jax.ShapeDtypeStruct((B, OUTW * OUTW * B), jnp.bfloat16),
        in_specs=[pl.BlockSpec(memory_space=vmem)] * 3,
        out_specs=pl.BlockSpec(memory_space=vmem),
    )(keep2, up_in, down_in)
    return out.reshape(1, 1, B, OUTW * OUTW * B)


def solution(mesh):
    in_specs = (
        P("row", "col", None, None),
        P("row", "col", None),
        P("row", "col"),
        P("row", "col", None, None),
        P("row", "col", None),
        P("row", "col"),
    )
    out_specs = P("row", "col", None, None)
    return jax.shard_map(
        per_device, mesh=mesh, in_specs=in_specs, out_specs=out_specs, check_vma=False
    )
```

```python
import jax
import jax.numpy as jnp
from jax import lax
from jax.experimental import pallas as pl
from jax.experimental.pallas import tpu as pltpu
from jax.sharding import PartitionSpec as P

B = 64
KA = 9
KP = 4
AG = 4

NEAR = 3
WIN = 5
HOME = 3
OUTW = 7
TRASH = WIN * WIN
SEND = jnp.bfloat16


def shifted(value, by_row, by_col):
    rows = lax.axis_size("row")
    cols = lax.axis_size("col")
    pairs = []
    for r in range(rows):
        for c in range(cols):
            tr, tc = r + by_row, c + by_col
            if 0 <= tr < rows and 0 <= tc < cols:
                pairs.append((r * cols + c, tr * cols + tc))
    return lax.ppermute(value, ("row", "col"), pairs)


def galerkin_kernel(pos_ref, nslot_ref, count_ref, home_ref, a_ref, own_ref, above_ref, below_ref,
                    left_ref, right_ref, keep_ref, to_right_ref, to_left_ref,
                    acc_ref, prod_ref, dpt_ref, p_ref):
    patches = a_ref.shape[0]
    rows, cols = AG, AG
    hc = cols + 2
    for x in range(rows):
        for y in range(cols):
            p_ref[(x + 1) * hc + y + 1] = own_ref[x * cols + y]
    for y in range(cols):
        p_ref[y + 1] = above_ref[y * B:(y + 1) * B]
        p_ref[(rows + 1) * hc + y + 1] = below_ref[y * B:(y + 1) * B]
    for x in range(rows + 2):
        p_ref[x * hc] = left_ref[x * B:(x + 1) * B]
        p_ref[x * hc + hc - 1] = right_ref[x * B:(x + 1) * B]

    def one_patch(i, carry):
        acc_ref[...] = jnp.zeros(acc_ref.shape, jnp.float32)
        x = i // AG
        y = i % AG
        count = count_ref[x, y]
        for k in range(KA):
            pos = pos_ref[x, y, k]
            a_blk = a_ref[i, :, k * B:(k + 1) * B]
            term = jnp.dot(a_blk, p_ref[pos], preferred_element_type=jnp.float32)
            for q in range(KP):
                s = jnp.where(k < count, nslot_ref[pos * KP + q], TRASH)
                acc_ref[s] = acc_ref[s] + term[:, q * B:(q + 1) * B]
        row = pl.multiple_of(i * B, B)
        for w in range(WIN * WIN):
            prod_ref[pl.ds(row, B), w * B:(w + 1) * B] = acc_ref[w].astype(jnp.bfloat16)
        return carry

    lax.fori_loop(0, patches, one_patch, 0)

    dpt_ref[...] = jnp.zeros(dpt_ref.shape, jnp.float32)
    for i in range(patches):
        flipped = own_ref[i].astype(jnp.float32).T
        for p in range(KP):
            start = pl.multiple_of(home_ref[i // AG, i % AG, p] * B, B)
            dpt_ref[pl.ds(start, B), i * B:(i + 1) * B] += flipped[p * B:(p + 1) * B, :]

    prod = prod_ref[...]
    group = HOME * B
    for out, at in ((to_right_ref, 0), (keep_ref, 1), (to_left_ref, 2)):
        terms = jnp.dot(dpt_ref[at * group:(at + 1) * group].astype(jnp.bfloat16), prod,
                        preferred_element_type=jnp.float32)
        out[...] = terms.reshape(out.shape).astype(out.dtype)


def fold_cols_kernel(keep_ref, left_ref, right_ref, keep_out, minus_out, plus_out):
    src_w = WIN * B
    dst_w = OUTW * B
    for d in range(HOME):
        out = (minus_out, keep_out, plus_out)[d]
        for sx in range(WIN):
            lo = sx * dst_w
            s0 = sx * src_w
            own = keep_ref[d, :, s0:s0 + src_w]
            left = left_ref[d, :, s0:s0 + src_w].astype(jnp.float32)
            right = right_ref[d, :, s0:s0 + src_w].astype(jnp.float32)
            first = left[:, :B]
            mid = left[:, B:2 * B] + own[:, :B]
            core = left[:, 2 * B:] + own[:, B:src_w - B] + right[:, :src_w - 2 * B]
            tail = own[:, src_w - B:] + right[:, src_w - 2 * B:src_w - B]
            last = right[:, src_w - B:]
            out[:, lo:lo + B] = first.astype(out.dtype)
            out[:, lo + B:lo + 2 * B] = mid.astype(out.dtype)
            out[:, lo + 2 * B:lo + 5 * B] = core.astype(out.dtype)
            out[:, lo + 5 * B:lo + 6 * B] = tail.astype(out.dtype)
            out[:, lo + 6 * B:lo + 7 * B] = last.astype(out.dtype)


def fold_rows_kernel(keep_ref, up_ref, down_ref, out_ref):
    band = OUTW * B
    for s in range(OUTW):
        parts = []
        if 1 <= s <= WIN:
            parts.append(keep_ref[:, (s - 1) * band:s * band])
        if s <= WIN - 1:
            parts.append(up_ref[:, s * band:(s + 1) * band].astype(jnp.float32))
        if s >= 2:
            parts.append(down_ref[:, (s - 2) * band:(s - 1) * band].astype(jnp.float32))
        total = parts[0]
        for extra in parts[1:]:
            total = total + extra
        out_ref[:, s * band:(s + 1) * band] = total.astype(out_ref.dtype)


def per_device(
    fine_blocks, fine_columns, fine_counts, prolong_blocks, prolong_columns, prolong_counts
):
    tile_rows, tile_cols = fine_counts.shape
    assert tile_rows == AG and tile_cols == AG
    patches = tile_rows * tile_cols
    grid_cols = tile_cols * lax.axis_size("col")
    coarse_grid_cols = lax.axis_size("col")
    row_index = lax.axis_index("row")
    col_index = lax.axis_index("col")

    prolong = prolong_blocks
    entries = jnp.arange(KP, dtype=jnp.int32)
    kept = entries[None, None, :] < prolong_counts[:, :, None]

    own_codes = prolong_columns
    hrow = jnp.clip(own_codes // coarse_grid_cols - row_index + 1, 0, HOME - 1)
    hcol = jnp.clip(own_codes % coarse_grid_cols - col_index + 1, 0, HOME - 1)
    rel = jnp.where(kept, hrow * HOME + hcol, HOME * HOME)
    home_rc = hcol * HOME + hrow

    def payload(p_part, rel_part):
        count = p_part.shape[0]
        flat = p_part.reshape(count * B, KP * B)
        extra = jnp.zeros((16, KP * B), jnp.bfloat16)
        extra = extra.at[0, :count * KP].set(rel_part.reshape(-1).astype(jnp.bfloat16))
        return jnp.concatenate([flat, extra], axis=0)

    def unpack(got, count):
        p_part = got[:count * B].reshape(count, B, KP * B)
        rel_part = got[count * B, :count * KP].astype(jnp.int32).reshape(count, KP)
        return p_part, rel_part

    hr, hc = tile_rows + 2, tile_cols + 2
    above_in = shifted(payload(prolong[tile_rows - 1], rel[tile_rows - 1]), 1, 0)
    below_in = shifted(payload(prolong[0], rel[0]), -1, 0)
    above, above_rel = unpack(above_in, tile_cols)
    below, below_rel = unpack(below_in, tile_cols)
    tall = jnp.concatenate([above[None], prolong, below[None]], axis=0)
    tall_rel = jnp.concatenate([above_rel[None], rel, below_rel[None]], axis=0)
    left_in = shifted(payload(tall[:, tile_cols - 1], tall_rel[:, tile_cols - 1]), 0, 1)
    right_in = shifted(payload(tall[:, 0], tall_rel[:, 0]), 0, -1)
    left_rel = unpack(left_in, hr)[1]
    right_rel = unpack(right_in, hr)[1]
    near_rel = jnp.concatenate([left_rel[:, None], tall_rel, right_rel[:, None]], axis=1)

    off_r = (jnp.arange(hr, dtype=jnp.int32) + tile_rows - 1) // tile_rows - 1
    off_c = (jnp.arange(hc, dtype=jnp.int32) + tile_cols - 1) // tile_cols - 1
    near_slot = (near_rel // HOME + off_r[:, None, None] + 1) * WIN + near_rel % HOME + off_c[None, :, None] + 1
    near_slot = jnp.where(near_rel < HOME * HOME, near_slot, TRASH).reshape(hr * hc * KP)

    first_row = row_index * tile_rows
    first_col = col_index * tile_cols
    targets = fine_columns
    pos = (targets // grid_cols - first_row + 1) * hc + targets % grid_cols - first_col + 1
    pos = jnp.clip(pos, 0, hr * hc - 1)
    home = jnp.where(kept, home_rc, HOME * HOME)

    smem = pltpu.MemorySpace.SMEM
    vmem = pltpu.MemorySpace.VMEM
    width = WIN * WIN * B
    keep, to_right, to_left = pl.pallas_call(
        galerkin_kernel,
        out_shape=(
            jax.ShapeDtypeStruct((HOME, B, width), jnp.float32),
            jax.ShapeDtypeStruct((HOME, B, width), SEND),
            jax.ShapeDtypeStruct((HOME, B, width), SEND),
        ),
        in_specs=[pl.BlockSpec(memory_space=smem)] * 4 + [pl.BlockSpec(memory_space=vmem)] * 6,
        out_specs=(pl.BlockSpec(memory_space=vmem),) * 3,
        scratch_shapes=[
            pltpu.VMEM((TRASH + 1, B, B), jnp.float32),
            pltpu.VMEM((patches * B, width), jnp.bfloat16),
            pltpu.VMEM(((HOME * HOME + 1) * B, patches * B), jnp.float32),
            pltpu.VMEM((hr * hc, B, KP * B), jnp.bfloat16),
        ],
    )(
        pos.astype(jnp.int32),
        near_slot.astype(jnp.int32),
        fine_counts.astype(jnp.int32),
        home.astype(jnp.int32),
        fine_blocks.reshape(patches, B, KA * B),
        prolong.reshape(patches, B, KP * B),
        above_in,
        below_in,
        left_in,
        right_in,
    )
    from_left = shifted(to_left, 0, 1)
    from_right = shifted(to_right, 0, -1)
    band = WIN * OUTW * B
    keep2, minus, plus = pl.pallas_call(
        fold_cols_kernel,
        out_shape=(
            jax.ShapeDtypeStruct((B, band), jnp.float32),
            jax.ShapeDtypeStruct((B, band), SEND),
            jax.ShapeDtypeStruct((B, band), SEND),
        ),
        in_specs=[pl.BlockSpec(memory_space=vmem)] * 3,
        out_specs=(pl.BlockSpec(memory_space=vmem),) * 3,
    )(keep, from_left, from_right)
    up_in = shifted(plus, 1, 0)
    down_in = shifted(minus, -1, 0)
    out = pl.pallas_call(
        fold_rows_kernel,
        out_shape=jax.ShapeDtypeStruct((B, OUTW * OUTW * B), jnp.bfloat16),
        in_specs=[pl.BlockSpec(memory_space=vmem)] * 3,
        out_specs=pl.BlockSpec(memory_space=vmem),
    )(keep2, up_in, down_in)
    return out.reshape(1, 1, B, OUTW * OUTW * B)


def solution(mesh):
    in_specs = (
        P("row", "col", None, None),
        P("row", "col", None),
        P("row", "col"),
        P("row", "col", None, None),
        P("row", "col", None),
        P("row", "col"),
    )
    out_specs = P("row", "col", None, None)
    return jax.shard_map(
        per_device, mesh=mesh, in_specs=in_specs, out_specs=out_specs, check_vma=False
    )
```

```python
import jax
import jax.numpy as jnp
from jax import lax
from jax.experimental import pallas as pl
from jax.experimental.pallas import tpu as pltpu
from jax.sharding import PartitionSpec as P

B = 64
KA = 9
KP = 4
AG = 4

NEAR = 3
WIN = 5
HOME = 3
OUTW = 7
TRASH = WIN * WIN
SEND = jnp.bfloat16


def shifted(value, by_row, by_col):
    rows = lax.axis_size("row")
    cols = lax.axis_size("col")
    pairs = []
    for r in range(rows):
        for c in range(cols):
            tr, tc = r + by_row, c + by_col
            if 0 <= tr < rows and 0 <= tc < cols:
                pairs.append((r * cols + c, tr * cols + tc))
    return lax.ppermute(value, ("row", "col"), pairs)


def is_local(pos):
    hc = AG + 2
    px = pos // hc
    py = pos % hc
    inside = (px >= 1) & (px <= AG) & (py >= 1) & (py <= AG)
    return inside, jnp.clip((px - 1) * AG + py - 1, 0, AG * AG - 1)


def local_kernel(pos_ref, lslot_ref, count_ref, home_ref, a_ref, own_ref, part_ref, dpt_out,
                 acc_ref, dpt_ref):
    patches = a_ref.shape[0]

    def one_patch(i, carry):
        acc_ref[...] = jnp.zeros(acc_ref.shape, jnp.float32)
        x = i // AG
        y = i % AG
        count = count_ref[x, y]
        for k in range(KA):
            inside, li = is_local(pos_ref[x, y, k])

            @pl.when(inside & (k < count))
            def _():
                term = jnp.dot(a_ref[i, :, k * B:(k + 1) * B], own_ref[li],
                               preferred_element_type=jnp.float32)
                for q in range(KP):
                    s = lslot_ref[li // AG, li % AG, q]
                    acc_ref[s] = acc_ref[s] + term[:, q * B:(q + 1) * B]

        row = pl.multiple_of(i * B, B)
        for w in range(WIN * WIN):
            part_ref[pl.ds(row, B), w * B:(w + 1) * B] = acc_ref[w]
        return carry

    lax.fori_loop(0, patches, one_patch, 0)

    dpt_ref[...] = jnp.zeros(dpt_ref.shape, jnp.float32)
    for i in range(patches):
        flipped = own_ref[i].astype(jnp.float32).T
        for p in range(KP):
            start = pl.multiple_of(home_ref[i // AG, i % AG, p] * B, B)
            dpt_ref[pl.ds(start, B), i * B:(i + 1) * B] += flipped[p * B:(p + 1) * B, :]
    dpt_out[...] = dpt_ref[...].astype(dpt_out.dtype)


def galerkin_kernel(pos_ref, nslot_ref, count_ref, a_ref, own_ref, above_ref, below_ref,
                    left_ref, right_ref, part_ref, dpt_ref, keep_ref, to_right_ref, to_left_ref,
                    acc_ref, prod_ref, p_ref):
    patches = a_ref.shape[0]
    rows, cols = AG, AG
    hc = cols + 2
    for x in range(rows):
        for y in range(cols):
            p_ref[(x + 1) * hc + y + 1] = own_ref[x * cols + y]
    for y in range(cols):
        p_ref[y + 1] = above_ref[y * B:(y + 1) * B]
        p_ref[(rows + 1) * hc + y + 1] = below_ref[y * B:(y + 1) * B]
    for x in range(rows + 2):
        p_ref[x * hc] = left_ref[x * B:(x + 1) * B]
        p_ref[x * hc + hc - 1] = right_ref[x * B:(x + 1) * B]

    def one_patch(i, carry):
        row = pl.multiple_of(i * B, B)
        for w in range(WIN * WIN):
            acc_ref[w] = part_ref[pl.ds(row, B), w * B:(w + 1) * B]
        acc_ref[TRASH] = jnp.zeros((B, B), jnp.float32)
        x = i // AG
        y = i % AG
        count = count_ref[x, y]
        for k in range(KA):
            pos = pos_ref[x, y, k]
            inside, _ = is_local(pos)

            @pl.when(jnp.logical_not(inside) & (k < count))
            def _():
                term = jnp.dot(a_ref[i, :, k * B:(k + 1) * B], p_ref[pos],
                               preferred_element_type=jnp.float32)
                for q in range(KP):
                    s = nslot_ref[pos * KP + q]
                    acc_ref[s] = acc_ref[s] + term[:, q * B:(q + 1) * B]

        for w in range(WIN * WIN):
            prod_ref[pl.ds(row, B), w * B:(w + 1) * B] = acc_ref[w].astype(jnp.bfloat16)
        return carry

    lax.fori_loop(0, patches, one_patch, 0)

    prod = prod_ref[...]
    group = HOME * B
    for out, at in ((to_right_ref, 0), (keep_ref, 1), (to_left_ref, 2)):
        terms = jnp.dot(dpt_ref[at * group:(at + 1) * group], prod,
                        preferred_element_type=jnp.float32)
        out[...] = terms.reshape(out.shape).astype(out.dtype)


def fold_cols_kernel(keep_ref, left_ref, right_ref, keep_out, minus_out, plus_out):
    src_w = WIN * B
    dst_w = OUTW * B
    for d in range(HOME):
        out = (minus_out, keep_out, plus_out)[d]
        for sx in range(WIN):
            lo = sx * dst_w
            s0 = sx * src_w
            own = keep_ref[d, :, s0:s0 + src_w]
            left = left_ref[d, :, s0:s0 + src_w].astype(jnp.float32)
            right = right_ref[d, :, s0:s0 + src_w].astype(jnp.float32)
            first = left[:, :B]
            mid = left[:, B:2 * B] + own[:, :B]
            core = left[:, 2 * B:] + own[:, B:src_w - B] + right[:, :src_w - 2 * B]
            tail = own[:, src_w - B:] + right[:, src_w - 2 * B:src_w - B]
            last = right[:, src_w - B:]
            out[:, lo:lo + B] = first.astype(out.dtype)
            out[:, lo + B:lo + 2 * B] = mid.astype(out.dtype)
            out[:, lo + 2 * B:lo + 5 * B] = core.astype(out.dtype)
            out[:, lo + 5 * B:lo + 6 * B] = tail.astype(out.dtype)
            out[:, lo + 6 * B:lo + 7 * B] = last.astype(out.dtype)


def fold_rows_kernel(keep_ref, up_ref, down_ref, out_ref):
    band = OUTW * B
    for s in range(OUTW):
        parts = []
        if 1 <= s <= WIN:
            parts.append(keep_ref[:, (s - 1) * band:s * band])
        if s <= WIN - 1:
            parts.append(up_ref[:, s * band:(s + 1) * band].astype(jnp.float32))
        if s >= 2:
            parts.append(down_ref[:, (s - 2) * band:(s - 1) * band].astype(jnp.float32))
        total = parts[0]
        for extra in parts[1:]:
            total = total + extra
        out_ref[:, s * band:(s + 1) * band] = total.astype(out_ref.dtype)


def per_device(
    fine_blocks, fine_columns, fine_counts, prolong_blocks, prolong_columns, prolong_counts
):
    tile_rows, tile_cols = fine_counts.shape
    assert tile_rows == AG and tile_cols == AG
    patches = tile_rows * tile_cols
    grid_cols = tile_cols * lax.axis_size("col")
    coarse_grid_cols = lax.axis_size("col")
    row_index = lax.axis_index("row")
    col_index = lax.axis_index("col")

    prolong = prolong_blocks
    entries = jnp.arange(KP, dtype=jnp.int32)
    kept = entries[None, None, :] < prolong_counts[:, :, None]

    own_codes = prolong_columns
    hrow = jnp.clip(own_codes // coarse_grid_cols - row_index + 1, 0, HOME - 1)
    hcol = jnp.clip(own_codes % coarse_grid_cols - col_index + 1, 0, HOME - 1)
    rel = jnp.where(kept, hrow * HOME + hcol, HOME * HOME)
    home_rc = hcol * HOME + hrow

    def payload(p_part, rel_part):
        count = p_part.shape[0]
        flat = p_part.reshape(count * B, KP * B)
        extra = jnp.zeros((16, KP * B), jnp.bfloat16)
        extra = extra.at[0, :count * KP].set(rel_part.reshape(-1).astype(jnp.bfloat16))
        return jnp.concatenate([flat, extra], axis=0)

    def unpack(got, count):
        p_part = got[:count * B].reshape(count, B, KP * B)
        rel_part = got[count * B, :count * KP].astype(jnp.int32).reshape(count, KP)
        return p_part, rel_part

    hr, hc = tile_rows + 2, tile_cols + 2
    above_in = shifted(payload(prolong[tile_rows - 1], rel[tile_rows - 1]), 1, 0)
    below_in = shifted(payload(prolong[0], rel[0]), -1, 0)
    above, above_rel = unpack(above_in, tile_cols)
    below, below_rel = unpack(below_in, tile_cols)
    tall = jnp.concatenate([above[None], prolong, below[None]], axis=0)
    tall_rel = jnp.concatenate([above_rel[None], rel, below_rel[None]], axis=0)
    left_in = shifted(payload(tall[:, tile_cols - 1], tall_rel[:, tile_cols - 1]), 0, 1)
    right_in = shifted(payload(tall[:, 0], tall_rel[:, 0]), 0, -1)
    left_rel = unpack(left_in, hr)[1]
    right_rel = unpack(right_in, hr)[1]
    near_rel = jnp.concatenate([left_rel[:, None], tall_rel, right_rel[:, None]], axis=1)

    off_r = (jnp.arange(hr, dtype=jnp.int32) + tile_rows - 1) // tile_rows - 1
    off_c = (jnp.arange(hc, dtype=jnp.int32) + tile_cols - 1) // tile_cols - 1
    near_slot = (near_rel // HOME + off_r[:, None, None] + 1) * WIN + near_rel % HOME + off_c[None, :, None] + 1
    near_slot = jnp.where(near_rel < HOME * HOME, near_slot, TRASH).reshape(hr * hc * KP)

    first_row = row_index * tile_rows
    first_col = col_index * tile_cols
    targets = fine_columns
    pos = (targets // grid_cols - first_row + 1) * hc + targets % grid_cols - first_col + 1
    pos = jnp.clip(pos, 0, hr * hc - 1)
    home = jnp.where(kept, home_rc, HOME * HOME)

    smem = pltpu.MemorySpace.SMEM
    vmem = pltpu.MemorySpace.VMEM
    width = WIN * WIN * B
    local_slot = (rel // HOME + 1) * WIN + rel % HOME + 1
    local_slot = jnp.where(rel < HOME * HOME, local_slot, TRASH)
    part, dpt = pl.pallas_call(
        local_kernel,
        out_shape=(
            jax.ShapeDtypeStruct((patches * B, width), jnp.float32),
            jax.ShapeDtypeStruct(((HOME * HOME + 1) * B, patches * B), jnp.bfloat16),
        ),
        in_specs=[pl.BlockSpec(memory_space=smem)] * 4 + [pl.BlockSpec(memory_space=vmem)] * 2,
        out_specs=(pl.BlockSpec(memory_space=vmem),) * 2,
        scratch_shapes=[
            pltpu.VMEM((TRASH + 1, B, B), jnp.float32),
            pltpu.VMEM(((HOME * HOME + 1) * B, patches * B), jnp.float32),
        ],
    )(
        pos.astype(jnp.int32),
        local_slot.astype(jnp.int32),
        fine_counts.astype(jnp.int32),
        home.astype(jnp.int32),
        fine_blocks.reshape(patches, B, KA * B),
        prolong.reshape(patches, B, KP * B),
    )
    keep, to_right, to_left = pl.pallas_call(
        galerkin_kernel,
        out_shape=(
            jax.ShapeDtypeStruct((HOME, B, width), jnp.float32),
            jax.ShapeDtypeStruct((HOME, B, width), SEND),
            jax.ShapeDtypeStruct((HOME, B, width), SEND),
        ),
        in_specs=[pl.BlockSpec(memory_space=smem)] * 3 + [pl.BlockSpec(memory_space=vmem)] * 8,
        out_specs=(pl.BlockSpec(memory_space=vmem),) * 3,
        scratch_shapes=[
            pltpu.VMEM((TRASH + 1, B, B), jnp.float32),
            pltpu.VMEM((patches * B, width), jnp.bfloat16),
            pltpu.VMEM((hr * hc, B, KP * B), jnp.bfloat16),
        ],
    )(
        pos.astype(jnp.int32),
        near_slot.astype(jnp.int32),
        fine_counts.astype(jnp.int32),
        fine_blocks.reshape(patches, B, KA * B),
        prolong.reshape(patches, B, KP * B),
        above_in,
        below_in,
        left_in,
        right_in,
        part,
        dpt,
    )
    from_left = shifted(to_left, 0, 1)
    from_right = shifted(to_right, 0, -1)
    band = WIN * OUTW * B
    keep2, minus, plus = pl.pallas_call(
        fold_cols_kernel,
        out_shape=(
            jax.ShapeDtypeStruct((B, band), jnp.float32),
            jax.ShapeDtypeStruct((B, band), SEND),
            jax.ShapeDtypeStruct((B, band), SEND),
        ),
        in_specs=[pl.BlockSpec(memory_space=vmem)] * 3,
        out_specs=(pl.BlockSpec(memory_space=vmem),) * 3,
    )(keep, from_left, from_right)
    up_in = shifted(plus, 1, 0)
    down_in = shifted(minus, -1, 0)
    out = pl.pallas_call(
        fold_rows_kernel,
        out_shape=jax.ShapeDtypeStruct((B, OUTW * OUTW * B), jnp.bfloat16),
        in_specs=[pl.BlockSpec(memory_space=vmem)] * 3,
        out_specs=pl.BlockSpec(memory_space=vmem),
    )(keep2, up_in, down_in)
    return out.reshape(1, 1, B, OUTW * OUTW * B)


def solution(mesh):
    in_specs = (
        P("row", "col", None, None),
        P("row", "col", None),
        P("row", "col"),
        P("row", "col", None, None),
        P("row", "col", None),
        P("row", "col"),
    )
    out_specs = P("row", "col", None, None)
    return jax.shard_map(
        per_device, mesh=mesh, in_specs=in_specs, out_specs=out_specs, check_vma=False
    )
```

```python
import jax
import jax.numpy as jnp
from jax import lax
from jax.experimental import pallas as pl
from jax.experimental.pallas import tpu as pltpu
from jax.sharding import PartitionSpec as P

B = 64
KA = 9
KP = 4
AG = 4

NEAR = 3
WIN = 5
HOME = 3
OUTW = 7
TRASH = WIN * WIN
SEND = jnp.bfloat16


def shifted(value, by_row, by_col):
    rows = lax.axis_size("row")
    cols = lax.axis_size("col")
    pairs = []
    for r in range(rows):
        for c in range(cols):
            tr, tc = r + by_row, c + by_col
            if 0 <= tr < rows and 0 <= tc < cols:
                pairs.append((r * cols + c, tr * cols + tc))
    return lax.ppermute(value, ("row", "col"), pairs)


def galerkin_kernel(pos_ref, nslot_ref, count_ref, home_ref, a_ref, own_ref, above_ref, below_ref,
                    left_ref, right_ref, keep_ref, to_right_ref, to_left_ref,
                    acc_ref, prod_ref, dpt_ref, p_ref):
    patches = a_ref.shape[0]
    rows, cols = AG, AG
    hc = cols + 2
    for x in range(rows):
        for y in range(cols):
            p_ref[(x + 1) * hc + y + 1] = own_ref[x * cols + y]
    for y in range(cols):
        p_ref[y + 1] = above_ref[y * B:(y + 1) * B]
        p_ref[(rows + 1) * hc + y + 1] = below_ref[y * B:(y + 1) * B]
    for x in range(rows + 2):
        p_ref[x * hc] = left_ref[x * B:(x + 1) * B]
        p_ref[x * hc + hc - 1] = right_ref[x * B:(x + 1) * B]

    def one_patch(i, carry):
        acc_ref[...] = jnp.zeros(acc_ref.shape, jnp.float32)
        x = i // AG
        y = i % AG
        count = count_ref[x, y]
        for k in range(KA):
            pos = pos_ref[x, y, k]
            a_blk = a_ref[i, :, k * B:(k + 1) * B]
            term = jnp.dot(a_blk, p_ref[pos], preferred_element_type=jnp.float32)
            for q in range(KP):
                s = jnp.where(k < count, nslot_ref[pos * KP + q], TRASH)
                acc_ref[s] = acc_ref[s] + term[:, q * B:(q + 1) * B]
        row = pl.multiple_of(i * B, B)
        for w in range(WIN * WIN):
            prod_ref[pl.ds(row, B), w * B:(w + 1) * B] = acc_ref[w].astype(jnp.bfloat16)
        return carry

    lax.fori_loop(0, patches, one_patch, 0)

    dpt_ref[...] = jnp.zeros(dpt_ref.shape, jnp.float32)
    for i in range(patches):
        flipped = own_ref[i].astype(jnp.float32).T
        for p in range(KP):
            start = pl.multiple_of(home_ref[i // AG, i % AG, p] * B, B)
            dpt_ref[pl.ds(start, B), i * B:(i + 1) * B] += flipped[p * B:(p + 1) * B, :]

    prod = prod_ref[...]
    group = HOME * B
    for out, at in ((to_right_ref, 0), (keep_ref, 1), (to_left_ref, 2)):
        terms = jnp.dot(dpt_ref[at * group:(at + 1) * group].astype(jnp.bfloat16), prod,
                        preferred_element_type=jnp.float32)
        out[...] = terms.reshape(out.shape).astype(out.dtype)


def fold_cols_band(keep_ref, left_ref, right_ref, d, out):
    src_w = WIN * B
    dst_w = OUTW * B
    for sx in range(WIN):
        lo = sx * dst_w
        s0 = sx * src_w
        own = keep_ref[d, :, s0:s0 + src_w]
        left = left_ref[d, :, s0:s0 + src_w].astype(jnp.float32)
        right = right_ref[d, :, s0:s0 + src_w].astype(jnp.float32)
        first = left[:, :B]
        mid = left[:, B:2 * B] + own[:, :B]
        core = left[:, 2 * B:] + own[:, B:src_w - B] + right[:, :src_w - 2 * B]
        tail = own[:, src_w - B:] + right[:, src_w - 2 * B:src_w - B]
        last = right[:, src_w - B:]
        out[:, lo:lo + B] = first.astype(out.dtype)
        out[:, lo + B:lo + 2 * B] = mid.astype(out.dtype)
        out[:, lo + 2 * B:lo + 5 * B] = core.astype(out.dtype)
        out[:, lo + 5 * B:lo + 6 * B] = tail.astype(out.dtype)
        out[:, lo + 6 * B:lo + 7 * B] = last.astype(out.dtype)


def fold_cols_send_kernel(keep_ref, left_ref, right_ref, minus_out, plus_out):
    fold_cols_band(keep_ref, left_ref, right_ref, 0, minus_out)
    fold_cols_band(keep_ref, left_ref, right_ref, 2, plus_out)


def fold_cols_keep_kernel(keep_ref, left_ref, right_ref, keep_out):
    fold_cols_band(keep_ref, left_ref, right_ref, 1, keep_out)


def fold_rows_kernel(keep_ref, up_ref, down_ref, out_ref):
    band = OUTW * B
    for s in range(OUTW):
        parts = []
        if 1 <= s <= WIN:
            parts.append(keep_ref[:, (s - 1) * band:s * band])
        if s <= WIN - 1:
            parts.append(up_ref[:, s * band:(s + 1) * band].astype(jnp.float32))
        if s >= 2:
            parts.append(down_ref[:, (s - 2) * band:(s - 1) * band].astype(jnp.float32))
        total = parts[0]
        for extra in parts[1:]:
            total = total + extra
        out_ref[:, s * band:(s + 1) * band] = total.astype(out_ref.dtype)


def per_device(
    fine_blocks, fine_columns, fine_counts, prolong_blocks, prolong_columns, prolong_counts
):
    tile_rows, tile_cols = fine_counts.shape
    assert tile_rows == AG and tile_cols == AG
    patches = tile_rows * tile_cols
    grid_cols = tile_cols * lax.axis_size("col")
    coarse_grid_cols = lax.axis_size("col")
    row_index = lax.axis_index("row")
    col_index = lax.axis_index("col")

    prolong = prolong_blocks
    entries = jnp.arange(KP, dtype=jnp.int32)
    kept = entries[None, None, :] < prolong_counts[:, :, None]

    own_codes = prolong_columns
    hrow = jnp.clip(own_codes // coarse_grid_cols - row_index + 1, 0, HOME - 1)
    hcol = jnp.clip(own_codes % coarse_grid_cols - col_index + 1, 0, HOME - 1)
    rel = jnp.where(kept, hrow * HOME + hcol, HOME * HOME)
    home_rc = hcol * HOME + hrow

    def payload(p_part, rel_part):
        count = p_part.shape[0]
        flat = p_part.reshape(count * B, KP * B)
        extra = jnp.zeros((16, KP * B), jnp.bfloat16)
        extra = extra.at[0, :count * KP].set(rel_part.reshape(-1).astype(jnp.bfloat16))
        return jnp.concatenate([flat, extra], axis=0)

    def unpack(got, count):
        p_part = got[:count * B].reshape(count, B, KP * B)
        rel_part = got[count * B, :count * KP].astype(jnp.int32).reshape(count, KP)
        return p_part, rel_part

    hr, hc = tile_rows + 2, tile_cols + 2
    above_in = shifted(payload(prolong[tile_rows - 1], rel[tile_rows - 1]), 1, 0)
    below_in = shifted(payload(prolong[0], rel[0]), -1, 0)
    above, above_rel = unpack(above_in, tile_cols)
    below, below_rel = unpack(below_in, tile_cols)
    tall = jnp.concatenate([above[None], prolong, below[None]], axis=0)
    tall_rel = jnp.concatenate([above_rel[None], rel, below_rel[None]], axis=0)
    left_in = shifted(payload(tall[:, tile_cols - 1], tall_rel[:, tile_cols - 1]), 0, 1)
    right_in = shifted(payload(tall[:, 0], tall_rel[:, 0]), 0, -1)
    left_rel = unpack(left_in, hr)[1]
    right_rel = unpack(right_in, hr)[1]
    near_rel = jnp.concatenate([left_rel[:, None], tall_rel, right_rel[:, None]], axis=1)

    off_r = (jnp.arange(hr, dtype=jnp.int32) + tile_rows - 1) // tile_rows - 1
    off_c = (jnp.arange(hc, dtype=jnp.int32) + tile_cols - 1) // tile_cols - 1
    near_slot = (near_rel // HOME + off_r[:, None, None] + 1) * WIN + near_rel % HOME + off_c[None, :, None] + 1
    near_slot = jnp.where(near_rel < HOME * HOME, near_slot, TRASH).reshape(hr * hc * KP)

    first_row = row_index * tile_rows
    first_col = col_index * tile_cols
    targets = fine_columns
    pos = (targets // grid_cols - first_row + 1) * hc + targets % grid_cols - first_col + 1
    pos = jnp.clip(pos, 0, hr * hc - 1)
    home = jnp.where(kept, home_rc, HOME * HOME)

    smem = pltpu.MemorySpace.SMEM
    vmem = pltpu.MemorySpace.VMEM
    width = WIN * WIN * B
    keep, to_right, to_left = pl.pallas_call(
        galerkin_kernel,
        out_shape=(
            jax.ShapeDtypeStruct((HOME, B, width), jnp.float32),
            jax.ShapeDtypeStruct((HOME, B, width), SEND),
            jax.ShapeDtypeStruct((HOME, B, width), SEND),
        ),
        in_specs=[pl.BlockSpec(memory_space=smem)] * 4 + [pl.BlockSpec(memory_space=vmem)] * 6,
        out_specs=(pl.BlockSpec(memory_space=vmem),) * 3,
        scratch_shapes=[
            pltpu.VMEM((TRASH + 1, B, B), jnp.float32),
            pltpu.VMEM((patches * B, width), jnp.bfloat16),
            pltpu.VMEM(((HOME * HOME + 1) * B, patches * B), jnp.float32),
            pltpu.VMEM((hr * hc, B, KP * B), jnp.bfloat16),
        ],
    )(
        pos.astype(jnp.int32),
        near_slot.astype(jnp.int32),
        fine_counts.astype(jnp.int32),
        home.astype(jnp.int32),
        fine_blocks.reshape(patches, B, KA * B),
        prolong.reshape(patches, B, KP * B),
        above_in,
        below_in,
        left_in,
        right_in,
    )
    from_left = shifted(to_left, 0, 1)
    from_right = shifted(to_right, 0, -1)
    band = WIN * OUTW * B
    minus, plus = pl.pallas_call(
        fold_cols_send_kernel,
        out_shape=(
            jax.ShapeDtypeStruct((B, band), SEND),
            jax.ShapeDtypeStruct((B, band), SEND),
        ),
        in_specs=[pl.BlockSpec(memory_space=vmem)] * 3,
        out_specs=(pl.BlockSpec(memory_space=vmem),) * 2,
    )(keep, from_left, from_right)
    keep2 = pl.pallas_call(
        fold_cols_keep_kernel,
        out_shape=jax.ShapeDtypeStruct((B, band), jnp.float32),
        in_specs=[pl.BlockSpec(memory_space=vmem)] * 3,
        out_specs=pl.BlockSpec(memory_space=vmem),
    )(keep, from_left, from_right)
    up_in = shifted(plus, 1, 0)
    down_in = shifted(minus, -1, 0)
    out = pl.pallas_call(
        fold_rows_kernel,
        out_shape=jax.ShapeDtypeStruct((B, OUTW * OUTW * B), jnp.bfloat16),
        in_specs=[pl.BlockSpec(memory_space=vmem)] * 3,
        out_specs=pl.BlockSpec(memory_space=vmem),
    )(keep2, up_in, down_in)
    return out.reshape(1, 1, B, OUTW * OUTW * B)


def solution(mesh):
    in_specs = (
        P("row", "col", None, None),
        P("row", "col", None),
        P("row", "col"),
        P("row", "col", None, None),
        P("row", "col", None),
        P("row", "col"),
    )
    out_specs = P("row", "col", None, None)
    return jax.shard_map(
        per_device, mesh=mesh, in_specs=in_specs, out_specs=out_specs, check_vma=False
    )
```

```python
import jax
import jax.numpy as jnp
from jax import lax
from jax.experimental import pallas as pl
from jax.experimental.pallas import tpu as pltpu
from jax.sharding import PartitionSpec as P

B = 64
KA = 9
KP = 4
AG = 4

NEAR = 3
WIN = 5
HOME = 3
OUTW = 7
TRASH = WIN * WIN
SEND = jnp.bfloat16


def shifted(value, by_row, by_col):
    rows = lax.axis_size("row")
    cols = lax.axis_size("col")
    pairs = []
    for r in range(rows):
        for c in range(cols):
            tr, tc = r + by_row, c + by_col
            if 0 <= tr < rows and 0 <= tc < cols:
                pairs.append((r * cols + c, tr * cols + tc))
    return lax.ppermute(value, ("row", "col"), pairs)


def galerkin_kernel(pos_ref, nslot_ref, count_ref, home_ref, a_ref, own_ref, above_ref, below_ref,
                    left_ref, right_ref, keep_ref, to_right_ref, to_left_ref,
                    acc_ref, prod_ref, dpt_ref, p_ref):
    patches = a_ref.shape[0]
    rows, cols = AG, AG
    hc = cols + 2
    for x in range(rows):
        for y in range(cols):
            p_ref[(x + 1) * hc + y + 1] = own_ref[x * cols + y]
    for y in range(cols):
        p_ref[y + 1] = above_ref[y * B:(y + 1) * B]
        p_ref[(rows + 1) * hc + y + 1] = below_ref[y * B:(y + 1) * B]
    for x in range(rows + 2):
        p_ref[x * hc] = left_ref[x * B:(x + 1) * B]
        p_ref[x * hc + hc - 1] = right_ref[x * B:(x + 1) * B]

    def one_patch(i, carry):
        acc_ref[...] = jnp.zeros(acc_ref.shape, jnp.float32)
        x = i // AG
        y = i % AG
        count = count_ref[x, y]
        for k in range(KA):
            pos = pos_ref[x, y, k]
            a_blk = a_ref[i, :, k * B:(k + 1) * B]
            term = jnp.dot(a_blk, p_ref[pos], preferred_element_type=jnp.float32)
            for q in range(KP):
                s = jnp.where(k < count, nslot_ref[pos * KP + q], TRASH)
                acc_ref[s] = acc_ref[s] + term[:, q * B:(q + 1) * B]
        row = pl.multiple_of(i * B, B)
        for w in range(WIN * WIN):
            prod_ref[pl.ds(row, B), w * B:(w + 1) * B] = acc_ref[w].astype(jnp.bfloat16)
        return carry

    lax.fori_loop(0, patches, one_patch, 0)

    dpt_ref[...] = jnp.zeros(dpt_ref.shape, jnp.float32)
    for i in range(patches):
        flipped = own_ref[i].astype(jnp.float32).T
        for p in range(KP):
            start = pl.multiple_of(home_ref[i // AG, i % AG, p] * B, B)
            dpt_ref[pl.ds(start, B), i * B:(i + 1) * B] += flipped[p * B:(p + 1) * B, :]

    prod = prod_ref[...]
    group = HOME * B
    for out, at in ((to_right_ref, 0), (keep_ref, 1), (to_left_ref, 2)):
        terms = jnp.dot(dpt_ref[at * group:(at + 1) * group].astype(jnp.bfloat16), prod,
                        preferred_element_type=jnp.float32)
        out[...] = terms.reshape(out.shape).astype(out.dtype)


def fold_cols_band(keep_ref, left_ref, right_ref, d, out):
    src_w = WIN * B
    dst_w = OUTW * B
    for sx in range(WIN):
        lo = sx * dst_w
        s0 = sx * src_w
        own = keep_ref[d, :, s0:s0 + src_w]
        left = left_ref[d, :, s0:s0 + src_w].astype(jnp.float32)
        right = right_ref[d, :, s0:s0 + src_w].astype(jnp.float32)
        first = left[:, :B]
        mid = left[:, B:2 * B] + own[:, :B]
        core = left[:, 2 * B:] + own[:, B:src_w - B] + right[:, :src_w - 2 * B]
        tail = own[:, src_w - B:] + right[:, src_w - 2 * B:src_w - B]
        last = right[:, src_w - B:]
        out[:, lo:lo + B] = first.astype(out.dtype)
        out[:, lo + B:lo + 2 * B] = mid.astype(out.dtype)
        out[:, lo + 2 * B:lo + 5 * B] = core.astype(out.dtype)
        out[:, lo + 5 * B:lo + 6 * B] = tail.astype(out.dtype)
        out[:, lo + 6 * B:lo + 7 * B] = last.astype(out.dtype)


def fold_cols_send_kernel(keep_ref, left_ref, right_ref, minus_out, plus_out):
    fold_cols_band(keep_ref, left_ref, right_ref, 0, minus_out)
    fold_cols_band(keep_ref, left_ref, right_ref, 2, plus_out)


def fold_cols_keep_kernel(keep_ref, left_ref, right_ref, keep_out):
    fold_cols_band(keep_ref, left_ref, right_ref, 1, keep_out)


def fold_rows_kernel(keep_ref, up_ref, down_ref, out_ref):
    band = OUTW * B
    for s in range(OUTW):
        parts = []
        if 1 <= s <= WIN:
            parts.append(keep_ref[:, (s - 1) * band:s * band])
        if s <= WIN - 1:
            parts.append(up_ref[:, s * band:(s + 1) * band].astype(jnp.float32))
        if s >= 2:
            parts.append(down_ref[:, (s - 2) * band:(s - 1) * band].astype(jnp.float32))
        total = parts[0]
        for extra in parts[1:]:
            total = total + extra
        out_ref[:, s * band:(s + 1) * band] = total.astype(out_ref.dtype)


def per_device(
    fine_blocks, fine_columns, fine_counts, prolong_blocks, prolong_columns, prolong_counts
):
    tile_rows, tile_cols = fine_counts.shape
    assert tile_rows == AG and tile_cols == AG
    patches = tile_rows * tile_cols
    grid_cols = tile_cols * lax.axis_size("col")
    coarse_grid_cols = lax.axis_size("col")
    row_index = lax.axis_index("row")
    col_index = lax.axis_index("col")

    prolong = prolong_blocks
    entries = jnp.arange(KP, dtype=jnp.int32)
    kept = entries[None, None, :] < prolong_counts[:, :, None]

    own_codes = prolong_columns
    hrow = jnp.clip(own_codes // coarse_grid_cols - row_index + 1, 0, HOME - 1)
    hcol = jnp.clip(own_codes % coarse_grid_cols - col_index + 1, 0, HOME - 1)
    rel = jnp.where(kept, hrow * WIN + hcol, 4 * TRASH)
    home_rc = hcol * HOME + hrow

    def payload(p_part, rel_part):
        count = p_part.shape[0]
        flat = p_part.reshape(count * B, KP * B)
        extra = jnp.pad(rel_part.reshape(1, count * KP).astype(jnp.bfloat16),
                        ((0, 15), (0, KP * B - count * KP)))
        return jnp.concatenate([flat, extra], axis=0)

    def unpack(got, count):
        p_part = got[:count * B].reshape(count, B, KP * B)
        rel_part = got[count * B, :count * KP].astype(jnp.int32).reshape(count, KP)
        return p_part, rel_part

    hr, hc = tile_rows + 2, tile_cols + 2
    above_in = shifted(payload(prolong[tile_rows - 1], rel[tile_rows - 1]), 1, 0)
    below_in = shifted(payload(prolong[0], rel[0]), -1, 0)
    above, above_rel = unpack(above_in, tile_cols)
    below, below_rel = unpack(below_in, tile_cols)
    tall = jnp.concatenate([above[None], prolong, below[None]], axis=0)
    tall_rel = jnp.concatenate([above_rel[None], rel, below_rel[None]], axis=0)
    left_in = shifted(payload(tall[:, tile_cols - 1], tall_rel[:, tile_cols - 1]), 0, 1)
    right_in = shifted(payload(tall[:, 0], tall_rel[:, 0]), 0, -1)
    left_rel = unpack(left_in, hr)[1]
    right_rel = unpack(right_in, hr)[1]
    near_rel = jnp.concatenate([left_rel[:, None], tall_rel, right_rel[:, None]], axis=1)

    off_r = (jnp.arange(hr, dtype=jnp.int32) + tile_rows - 1) // tile_rows - 1
    off_c = (jnp.arange(hc, dtype=jnp.int32) + tile_cols - 1) // tile_cols - 1
    base = (off_r[:, None, None] + 1) * WIN + off_c[None, :, None] + 1
    near_slot = jnp.minimum(near_rel + base, TRASH).reshape(hr * hc * KP)

    first_row = row_index * tile_rows
    first_col = col_index * tile_cols
    targets = fine_columns
    pos = (targets // grid_cols - first_row + 1) * hc + targets % grid_cols - first_col + 1
    pos = jnp.clip(pos, 0, hr * hc - 1)
    home = jnp.where(kept, home_rc, HOME * HOME)

    smem = pltpu.MemorySpace.SMEM
    vmem = pltpu.MemorySpace.VMEM
    width = WIN * WIN * B
    keep, to_right, to_left = pl.pallas_call(
        galerkin_kernel,
        out_shape=(
            jax.ShapeDtypeStruct((HOME, B, width), jnp.float32),
            jax.ShapeDtypeStruct((HOME, B, width), SEND),
            jax.ShapeDtypeStruct((HOME, B, width), SEND),
        ),
        in_specs=[pl.BlockSpec(memory_space=smem)] * 4 + [pl.BlockSpec(memory_space=vmem)] * 6,
        out_specs=(pl.BlockSpec(memory_space=vmem),) * 3,
        scratch_shapes=[
            pltpu.VMEM((TRASH + 1, B, B), jnp.float32),
            pltpu.VMEM((patches * B, width), jnp.bfloat16),
            pltpu.VMEM(((HOME * HOME + 1) * B, patches * B), jnp.float32),
            pltpu.VMEM((hr * hc, B, KP * B), jnp.bfloat16),
        ],
    )(
        pos.astype(jnp.int32),
        near_slot.astype(jnp.int32),
        fine_counts.astype(jnp.int32),
        home.astype(jnp.int32),
        fine_blocks.reshape(patches, B, KA * B),
        prolong.reshape(patches, B, KP * B),
        above_in,
        below_in,
        left_in,
        right_in,
    )
    from_left = shifted(to_left, 0, 1)
    from_right = shifted(to_right, 0, -1)
    band = WIN * OUTW * B
    minus, plus = pl.pallas_call(
        fold_cols_send_kernel,
        out_shape=(
            jax.ShapeDtypeStruct((B, band), SEND),
            jax.ShapeDtypeStruct((B, band), SEND),
        ),
        in_specs=[pl.BlockSpec(memory_space=vmem)] * 3,
        out_specs=(pl.BlockSpec(memory_space=vmem),) * 2,
    )(keep, from_left, from_right)
    keep2 = pl.pallas_call(
        fold_cols_keep_kernel,
        out_shape=jax.ShapeDtypeStruct((B, band), jnp.float32),
        in_specs=[pl.BlockSpec(memory_space=vmem)] * 3,
        out_specs=pl.BlockSpec(memory_space=vmem),
    )(keep, from_left, from_right)
    up_in = shifted(plus, 1, 0)
    down_in = shifted(minus, -1, 0)
    out = pl.pallas_call(
        fold_rows_kernel,
        out_shape=jax.ShapeDtypeStruct((B, OUTW * OUTW * B), jnp.bfloat16),
        in_specs=[pl.BlockSpec(memory_space=vmem)] * 3,
        out_specs=pl.BlockSpec(memory_space=vmem),
    )(keep2, up_in, down_in)
    return out.reshape(1, 1, B, OUTW * OUTW * B)


def solution(mesh):
    in_specs = (
        P("row", "col", None, None),
        P("row", "col", None),
        P("row", "col"),
        P("row", "col", None, None),
        P("row", "col", None),
        P("row", "col"),
    )
    out_specs = P("row", "col", None, None)
    return jax.shard_map(
        per_device, mesh=mesh, in_specs=in_specs, out_specs=out_specs, check_vma=False
    )
```

```python
import jax
import jax.numpy as jnp
from jax import lax
from jax.experimental import pallas as pl
from jax.experimental.pallas import tpu as pltpu
from jax.sharding import PartitionSpec as P

B = 64
KA = 9
KP = 4
AG = 4

NEAR = 3
WIN = 5
HOME = 3
OUTW = 7
TRASH = WIN * WIN
SEND = jnp.bfloat16


def shifted(value, by_row, by_col):
    rows = lax.axis_size("row")
    cols = lax.axis_size("col")
    pairs = []
    for r in range(rows):
        for c in range(cols):
            tr, tc = r + by_row, c + by_col
            if 0 <= tr < rows and 0 <= tc < cols:
                pairs.append((r * cols + c, tr * cols + tc))
    return lax.ppermute(value, ("row", "col"), pairs)


def exchange(to_prev, to_next, axis):
    count = lax.axis_size(axis)
    even = lax.axis_index(axis) % 2 == 0
    first = [(j, j ^ 1) for j in range(count) if (j ^ 1) < count]
    second = [(j, j + 1) for j in range(1, count - 1, 2)] + [(j + 1, j) for j in range(1, count - 1, 2)]
    got_first = lax.ppermute(jnp.where(even, to_next, to_prev), axis, first)
    got_second = lax.ppermute(jnp.where(even, to_prev, to_next), axis, second)
    from_prev = jnp.where(even, got_second, got_first)
    from_next = jnp.where(even, got_first, got_second)
    return from_prev, from_next


def galerkin_kernel(pos_ref, nslot_ref, count_ref, home_ref, a_ref, own_ref, above_ref, below_ref,
                    left_ref, right_ref, keep_ref, to_right_ref, to_left_ref,
                    acc_ref, prod_ref, dpt_ref, p_ref):
    patches = a_ref.shape[0]
    rows, cols = AG, AG
    hc = cols + 2
    for x in range(rows):
        for y in range(cols):
            p_ref[(x + 1) * hc + y + 1] = own_ref[x * cols + y]
    for y in range(cols):
        p_ref[y + 1] = above_ref[y * B:(y + 1) * B]
        p_ref[(rows + 1) * hc + y + 1] = below_ref[y * B:(y + 1) * B]
    for x in range(rows + 2):
        p_ref[x * hc] = left_ref[x * B:(x + 1) * B]
        p_ref[x * hc + hc - 1] = right_ref[x * B:(x + 1) * B]

    def one_patch(i, carry):
        acc_ref[...] = jnp.zeros(acc_ref.shape, jnp.float32)
        x = i // AG
        y = i % AG
        count = count_ref[x, y]
        for k in range(KA):
            pos = pos_ref[x, y, k]
            a_blk = a_ref[i, :, k * B:(k + 1) * B]
            term = jnp.dot(a_blk, p_ref[pos], preferred_element_type=jnp.float32)
            for q in range(KP):
                s = jnp.where(k < count, nslot_ref[pos * KP + q], TRASH)
                acc_ref[s] = acc_ref[s] + term[:, q * B:(q + 1) * B]
        row = pl.multiple_of(i * B, B)
        for w in range(WIN * WIN):
            prod_ref[pl.ds(row, B), w * B:(w + 1) * B] = acc_ref[w].astype(jnp.bfloat16)
        return carry

    lax.fori_loop(0, patches, one_patch, 0)

    dpt_ref[...] = jnp.zeros(dpt_ref.shape, jnp.float32)
    for i in range(patches):
        flipped = own_ref[i].astype(jnp.float32).T
        for p in range(KP):
            start = pl.multiple_of(home_ref[i // AG, i % AG, p] * B, B)
            dpt_ref[pl.ds(start, B), i * B:(i + 1) * B] += flipped[p * B:(p + 1) * B, :]

    prod = prod_ref[...]
    group = HOME * B
    for out, at in ((to_right_ref, 0), (keep_ref, 1), (to_left_ref, 2)):
        terms = jnp.dot(dpt_ref[at * group:(at + 1) * group].astype(jnp.bfloat16), prod,
                        preferred_element_type=jnp.float32)
        out[...] = terms.reshape(out.shape).astype(out.dtype)


def fold_cols_band(keep_ref, left_ref, right_ref, d, out):
    src_w = WIN * B
    dst_w = OUTW * B
    for sx in range(WIN):
        lo = sx * dst_w
        s0 = sx * src_w
        own = keep_ref[d, :, s0:s0 + src_w]
        left = left_ref[d, :, s0:s0 + src_w].astype(jnp.float32)
        right = right_ref[d, :, s0:s0 + src_w].astype(jnp.float32)
        first = left[:, :B]
        mid = left[:, B:2 * B] + own[:, :B]
        core = left[:, 2 * B:] + own[:, B:src_w - B] + right[:, :src_w - 2 * B]
        tail = own[:, src_w - B:] + right[:, src_w - 2 * B:src_w - B]
        last = right[:, src_w - B:]
        out[:, lo:lo + B] = first.astype(out.dtype)
        out[:, lo + B:lo + 2 * B] = mid.astype(out.dtype)
        out[:, lo + 2 * B:lo + 5 * B] = core.astype(out.dtype)
        out[:, lo + 5 * B:lo + 6 * B] = tail.astype(out.dtype)
        out[:, lo + 6 * B:lo + 7 * B] = last.astype(out.dtype)


def fold_cols_send_kernel(keep_ref, left_ref, right_ref, minus_out, plus_out):
    fold_cols_band(keep_ref, left_ref, right_ref, 0, minus_out)
    fold_cols_band(keep_ref, left_ref, right_ref, 2, plus_out)


def fold_cols_keep_kernel(keep_ref, left_ref, right_ref, keep_out):
    fold_cols_band(keep_ref, left_ref, right_ref, 1, keep_out)


def fold_rows_kernel(keep_ref, up_ref, down_ref, out_ref):
    band = OUTW * B
    for s in range(OUTW):
        parts = []
        if 1 <= s <= WIN:
            parts.append(keep_ref[:, (s - 1) * band:s * band])
        if s <= WIN - 1:
            parts.append(up_ref[:, s * band:(s + 1) * band].astype(jnp.float32))
        if s >= 2:
            parts.append(down_ref[:, (s - 2) * band:(s - 1) * band].astype(jnp.float32))
        total = parts[0]
        for extra in parts[1:]:
            total = total + extra
        out_ref[:, s * band:(s + 1) * band] = total.astype(out_ref.dtype)


def per_device(
    fine_blocks, fine_columns, fine_counts, prolong_blocks, prolong_columns, prolong_counts
):
    tile_rows, tile_cols = fine_counts.shape
    assert tile_rows == AG and tile_cols == AG
    patches = tile_rows * tile_cols
    grid_cols = tile_cols * lax.axis_size("col")
    coarse_grid_cols = lax.axis_size("col")
    row_index = lax.axis_index("row")
    col_index = lax.axis_index("col")

    prolong = prolong_blocks
    entries = jnp.arange(KP, dtype=jnp.int32)
    kept = entries[None, None, :] < prolong_counts[:, :, None]

    own_codes = prolong_columns
    hrow = jnp.clip(own_codes // coarse_grid_cols - row_index + 1, 0, HOME - 1)
    hcol = jnp.clip(own_codes % coarse_grid_cols - col_index + 1, 0, HOME - 1)
    rel = jnp.where(kept, hrow * WIN + hcol, 4 * TRASH)
    home_rc = hcol * HOME + hrow

    def payload(p_part, rel_part):
        count = p_part.shape[0]
        flat = p_part.reshape(count * B, KP * B)
        extra = jnp.pad(rel_part.reshape(1, count * KP).astype(jnp.bfloat16),
                        ((0, 15), (0, KP * B - count * KP)))
        return jnp.concatenate([flat, extra], axis=0)

    def unpack(got, count):
        p_part = got[:count * B].reshape(count, B, KP * B)
        rel_part = got[count * B, :count * KP].astype(jnp.int32).reshape(count, KP)
        return p_part, rel_part

    hr, hc = tile_rows + 2, tile_cols + 2
    above_in, below_in = exchange(
        payload(prolong[0], rel[0]), payload(prolong[tile_rows - 1], rel[tile_rows - 1]), "row")
    above, above_rel = unpack(above_in, tile_cols)
    below, below_rel = unpack(below_in, tile_cols)
    tall = jnp.concatenate([above[None], prolong, below[None]], axis=0)
    tall_rel = jnp.concatenate([above_rel[None], rel, below_rel[None]], axis=0)
    left_in, right_in = exchange(
        payload(tall[:, 0], tall_rel[:, 0]), payload(tall[:, tile_cols - 1], tall_rel[:, tile_cols - 1]), "col")
    left_rel = unpack(left_in, hr)[1]
    right_rel = unpack(right_in, hr)[1]
    near_rel = jnp.concatenate([left_rel[:, None], tall_rel, right_rel[:, None]], axis=1)

    off_r = (jnp.arange(hr, dtype=jnp.int32) + tile_rows - 1) // tile_rows - 1
    off_c = (jnp.arange(hc, dtype=jnp.int32) + tile_cols - 1) // tile_cols - 1
    base = (off_r[:, None, None] + 1) * WIN + off_c[None, :, None] + 1
    near_slot = jnp.minimum(near_rel + base, TRASH).reshape(hr * hc * KP)

    first_row = row_index * tile_rows
    first_col = col_index * tile_cols
    targets = fine_columns
    pos = (targets // grid_cols - first_row + 1) * hc + targets % grid_cols - first_col + 1
    pos = jnp.clip(pos, 0, hr * hc - 1)
    home = jnp.where(kept, home_rc, HOME * HOME)

    smem = pltpu.MemorySpace.SMEM
    vmem = pltpu.MemorySpace.VMEM
    width = WIN * WIN * B
    keep, to_right, to_left = pl.pallas_call(
        galerkin_kernel,
        out_shape=(
            jax.ShapeDtypeStruct((HOME, B, width), jnp.float32),
            jax.ShapeDtypeStruct((HOME, B, width), SEND),
            jax.ShapeDtypeStruct((HOME, B, width), SEND),
        ),
        in_specs=[pl.BlockSpec(memory_space=smem)] * 4 + [pl.BlockSpec(memory_space=vmem)] * 6,
        out_specs=(pl.BlockSpec(memory_space=vmem),) * 3,
        scratch_shapes=[
            pltpu.VMEM((TRASH + 1, B, B), jnp.float32),
            pltpu.VMEM((patches * B, width), jnp.bfloat16),
            pltpu.VMEM(((HOME * HOME + 1) * B, patches * B), jnp.float32),
            pltpu.VMEM((hr * hc, B, KP * B), jnp.bfloat16),
        ],
    )(
        pos.astype(jnp.int32),
        near_slot.astype(jnp.int32),
        fine_counts.astype(jnp.int32),
        home.astype(jnp.int32),
        fine_blocks.reshape(patches, B, KA * B),
        prolong.reshape(patches, B, KP * B),
        above_in,
        below_in,
        left_in,
        right_in,
    )
    from_left, from_right = exchange(to_right, to_left, "col")
    band = WIN * OUTW * B
    minus, plus = pl.pallas_call(
        fold_cols_send_kernel,
        out_shape=(
            jax.ShapeDtypeStruct((B, band), SEND),
            jax.ShapeDtypeStruct((B, band), SEND),
        ),
        in_specs=[pl.BlockSpec(memory_space=vmem)] * 3,
        out_specs=(pl.BlockSpec(memory_space=vmem),) * 2,
    )(keep, from_left, from_right)
    keep2 = pl.pallas_call(
        fold_cols_keep_kernel,
        out_shape=jax.ShapeDtypeStruct((B, band), jnp.float32),
        in_specs=[pl.BlockSpec(memory_space=vmem)] * 3,
        out_specs=pl.BlockSpec(memory_space=vmem),
    )(keep, from_left, from_right)
    up_in, down_in = exchange(minus, plus, "row")
    out = pl.pallas_call(
        fold_rows_kernel,
        out_shape=jax.ShapeDtypeStruct((B, OUTW * OUTW * B), jnp.bfloat16),
        in_specs=[pl.BlockSpec(memory_space=vmem)] * 3,
        out_specs=pl.BlockSpec(memory_space=vmem),
    )(keep2, up_in, down_in)
    return out.reshape(1, 1, B, OUTW * OUTW * B)


def solution(mesh):
    in_specs = (
        P("row", "col", None, None),
        P("row", "col", None),
        P("row", "col"),
        P("row", "col", None, None),
        P("row", "col", None),
        P("row", "col"),
    )
    out_specs = P("row", "col", None, None)
    return jax.shard_map(
        per_device, mesh=mesh, in_specs=in_specs, out_specs=out_specs, check_vma=False
    )
```

```python
import jax
import jax.numpy as jnp
from jax import lax
from jax.experimental import pallas as pl
from jax.experimental.pallas import tpu as pltpu
from jax.sharding import PartitionSpec as P

B = 64
KA = 9
KP = 4
AG = 4

NEAR = 3
WIN = 5
HOME = 3
OUTW = 7
TRASH = WIN * WIN
SEND = jnp.bfloat16


def shifted(value, by_row, by_col):
    rows = lax.axis_size("row")
    cols = lax.axis_size("col")
    pairs = []
    for r in range(rows):
        for c in range(cols):
            tr, tc = r + by_row, c + by_col
            if 0 <= tr < rows and 0 <= tc < cols:
                pairs.append((r * cols + c, tr * cols + tc))
    return lax.ppermute(value, ("row", "col"), pairs)


def exchange(to_prev, to_next, axis):
    count = lax.axis_size(axis)
    even = lax.axis_index(axis) % 2 == 0
    first = [(j, j ^ 1) for j in range(count) if (j ^ 1) < count]
    second = [(j, j + 1) for j in range(1, count - 1, 2)] + [(j + 1, j) for j in range(1, count - 1, 2)]
    got_first = lax.ppermute(jnp.where(even, to_next, to_prev), axis, first)
    got_second = lax.ppermute(jnp.where(even, to_prev, to_next), axis, second)
    from_prev = jnp.where(even, got_second, got_first)
    from_next = jnp.where(even, got_first, got_second)
    return from_prev, from_next


def swap_rounds(first, second, axis):
    count = lax.axis_size(axis)
    pairs_a = [(j, j ^ 1) for j in range(count) if (j ^ 1) < count]
    pairs_b = [(j, j + 1) for j in range(1, count - 1, 2)] + [(j + 1, j) for j in range(1, count - 1, 2)]
    return lax.ppermute(first, axis, pairs_a), lax.ppermute(second, axis, pairs_b)


def galerkin_kernel(par_ref, pos_ref, nslot_ref, count_ref, home_ref, a_ref, own_ref, above_ref, below_ref,
                    left_ref, right_ref, keep_ref, first_ref, second_ref,
                    acc_ref, prod_ref, dpt_ref, p_ref):
    patches = a_ref.shape[0]
    rows, cols = AG, AG
    hc = cols + 2
    for x in range(rows):
        for y in range(cols):
            p_ref[(x + 1) * hc + y + 1] = own_ref[x * cols + y]
    for y in range(cols):
        p_ref[y + 1] = above_ref[y * B:(y + 1) * B]
        p_ref[(rows + 1) * hc + y + 1] = below_ref[y * B:(y + 1) * B]
    for x in range(rows + 2):
        p_ref[x * hc] = left_ref[x * B:(x + 1) * B]
        p_ref[x * hc + hc - 1] = right_ref[x * B:(x + 1) * B]

    def one_patch(i, carry):
        acc_ref[...] = jnp.zeros(acc_ref.shape, jnp.float32)
        x = i // AG
        y = i % AG
        count = count_ref[x, y]
        for k in range(KA):
            pos = pos_ref[x, y, k]
            a_blk = a_ref[i, :, k * B:(k + 1) * B]
            term = jnp.dot(a_blk, p_ref[pos], preferred_element_type=jnp.float32)
            for q in range(KP):
                s = jnp.where(k < count, nslot_ref[pos * KP + q], TRASH)
                acc_ref[s] = acc_ref[s] + term[:, q * B:(q + 1) * B]
        row = pl.multiple_of(i * B, B)
        for w in range(WIN * WIN):
            prod_ref[pl.ds(row, B), w * B:(w + 1) * B] = acc_ref[w].astype(jnp.bfloat16)
        return carry

    lax.fori_loop(0, patches, one_patch, 0)

    dpt_ref[...] = jnp.zeros(dpt_ref.shape, jnp.float32)
    for i in range(patches):
        flipped = own_ref[i].astype(jnp.float32).T
        for p in range(KP):
            start = pl.multiple_of(home_ref[i // AG, i % AG, p] * B, B)
            dpt_ref[pl.ds(start, B), i * B:(i + 1) * B] += flipped[p * B:(p + 1) * B, :]

    prod = prod_ref[...]
    group = HOME * B
    odd = par_ref[0]
    for out, at in ((first_ref, 2 - 2 * odd), (keep_ref, 1), (second_ref, 2 * odd)):
        start = pl.multiple_of(at * group, group)
        terms = jnp.dot(dpt_ref[pl.ds(start, group)].astype(jnp.bfloat16), prod,
                        preferred_element_type=jnp.float32)
        out[...] = terms.reshape(out.shape).astype(out.dtype)


def fold_cols_band(keep_ref, a_ref, b_ref, even, d, out):
    src_w = WIN * B
    dst_w = OUTW * B
    for sx in range(WIN):
        lo = sx * dst_w
        s0 = sx * src_w
        own = keep_ref[d, :, s0:s0 + src_w]
        got_a = a_ref[d, :, s0:s0 + src_w].astype(jnp.float32)
        got_b = b_ref[d, :, s0:s0 + src_w].astype(jnp.float32)
        left = jnp.where(even, got_b, got_a)
        right = jnp.where(even, got_a, got_b)
        first = left[:, :B]
        mid = left[:, B:2 * B] + own[:, :B]
        core = left[:, 2 * B:] + own[:, B:src_w - B] + right[:, :src_w - 2 * B]
        tail = own[:, src_w - B:] + right[:, src_w - 2 * B:src_w - B]
        last = right[:, src_w - B:]
        out[:, lo:lo + B] = first.astype(out.dtype)
        out[:, lo + B:lo + 2 * B] = mid.astype(out.dtype)
        out[:, lo + 2 * B:lo + 5 * B] = core.astype(out.dtype)
        out[:, lo + 5 * B:lo + 6 * B] = tail.astype(out.dtype)
        out[:, lo + 6 * B:lo + 7 * B] = last.astype(out.dtype)


def fold_cols_send_kernel(par_ref, keep_ref, a_ref, b_ref, first_out, second_out):
    even_col = par_ref[0] == 0
    odd_row = par_ref[1]
    fold_cols_band(keep_ref, a_ref, b_ref, even_col, 2 - 2 * odd_row, first_out)
    fold_cols_band(keep_ref, a_ref, b_ref, even_col, 2 * odd_row, second_out)


def fold_cols_keep_kernel(par_ref, keep_ref, a_ref, b_ref, keep_out):
    fold_cols_band(keep_ref, a_ref, b_ref, par_ref[0] == 0, 1, keep_out)


def fold_rows_kernel(par_ref, keep_ref, a_ref, b_ref, out_ref):
    band = OUTW * B
    even = par_ref[1] == 0
    for s in range(OUTW):
        parts = []
        if 1 <= s <= WIN:
            parts.append(keep_ref[:, (s - 1) * band:s * band])
        if s <= WIN - 1:
            lanes = slice(s * band, (s + 1) * band)
            parts.append(jnp.where(even, b_ref[:, lanes], a_ref[:, lanes]).astype(jnp.float32))
        if s >= 2:
            lanes = slice((s - 2) * band, (s - 1) * band)
            parts.append(jnp.where(even, a_ref[:, lanes], b_ref[:, lanes]).astype(jnp.float32))
        total = parts[0]
        for extra in parts[1:]:
            total = total + extra
        out_ref[:, s * band:(s + 1) * band] = total.astype(out_ref.dtype)


def per_device(
    fine_blocks, fine_columns, fine_counts, prolong_blocks, prolong_columns, prolong_counts
):
    tile_rows, tile_cols = fine_counts.shape
    assert tile_rows == AG and tile_cols == AG
    patches = tile_rows * tile_cols
    grid_cols = tile_cols * lax.axis_size("col")
    coarse_grid_cols = lax.axis_size("col")
    row_index = lax.axis_index("row")
    col_index = lax.axis_index("col")

    prolong = prolong_blocks
    entries = jnp.arange(KP, dtype=jnp.int32)
    kept = entries[None, None, :] < prolong_counts[:, :, None]

    own_codes = prolong_columns
    hrow = jnp.clip(own_codes // coarse_grid_cols - row_index + 1, 0, HOME - 1)
    hcol = jnp.clip(own_codes % coarse_grid_cols - col_index + 1, 0, HOME - 1)
    rel = jnp.where(kept, hrow * WIN + hcol, 4 * TRASH)
    home_rc = hcol * HOME + hrow

    def payload(p_part, rel_part):
        count = p_part.shape[0]
        flat = p_part.reshape(count * B, KP * B)
        extra = jnp.pad(rel_part.reshape(1, count * KP).astype(jnp.bfloat16),
                        ((0, 15), (0, KP * B - count * KP)))
        return jnp.concatenate([flat, extra], axis=0)

    def unpack(got, count):
        p_part = got[:count * B].reshape(count, B, KP * B)
        rel_part = got[count * B, :count * KP].astype(jnp.int32).reshape(count, KP)
        return p_part, rel_part

    hr, hc = tile_rows + 2, tile_cols + 2
    above_in, below_in = exchange(
        payload(prolong[0], rel[0]), payload(prolong[tile_rows - 1], rel[tile_rows - 1]), "row")
    above, above_rel = unpack(above_in, tile_cols)
    below, below_rel = unpack(below_in, tile_cols)
    tall = jnp.concatenate([above[None], prolong, below[None]], axis=0)
    tall_rel = jnp.concatenate([above_rel[None], rel, below_rel[None]], axis=0)
    left_in, right_in = exchange(
        payload(tall[:, 0], tall_rel[:, 0]), payload(tall[:, tile_cols - 1], tall_rel[:, tile_cols - 1]), "col")
    left_rel = unpack(left_in, hr)[1]
    right_rel = unpack(right_in, hr)[1]
    near_rel = jnp.concatenate([left_rel[:, None], tall_rel, right_rel[:, None]], axis=1)

    off_r = (jnp.arange(hr, dtype=jnp.int32) + tile_rows - 1) // tile_rows - 1
    off_c = (jnp.arange(hc, dtype=jnp.int32) + tile_cols - 1) // tile_cols - 1
    base = (off_r[:, None, None] + 1) * WIN + off_c[None, :, None] + 1
    near_slot = jnp.minimum(near_rel + base, TRASH).reshape(hr * hc * KP)

    first_row = row_index * tile_rows
    first_col = col_index * tile_cols
    targets = fine_columns
    pos = (targets // grid_cols - first_row + 1) * hc + targets % grid_cols - first_col + 1
    pos = jnp.clip(pos, 0, hr * hc - 1)
    home = jnp.where(kept, home_rc, HOME * HOME)

    smem = pltpu.MemorySpace.SMEM
    vmem = pltpu.MemorySpace.VMEM
    width = WIN * WIN * B
    parity = jnp.stack([col_index % 2, row_index % 2]).astype(jnp.int32)
    keep, first, second = pl.pallas_call(
        galerkin_kernel,
        out_shape=(
            jax.ShapeDtypeStruct((HOME, B, width), jnp.float32),
            jax.ShapeDtypeStruct((HOME, B, width), SEND),
            jax.ShapeDtypeStruct((HOME, B, width), SEND),
        ),
        in_specs=[pl.BlockSpec(memory_space=smem)] * 5 + [pl.BlockSpec(memory_space=vmem)] * 6,
        out_specs=(pl.BlockSpec(memory_space=vmem),) * 3,
        scratch_shapes=[
            pltpu.VMEM((TRASH + 1, B, B), jnp.float32),
            pltpu.VMEM((patches * B, width), jnp.bfloat16),
            pltpu.VMEM(((HOME * HOME + 1) * B, patches * B), jnp.float32),
            pltpu.VMEM((hr * hc, B, KP * B), jnp.bfloat16),
        ],
    )(
        parity,
        pos.astype(jnp.int32),
        near_slot.astype(jnp.int32),
        fine_counts.astype(jnp.int32),
        home.astype(jnp.int32),
        fine_blocks.reshape(patches, B, KA * B),
        prolong.reshape(patches, B, KP * B),
        above_in,
        below_in,
        left_in,
        right_in,
    )
    got_a, got_b = swap_rounds(first, second, "col")
    band = WIN * OUTW * B
    first2, second2 = pl.pallas_call(
        fold_cols_send_kernel,
        out_shape=(
            jax.ShapeDtypeStruct((B, band), SEND),
            jax.ShapeDtypeStruct((B, band), SEND),
        ),
        in_specs=[pl.BlockSpec(memory_space=smem)] + [pl.BlockSpec(memory_space=vmem)] * 3,
        out_specs=(pl.BlockSpec(memory_space=vmem),) * 2,
    )(parity, keep, got_a, got_b)
    keep2 = pl.pallas_call(
        fold_cols_keep_kernel,
        out_shape=jax.ShapeDtypeStruct((B, band), jnp.float32),
        in_specs=[pl.BlockSpec(memory_space=smem)] + [pl.BlockSpec(memory_space=vmem)] * 3,
        out_specs=pl.BlockSpec(memory_space=vmem),
    )(parity, keep, got_a, got_b)
    row_a, row_b = swap_rounds(first2, second2, "row")
    out = pl.pallas_call(
        fold_rows_kernel,
        out_shape=jax.ShapeDtypeStruct((B, OUTW * OUTW * B), jnp.bfloat16),
        in_specs=[pl.BlockSpec(memory_space=smem)] + [pl.BlockSpec(memory_space=vmem)] * 3,
        out_specs=pl.BlockSpec(memory_space=vmem),
    )(parity, keep2, row_a, row_b)
    return out.reshape(1, 1, B, OUTW * OUTW * B)


def solution(mesh):
    in_specs = (
        P("row", "col", None, None),
        P("row", "col", None),
        P("row", "col"),
        P("row", "col", None, None),
        P("row", "col", None),
        P("row", "col"),
    )
    out_specs = P("row", "col", None, None)
    return jax.shard_map(
        per_device, mesh=mesh, in_specs=in_specs, out_specs=out_specs, check_vma=False
    )
```

```python
import jax
import jax.numpy as jnp
from jax import lax
from jax.experimental import pallas as pl
from jax.experimental.pallas import tpu as pltpu
from jax.sharding import PartitionSpec as P

B = 64
KA = 9
KP = 4
AG = 4

NEAR = 3
WIN = 5
HOME = 3
OUTW = 7
TRASH = WIN * WIN
SEND = jnp.bfloat16


def shifted(value, by_row, by_col):
    rows = lax.axis_size("row")
    cols = lax.axis_size("col")
    pairs = []
    for r in range(rows):
        for c in range(cols):
            tr, tc = r + by_row, c + by_col
            if 0 <= tr < rows and 0 <= tc < cols:
                pairs.append((r * cols + c, tr * cols + tc))
    return lax.ppermute(value, ("row", "col"), pairs)


def exchange(to_prev, to_next, axis):
    count = lax.axis_size(axis)
    even = lax.axis_index(axis) % 2 == 0
    first = [(j, j ^ 1) for j in range(count) if (j ^ 1) < count]
    second = [(j, j + 1) for j in range(1, count - 1, 2)] + [(j + 1, j) for j in range(1, count - 1, 2)]
    got_first = lax.ppermute(jnp.where(even, to_next, to_prev), axis, first)
    got_second = lax.ppermute(jnp.where(even, to_prev, to_next), axis, second)
    from_prev = jnp.where(even, got_second, got_first)
    from_next = jnp.where(even, got_first, got_second)
    return from_prev, from_next


def swap_rounds(first, second, axis):
    count = lax.axis_size(axis)
    pairs_a = [(j, j ^ 1) for j in range(count) if (j ^ 1) < count]
    pairs_b = [(j, j + 1) for j in range(1, count - 1, 2)] + [(j + 1, j) for j in range(1, count - 1, 2)]
    return lax.ppermute(first, axis, pairs_a), lax.ppermute(second, axis, pairs_b)


def galerkin_kernel(par_ref, pos_ref, nslot_ref, count_ref, home_ref, a_ref, own_ref, above_ref, below_ref,
                    left_ref, right_ref, keep_ref, first_ref, second_ref,
                    acc_ref, prod_ref, dpt_ref, p_ref):
    patches = a_ref.shape[0]
    rows, cols = AG, AG
    hc = cols + 2
    for x in range(rows):
        for y in range(cols):
            p_ref[(x + 1) * hc + y + 1] = own_ref[x * cols + y]
    for y in range(cols):
        p_ref[y + 1] = above_ref[y * B:(y + 1) * B]
        p_ref[(rows + 1) * hc + y + 1] = below_ref[y * B:(y + 1) * B]
    for x in range(rows + 2):
        p_ref[x * hc] = left_ref[x * B:(x + 1) * B]
        p_ref[x * hc + hc - 1] = right_ref[x * B:(x + 1) * B]

    def one_patch(i, carry):
        acc_ref[...] = jnp.zeros(acc_ref.shape, jnp.float32)
        x = i // AG
        y = i % AG
        count = count_ref[x, y]
        for k in range(KA):
            pos = pos_ref[x, y, k]
            a_blk = a_ref[i, :, k * B:(k + 1) * B]
            term = jnp.dot(a_blk, p_ref[pos], preferred_element_type=jnp.float32)
            for q in range(KP):
                s = jnp.where(k < count, nslot_ref[pos * KP + q], TRASH)
                acc_ref[s] = acc_ref[s] + term[:, q * B:(q + 1) * B]
        row = pl.multiple_of(i * B, B)
        for w in range(WIN * WIN):
            prod_ref[pl.ds(row, B), w * B:(w + 1) * B] = acc_ref[w].astype(jnp.bfloat16)
        return carry

    lax.fori_loop(0, patches, one_patch, 0)

    dpt_ref[...] = jnp.zeros(dpt_ref.shape, jnp.float32)
    for i in range(patches):
        flipped = own_ref[i].astype(jnp.float32).T
        for p in range(KP):
            start = pl.multiple_of(home_ref[i // AG, i % AG, p] * B, B)
            dpt_ref[pl.ds(start, B), i * B:(i + 1) * B] += flipped[p * B:(p + 1) * B, :]

    prod = prod_ref[...]
    group = HOME * B
    odd = par_ref[0]
    for out, at in ((first_ref, 2 - 2 * odd), (keep_ref, 1), (second_ref, 2 * odd)):
        start = pl.multiple_of(at * group, group)
        terms = jnp.dot(dpt_ref[pl.ds(start, group)].astype(jnp.bfloat16), prod,
                        preferred_element_type=jnp.float32)
        out[...] = terms.reshape(out.shape).astype(out.dtype)


def fold_cols_band(keep_ref, a_ref, b_ref, even, d, out, shift=0):
    src_w = WIN * B
    dst_w = OUTW * B
    for sx in range(WIN):
        lo = (sx + shift) * dst_w
        s0 = sx * src_w
        own = keep_ref[d, :, s0:s0 + src_w]
        got_a = a_ref[d, :, s0:s0 + src_w].astype(jnp.float32)
        got_b = b_ref[d, :, s0:s0 + src_w].astype(jnp.float32)
        left = jnp.where(even, got_b, got_a)
        right = jnp.where(even, got_a, got_b)
        first = left[:, :B]
        mid = left[:, B:2 * B] + own[:, :B]
        core = left[:, 2 * B:] + own[:, B:src_w - B] + right[:, :src_w - 2 * B]
        tail = own[:, src_w - B:] + right[:, src_w - 2 * B:src_w - B]
        last = right[:, src_w - B:]
        out[:, lo:lo + B] = first.astype(out.dtype)
        out[:, lo + B:lo + 2 * B] = mid.astype(out.dtype)
        out[:, lo + 2 * B:lo + 5 * B] = core.astype(out.dtype)
        out[:, lo + 5 * B:lo + 6 * B] = tail.astype(out.dtype)
        out[:, lo + 6 * B:lo + 7 * B] = last.astype(out.dtype)


def fold_cols_send_kernel(par_ref, keep_ref, a_ref, b_ref, first_out, second_out):
    even_col = par_ref[0] == 0
    odd_row = par_ref[1]
    fold_cols_band(keep_ref, a_ref, b_ref, even_col, 2 - 2 * odd_row, first_out)
    fold_cols_band(keep_ref, a_ref, b_ref, even_col, 2 * odd_row, second_out)


def fold_cols_keep_kernel(par_ref, keep_ref, a_ref, b_ref, keep_out):
    band = OUTW * B
    keep_out[:, :band] = jnp.zeros((B, band), keep_out.dtype)
    keep_out[:, (OUTW - 1) * band:] = jnp.zeros((B, band), keep_out.dtype)
    fold_cols_band(keep_ref, a_ref, b_ref, par_ref[0] == 0, 1, keep_out, shift=1)


def fold_rows_kernel(par_ref, keep_ref, a_ref, b_ref, out_ref):
    band = OUTW * B
    even = par_ref[1] == 0
    low = 2 * band
    high = WIN * band
    from_prev_lo = jnp.where(even, b_ref[:, :low], a_ref[:, :low]).astype(jnp.float32)
    out_ref[:, :low] = (keep_ref[:, :low] + from_prev_lo).astype(out_ref.dtype)
    from_prev_mid = jnp.where(even, b_ref[:, low:high], a_ref[:, low:high]).astype(jnp.float32)
    from_next_mid = jnp.where(even, a_ref[:, :high - low], b_ref[:, :high - low]).astype(jnp.float32)
    out_ref[:, low:high] = (keep_ref[:, low:high] + from_prev_mid + from_next_mid).astype(out_ref.dtype)
    from_next_hi = jnp.where(even, a_ref[:, high - low:], b_ref[:, high - low:]).astype(jnp.float32)
    out_ref[:, high:] = (keep_ref[:, high:] + from_next_hi).astype(out_ref.dtype)


def per_device(
    fine_blocks, fine_columns, fine_counts, prolong_blocks, prolong_columns, prolong_counts
):
    tile_rows, tile_cols = fine_counts.shape
    assert tile_rows == AG and tile_cols == AG
    patches = tile_rows * tile_cols
    grid_cols = tile_cols * lax.axis_size("col")
    coarse_grid_cols = lax.axis_size("col")
    row_index = lax.axis_index("row")
    col_index = lax.axis_index("col")

    prolong = prolong_blocks
    entries = jnp.arange(KP, dtype=jnp.int32)
    kept = entries[None, None, :] < prolong_counts[:, :, None]

    own_codes = prolong_columns
    hrow = jnp.clip(own_codes // coarse_grid_cols - row_index + 1, 0, HOME - 1)
    hcol = jnp.clip(own_codes % coarse_grid_cols - col_index + 1, 0, HOME - 1)
    rel = jnp.where(kept, hrow * WIN + hcol, 4 * TRASH)
    home_rc = hcol * HOME + hrow

    def payload(p_part, rel_part):
        count = p_part.shape[0]
        flat = p_part.reshape(count * B, KP * B)
        extra = jnp.pad(rel_part.reshape(1, count * KP).astype(jnp.bfloat16),
                        ((0, 15), (0, KP * B - count * KP)))
        return jnp.concatenate([flat, extra], axis=0)

    def unpack(got, count):
        p_part = got[:count * B].reshape(count, B, KP * B)
        rel_part = got[count * B, :count * KP].astype(jnp.int32).reshape(count, KP)
        return p_part, rel_part

    hr, hc = tile_rows + 2, tile_cols + 2
    above_in, below_in = exchange(
        payload(prolong[0], rel[0]), payload(prolong[tile_rows - 1], rel[tile_rows - 1]), "row")
    above, above_rel = unpack(above_in, tile_cols)
    below, below_rel = unpack(below_in, tile_cols)
    tall = jnp.concatenate([above[None], prolong, below[None]], axis=0)
    tall_rel = jnp.concatenate([above_rel[None], rel, below_rel[None]], axis=0)
    left_in, right_in = exchange(
        payload(tall[:, 0], tall_rel[:, 0]), payload(tall[:, tile_cols - 1], tall_rel[:, tile_cols - 1]), "col")
    left_rel = unpack(left_in, hr)[1]
    right_rel = unpack(right_in, hr)[1]
    near_rel = jnp.concatenate([left_rel[:, None], tall_rel, right_rel[:, None]], axis=1)

    off_r = (jnp.arange(hr, dtype=jnp.int32) + tile_rows - 1) // tile_rows - 1
    off_c = (jnp.arange(hc, dtype=jnp.int32) + tile_cols - 1) // tile_cols - 1
    base = (off_r[:, None, None] + 1) * WIN + off_c[None, :, None] + 1
    near_slot = jnp.minimum(near_rel + base, TRASH).reshape(hr * hc * KP)

    first_row = row_index * tile_rows
    first_col = col_index * tile_cols
    targets = fine_columns
    pos = (targets // grid_cols - first_row + 1) * hc + targets % grid_cols - first_col + 1
    pos = jnp.clip(pos, 0, hr * hc - 1)
    home = jnp.where(kept, home_rc, HOME * HOME)

    smem = pltpu.MemorySpace.SMEM
    vmem = pltpu.MemorySpace.VMEM
    width = WIN * WIN * B
    parity = jnp.stack([col_index % 2, row_index % 2]).astype(jnp.int32)
    keep, first, second = pl.pallas_call(
        galerkin_kernel,
        out_shape=(
            jax.ShapeDtypeStruct((HOME, B, width), jnp.float32),
            jax.ShapeDtypeStruct((HOME, B, width), SEND),
            jax.ShapeDtypeStruct((HOME, B, width), SEND),
        ),
        in_specs=[pl.BlockSpec(memory_space=smem)] * 5 + [pl.BlockSpec(memory_space=vmem)] * 6,
        out_specs=(pl.BlockSpec(memory_space=vmem),) * 3,
        scratch_shapes=[
            pltpu.VMEM((TRASH + 1, B, B), jnp.float32),
            pltpu.VMEM((patches * B, width), jnp.bfloat16),
            pltpu.VMEM(((HOME * HOME + 1) * B, patches * B), jnp.float32),
            pltpu.VMEM((hr * hc, B, KP * B), jnp.bfloat16),
        ],
    )(
        parity,
        pos.astype(jnp.int32),
        near_slot.astype(jnp.int32),
        fine_counts.astype(jnp.int32),
        home.astype(jnp.int32),
        fine_blocks.reshape(patches, B, KA * B),
        prolong.reshape(patches, B, KP * B),
        above_in,
        below_in,
        left_in,
        right_in,
    )
    got_a, got_b = swap_rounds(first, second, "col")
    band = WIN * OUTW * B
    first2, second2 = pl.pallas_call(
        fold_cols_send_kernel,
        out_shape=(
            jax.ShapeDtypeStruct((B, band), SEND),
            jax.ShapeDtypeStruct((B, band), SEND),
        ),
        in_specs=[pl.BlockSpec(memory_space=smem)] + [pl.BlockSpec(memory_space=vmem)] * 3,
        out_specs=(pl.BlockSpec(memory_space=vmem),) * 2,
    )(parity, keep, got_a, got_b)
    keep2 = pl.pallas_call(
        fold_cols_keep_kernel,
        out_shape=jax.ShapeDtypeStruct((B, OUTW * OUTW * B), jnp.float32),
        in_specs=[pl.BlockSpec(memory_space=smem)] + [pl.BlockSpec(memory_space=vmem)] * 3,
        out_specs=pl.BlockSpec(memory_space=vmem),
    )(parity, keep, got_a, got_b)
    row_a, row_b = swap_rounds(first2, second2, "row")
    out = pl.pallas_call(
        fold_rows_kernel,
        out_shape=jax.ShapeDtypeStruct((B, OUTW * OUTW * B), jnp.bfloat16),
        in_specs=[pl.BlockSpec(memory_space=smem)] + [pl.BlockSpec(memory_space=vmem)] * 3,
        out_specs=pl.BlockSpec(memory_space=vmem),
    )(parity, keep2, row_a, row_b)
    return out.reshape(1, 1, B, OUTW * OUTW * B)


def solution(mesh):
    in_specs = (
        P("row", "col", None, None),
        P("row", "col", None),
        P("row", "col"),
        P("row", "col", None, None),
        P("row", "col", None),
        P("row", "col"),
    )
    out_specs = P("row", "col", None, None)
    return jax.shard_map(
        per_device, mesh=mesh, in_specs=in_specs, out_specs=out_specs, check_vma=False
    )
```

```python
import jax
import jax.numpy as jnp
from jax import lax
from jax.experimental import pallas as pl
from jax.experimental.pallas import tpu as pltpu
from jax.sharding import PartitionSpec as P

B = 64
KA = 9
KP = 4
AG = 4

NEAR = 3
WIN = 5
HOME = 3
OUTW = 7
TRASH = WIN * WIN
SEND = jnp.bfloat16


def shifted(value, by_row, by_col):
    rows = lax.axis_size("row")
    cols = lax.axis_size("col")
    pairs = []
    for r in range(rows):
        for c in range(cols):
            tr, tc = r + by_row, c + by_col
            if 0 <= tr < rows and 0 <= tc < cols:
                pairs.append((r * cols + c, tr * cols + tc))
    return lax.ppermute(value, ("row", "col"), pairs)


def exchange(to_prev, to_next, axis):
    count = lax.axis_size(axis)
    even = lax.axis_index(axis) % 2 == 0
    first = [(j, j ^ 1) for j in range(count) if (j ^ 1) < count]
    second = [(j, j + 1) for j in range(1, count - 1, 2)] + [(j + 1, j) for j in range(1, count - 1, 2)]
    got_first = lax.ppermute(jnp.where(even, to_next, to_prev), axis, first)
    got_second = lax.ppermute(jnp.where(even, to_prev, to_next), axis, second)
    from_prev = jnp.where(even, got_second, got_first)
    from_next = jnp.where(even, got_first, got_second)
    return from_prev, from_next


def swap_rounds(first, second, axis):
    count = lax.axis_size(axis)
    pairs_a = [(j, j ^ 1) for j in range(count) if (j ^ 1) < count]
    pairs_b = [(j, j + 1) for j in range(1, count - 1, 2)] + [(j + 1, j) for j in range(1, count - 1, 2)]
    return lax.ppermute(first, axis, pairs_a), lax.ppermute(second, axis, pairs_b)


def galerkin_kernel(par_ref, pos_ref, nslot_ref, count_ref, home_ref, a_ref, own_ref, above_ref, below_ref,
                    left_ref, right_ref, keep_ref, first_ref, second_ref,
                    acc_ref, prod_ref, dpt_ref, p_ref):
    patches = a_ref.shape[0]
    rows, cols = AG, AG
    hc = cols + 2
    for x in range(rows):
        for y in range(cols):
            p_ref[(x + 1) * hc + y + 1] = own_ref[x * cols + y]
    for y in range(cols):
        p_ref[y + 1] = above_ref[y * B:(y + 1) * B]
        p_ref[(rows + 1) * hc + y + 1] = below_ref[y * B:(y + 1) * B]
    for x in range(rows + 2):
        p_ref[x * hc] = left_ref[x * B:(x + 1) * B]
        p_ref[x * hc + hc - 1] = right_ref[x * B:(x + 1) * B]

    def one_patch(i, carry):
        acc_ref[...] = jnp.zeros(acc_ref.shape, jnp.float32)
        x = i // AG
        y = i % AG
        count = count_ref[x, y]
        for k in range(KA):
            pos = pos_ref[x, y, k]
            a_blk = a_ref[i, :, k * B:(k + 1) * B]
            term = jnp.dot(a_blk, p_ref[pos], preferred_element_type=jnp.float32)
            for q in range(KP):
                s = jnp.where(k < count, nslot_ref[pos * KP + q], TRASH)
                acc_ref[s] = acc_ref[s] + term[:, q * B:(q + 1) * B]
        row = pl.multiple_of(i * B, B)
        for w in range(0, WIN * WIN - 1, 2):
            pair = jnp.concatenate([acc_ref[w], acc_ref[w + 1]], axis=1)
            prod_ref[pl.ds(row, B), w * B:(w + 2) * B] = pair.astype(jnp.bfloat16)
        last = WIN * WIN - 1
        prod_ref[pl.ds(row, B), last * B:(last + 1) * B] = acc_ref[last].astype(jnp.bfloat16)
        return carry

    lax.fori_loop(0, patches, one_patch, 0)

    dpt_ref[...] = jnp.zeros(dpt_ref.shape, jnp.float32)
    for i in range(patches):
        flipped = own_ref[i].astype(jnp.float32).T
        for p in range(KP):
            start = pl.multiple_of(home_ref[i // AG, i % AG, p] * B, B)
            dpt_ref[pl.ds(start, B), i * B:(i + 1) * B] += flipped[p * B:(p + 1) * B, :]

    prod = prod_ref[...]
    group = HOME * B
    odd = par_ref[0]
    for out, at in ((first_ref, 2 - 2 * odd), (keep_ref, 1), (second_ref, 2 * odd)):
        start = pl.multiple_of(at * group, group)
        terms = jnp.dot(dpt_ref[pl.ds(start, group)].astype(jnp.bfloat16), prod,
                        preferred_element_type=jnp.float32)
        out[...] = terms.reshape(out.shape).astype(out.dtype)


def fold_cols_band(keep_ref, a_ref, b_ref, even, d, out, shift=0):
    src_w = WIN * B
    dst_w = OUTW * B
    for sx in range(WIN):
        lo = (sx + shift) * dst_w
        s0 = sx * src_w
        own = keep_ref[d, :, s0:s0 + src_w]
        got_a = a_ref[d, :, s0:s0 + src_w].astype(jnp.float32)
        got_b = b_ref[d, :, s0:s0 + src_w].astype(jnp.float32)
        left = jnp.where(even, got_b, got_a)
        right = jnp.where(even, got_a, got_b)
        first = left[:, :B]
        mid = left[:, B:2 * B] + own[:, :B]
        core = left[:, 2 * B:] + own[:, B:src_w - B] + right[:, :src_w - 2 * B]
        tail = own[:, src_w - B:] + right[:, src_w - 2 * B:src_w - B]
        last = right[:, src_w - B:]
        out[:, lo:lo + B] = first.astype(out.dtype)
        out[:, lo + B:lo + 2 * B] = mid.astype(out.dtype)
        out[:, lo + 2 * B:lo + 5 * B] = core.astype(out.dtype)
        out[:, lo + 5 * B:lo + 6 * B] = tail.astype(out.dtype)
        out[:, lo + 6 * B:lo + 7 * B] = last.astype(out.dtype)


def fold_cols_send_kernel(par_ref, keep_ref, a_ref, b_ref, first_out, second_out):
    even_col = par_ref[0] == 0
    odd_row = par_ref[1]
    fold_cols_band(keep_ref, a_ref, b_ref, even_col, 2 - 2 * odd_row, first_out)
    fold_cols_band(keep_ref, a_ref, b_ref, even_col, 2 * odd_row, second_out)


def fold_cols_keep_kernel(par_ref, keep_ref, a_ref, b_ref, keep_out):
    band = OUTW * B
    keep_out[:, :band] = jnp.zeros((B, band), keep_out.dtype)
    keep_out[:, (OUTW - 1) * band:] = jnp.zeros((B, band), keep_out.dtype)
    fold_cols_band(keep_ref, a_ref, b_ref, par_ref[0] == 0, 1, keep_out, shift=1)


def fold_rows_kernel(par_ref, keep_ref, a_ref, b_ref, out_ref):
    band = OUTW * B
    even = par_ref[1] == 0
    low = 2 * band
    high = WIN * band
    from_prev_lo = jnp.where(even, b_ref[:, :low], a_ref[:, :low]).astype(jnp.float32)
    out_ref[:, :low] = (keep_ref[:, :low] + from_prev_lo).astype(out_ref.dtype)
    from_prev_mid = jnp.where(even, b_ref[:, low:high], a_ref[:, low:high]).astype(jnp.float32)
    from_next_mid = jnp.where(even, a_ref[:, :high - low], b_ref[:, :high - low]).astype(jnp.float32)
    out_ref[:, low:high] = (keep_ref[:, low:high] + from_prev_mid + from_next_mid).astype(out_ref.dtype)
    from_next_hi = jnp.where(even, a_ref[:, high - low:], b_ref[:, high - low:]).astype(jnp.float32)
    out_ref[:, high:] = (keep_ref[:, high:] + from_next_hi).astype(out_ref.dtype)


def per_device(
    fine_blocks, fine_columns, fine_counts, prolong_blocks, prolong_columns, prolong_counts
):
    tile_rows, tile_cols = fine_counts.shape
    assert tile_rows == AG and tile_cols == AG
    patches = tile_rows * tile_cols
    grid_cols = tile_cols * lax.axis_size("col")
    coarse_grid_cols = lax.axis_size("col")
    row_index = lax.axis_index("row")
    col_index = lax.axis_index("col")

    prolong = prolong_blocks
    entries = jnp.arange(KP, dtype=jnp.int32)
    kept = entries[None, None, :] < prolong_counts[:, :, None]

    own_codes = prolong_columns
    hrow = jnp.clip(own_codes // coarse_grid_cols - row_index + 1, 0, HOME - 1)
    hcol = jnp.clip(own_codes % coarse_grid_cols - col_index + 1, 0, HOME - 1)
    rel = jnp.where(kept, hrow * WIN + hcol, 4 * TRASH)
    home_rc = hcol * HOME + hrow

    def payload(p_part, rel_part):
        count = p_part.shape[0]
        flat = p_part.reshape(count * B, KP * B)
        extra = jnp.pad(rel_part.reshape(1, count * KP).astype(jnp.bfloat16),
                        ((0, 15), (0, KP * B - count * KP)))
        return jnp.concatenate([flat, extra], axis=0)

    def unpack(got, count):
        p_part = got[:count * B].reshape(count, B, KP * B)
        rel_part = got[count * B, :count * KP].astype(jnp.int32).reshape(count, KP)
        return p_part, rel_part

    hr, hc = tile_rows + 2, tile_cols + 2
    above_in, below_in = exchange(
        payload(prolong[0], rel[0]), payload(prolong[tile_rows - 1], rel[tile_rows - 1]), "row")
    above, above_rel = unpack(above_in, tile_cols)
    below, below_rel = unpack(below_in, tile_cols)
    tall = jnp.concatenate([above[None], prolong, below[None]], axis=0)
    tall_rel = jnp.concatenate([above_rel[None], rel, below_rel[None]], axis=0)
    left_in, right_in = exchange(
        payload(tall[:, 0], tall_rel[:, 0]), payload(tall[:, tile_cols - 1], tall_rel[:, tile_cols - 1]), "col")
    left_rel = unpack(left_in, hr)[1]
    right_rel = unpack(right_in, hr)[1]
    near_rel = jnp.concatenate([left_rel[:, None], tall_rel, right_rel[:, None]], axis=1)

    off_r = (jnp.arange(hr, dtype=jnp.int32) + tile_rows - 1) // tile_rows - 1
    off_c = (jnp.arange(hc, dtype=jnp.int32) + tile_cols - 1) // tile_cols - 1
    base = (off_r[:, None, None] + 1) * WIN + off_c[None, :, None] + 1
    near_slot = jnp.minimum(near_rel + base, TRASH).reshape(hr * hc * KP)

    first_row = row_index * tile_rows
    first_col = col_index * tile_cols
    targets = fine_columns
    pos = (targets // grid_cols - first_row + 1) * hc + targets % grid_cols - first_col + 1
    pos = jnp.clip(pos, 0, hr * hc - 1)
    home = jnp.where(kept, home_rc, HOME * HOME)

    smem = pltpu.MemorySpace.SMEM
    vmem = pltpu.MemorySpace.VMEM
    width = WIN * WIN * B
    parity = jnp.stack([col_index % 2, row_index % 2]).astype(jnp.int32)
    keep, first, second = pl.pallas_call(
        galerkin_kernel,
        out_shape=(
            jax.ShapeDtypeStruct((HOME, B, width), jnp.float32),
            jax.ShapeDtypeStruct((HOME, B, width), SEND),
            jax.ShapeDtypeStruct((HOME, B, width), SEND),
        ),
        in_specs=[pl.BlockSpec(memory_space=smem)] * 5 + [pl.BlockSpec(memory_space=vmem)] * 6,
        out_specs=(pl.BlockSpec(memory_space=vmem),) * 3,
        scratch_shapes=[
            pltpu.VMEM((TRASH + 1, B, B), jnp.float32),
            pltpu.VMEM((patches * B, width), jnp.bfloat16),
            pltpu.VMEM(((HOME * HOME + 1) * B, patches * B), jnp.float32),
            pltpu.VMEM((hr * hc, B, KP * B), jnp.bfloat16),
        ],
    )(
        parity,
        pos.astype(jnp.int32),
        near_slot.astype(jnp.int32),
        fine_counts.astype(jnp.int32),
        home.astype(jnp.int32),
        fine_blocks.reshape(patches, B, KA * B),
        prolong.reshape(patches, B, KP * B),
        above_in,
        below_in,
        left_in,
        right_in,
    )
    got_a, got_b = swap_rounds(first, second, "col")
    band = WIN * OUTW * B
    first2, second2 = pl.pallas_call(
        fold_cols_send_kernel,
        out_shape=(
            jax.ShapeDtypeStruct((B, band), SEND),
            jax.ShapeDtypeStruct((B, band), SEND),
        ),
        in_specs=[pl.BlockSpec(memory_space=smem)] + [pl.BlockSpec(memory_space=vmem)] * 3,
        out_specs=(pl.BlockSpec(memory_space=vmem),) * 2,
    )(parity, keep, got_a, got_b)
    keep2 = pl.pallas_call(
        fold_cols_keep_kernel,
        out_shape=jax.ShapeDtypeStruct((B, OUTW * OUTW * B), jnp.float32),
        in_specs=[pl.BlockSpec(memory_space=smem)] + [pl.BlockSpec(memory_space=vmem)] * 3,
        out_specs=pl.BlockSpec(memory_space=vmem),
    )(parity, keep, got_a, got_b)
    row_a, row_b = swap_rounds(first2, second2, "row")
    out = pl.pallas_call(
        fold_rows_kernel,
        out_shape=jax.ShapeDtypeStruct((B, OUTW * OUTW * B), jnp.bfloat16),
        in_specs=[pl.BlockSpec(memory_space=smem)] + [pl.BlockSpec(memory_space=vmem)] * 3,
        out_specs=pl.BlockSpec(memory_space=vmem),
    )(parity, keep2, row_a, row_b)
    return out.reshape(1, 1, B, OUTW * OUTW * B)


def solution(mesh):
    in_specs = (
        P("row", "col", None, None),
        P("row", "col", None),
        P("row", "col"),
        P("row", "col", None, None),
        P("row", "col", None),
        P("row", "col"),
    )
    out_specs = P("row", "col", None, None)
    return jax.shard_map(
        per_device, mesh=mesh, in_specs=in_specs, out_specs=out_specs, check_vma=False
    )
```

```python
import jax
import jax.numpy as jnp
from jax import lax
from jax.experimental import pallas as pl
from jax.experimental.pallas import tpu as pltpu
from jax.sharding import PartitionSpec as P

B = 64
KA = 9
KP = 4
AG = 4

NEAR = 3
WIN = 5
HOME = 3
OUTW = 7
TRASH = WIN * WIN
SEND = jnp.bfloat16


def shifted(value, by_row, by_col):
    rows = lax.axis_size("row")
    cols = lax.axis_size("col")
    pairs = []
    for r in range(rows):
        for c in range(cols):
            tr, tc = r + by_row, c + by_col
            if 0 <= tr < rows and 0 <= tc < cols:
                pairs.append((r * cols + c, tr * cols + tc))
    return lax.ppermute(value, ("row", "col"), pairs)


def exchange(to_prev, to_next, axis):
    count = lax.axis_size(axis)
    even = lax.axis_index(axis) % 2 == 0
    first = [(j, j ^ 1) for j in range(count) if (j ^ 1) < count]
    second = [(j, j + 1) for j in range(1, count - 1, 2)] + [(j + 1, j) for j in range(1, count - 1, 2)]
    got_first = lax.ppermute(jnp.where(even, to_next, to_prev), axis, first)
    got_second = lax.ppermute(jnp.where(even, to_prev, to_next), axis, second)
    from_prev = jnp.where(even, got_second, got_first)
    from_next = jnp.where(even, got_first, got_second)
    return from_prev, from_next


def swap_rounds(first, second, axis):
    count = lax.axis_size(axis)
    pairs_a = [(j, j ^ 1) for j in range(count) if (j ^ 1) < count]
    pairs_b = [(j, j + 1) for j in range(1, count - 1, 2)] + [(j + 1, j) for j in range(1, count - 1, 2)]
    return lax.ppermute(first, axis, pairs_a), lax.ppermute(second, axis, pairs_b)


def galerkin_kernel(par_ref, pos_ref, nslot_ref, count_ref, home_ref, a_ref, own_ref, above_ref, below_ref,
                    left_ref, right_ref, keep_ref, first_ref, second_ref,
                    acc_ref, prod_ref, dpt_ref, p_ref):
    patches = a_ref.shape[0]
    rows, cols = AG, AG
    hc = cols + 2
    for x in range(rows):
        for y in range(cols):
            p_ref[(x + 1) * hc + y + 1] = own_ref[x * cols + y]
    for y in range(cols):
        p_ref[y + 1] = above_ref[y * B:(y + 1) * B]
        p_ref[(rows + 1) * hc + y + 1] = below_ref[y * B:(y + 1) * B]
    for x in range(rows + 2):
        p_ref[x * hc] = left_ref[x * B:(x + 1) * B]
        p_ref[x * hc + hc - 1] = right_ref[x * B:(x + 1) * B]

    def one_patch(i, carry):
        acc_ref[...] = jnp.zeros(acc_ref.shape, jnp.float32)
        x = i // AG
        y = i % AG
        count = count_ref[x, y]
        for k in range(KA):
            pos = pos_ref[x, y, k]
            a_blk = a_ref[i, :, k * B:(k + 1) * B]
            term = jnp.dot(a_blk, p_ref[pos], preferred_element_type=jnp.float32)
            for q in range(KP):
                s = jnp.where(k < count, nslot_ref[pos * KP + q], TRASH)
                acc_ref[s] = acc_ref[s] + term[:, q * B:(q + 1) * B]
        row = pl.multiple_of(i * B, B)
        for w in range(0, WIN * WIN - 1, 2):
            pair = jnp.concatenate([acc_ref[w], acc_ref[w + 1]], axis=1)
            prod_ref[pl.ds(row, B), w * B:(w + 2) * B] = pair.astype(jnp.bfloat16)
        last = WIN * WIN - 1
        prod_ref[pl.ds(row, B), last * B:(last + 1) * B] = acc_ref[last].astype(jnp.bfloat16)
        return carry

    lax.fori_loop(0, patches, one_patch, 0)

    dpt_ref[...] = jnp.zeros(dpt_ref.shape, jnp.float32)
    for i in range(patches):
        flipped = own_ref[i].astype(jnp.float32).T
        for p in range(KP):
            start = pl.multiple_of(home_ref[i // AG, i % AG, p] * B, B)
            dpt_ref[pl.ds(start, B), i * B:(i + 1) * B] += flipped[p * B:(p + 1) * B, :]

    prod = prod_ref[...]
    group = HOME * B
    odd = par_ref[0]
    for out, at in ((first_ref, 2 - 2 * odd), (keep_ref, 1), (second_ref, 2 * odd)):
        start = pl.multiple_of(at * group, group)
        terms = jnp.dot(dpt_ref[pl.ds(start, group)].astype(jnp.bfloat16), prod,
                        preferred_element_type=jnp.float32)
        out[...] = terms.reshape(out.shape).astype(out.dtype)


def fold_cols_band(keep_ref, a_ref, b_ref, even, d, out, shift=0):
    src_w = WIN * B
    dst_w = OUTW * B
    for sx in range(WIN):
        lo = (sx + shift) * dst_w
        s0 = sx * src_w
        own = keep_ref[d, :, s0:s0 + src_w]
        got_a = a_ref[d, :, s0:s0 + src_w].astype(jnp.float32)
        got_b = b_ref[d, :, s0:s0 + src_w].astype(jnp.float32)
        left = jnp.where(even, got_b, got_a)
        right = jnp.where(even, got_a, got_b)
        first = left[:, :B]
        mid = left[:, B:2 * B] + own[:, :B]
        core = left[:, 2 * B:] + own[:, B:src_w - B] + right[:, :src_w - 2 * B]
        tail = own[:, src_w - B:] + right[:, src_w - 2 * B:src_w - B]
        last = right[:, src_w - B:]
        out[:, lo:lo + B] = first.astype(out.dtype)
        out[:, lo + B:lo + 2 * B] = mid.astype(out.dtype)
        out[:, lo + 2 * B:lo + 5 * B] = core.astype(out.dtype)
        out[:, lo + 5 * B:lo + 6 * B] = tail.astype(out.dtype)
        out[:, lo + 6 * B:lo + 7 * B] = last.astype(out.dtype)


def fold_cols_send_kernel(par_ref, keep_ref, a_ref, b_ref, first_out, second_out):
    even_col = par_ref[0] == 0
    odd_row = par_ref[1]
    fold_cols_band(keep_ref, a_ref, b_ref, even_col, 2 - 2 * odd_row, first_out)
    fold_cols_band(keep_ref, a_ref, b_ref, even_col, 2 * odd_row, second_out)


def fold_cols_keep_kernel(par_ref, keep_ref, a_ref, b_ref, keep_out):
    band = OUTW * B
    keep_out[:, :band] = jnp.zeros((B, band), keep_out.dtype)
    keep_out[:, (OUTW - 1) * band:] = jnp.zeros((B, band), keep_out.dtype)
    fold_cols_band(keep_ref, a_ref, b_ref, par_ref[0] == 0, 1, keep_out, shift=1)


def fold_rows_kernel(par_ref, keep_ref, a_hbm, b_hbm, out_ref, a_ref, b_ref):
    pltpu.sync_copy(a_hbm, a_ref)
    pltpu.sync_copy(b_hbm, b_ref)
    band = OUTW * B
    even = par_ref[1] == 0
    low = 2 * band
    high = WIN * band
    from_prev_lo = jnp.where(even, b_ref[:, :low], a_ref[:, :low]).astype(jnp.float32)
    out_ref[:, :low] = (keep_ref[:, :low] + from_prev_lo).astype(out_ref.dtype)
    from_prev_mid = jnp.where(even, b_ref[:, low:high], a_ref[:, low:high]).astype(jnp.float32)
    from_next_mid = jnp.where(even, a_ref[:, :high - low], b_ref[:, :high - low]).astype(jnp.float32)
    out_ref[:, low:high] = (keep_ref[:, low:high] + from_prev_mid + from_next_mid).astype(out_ref.dtype)
    from_next_hi = jnp.where(even, a_ref[:, high - low:], b_ref[:, high - low:]).astype(jnp.float32)
    out_ref[:, high:] = (keep_ref[:, high:] + from_next_hi).astype(out_ref.dtype)


def per_device(
    fine_blocks, fine_columns, fine_counts, prolong_blocks, prolong_columns, prolong_counts
):
    tile_rows, tile_cols = fine_counts.shape
    assert tile_rows == AG and tile_cols == AG
    patches = tile_rows * tile_cols
    grid_cols = tile_cols * lax.axis_size("col")
    coarse_grid_cols = lax.axis_size("col")
    row_index = lax.axis_index("row")
    col_index = lax.axis_index("col")

    prolong = prolong_blocks
    entries = jnp.arange(KP, dtype=jnp.int32)
    kept = entries[None, None, :] < prolong_counts[:, :, None]

    own_codes = prolong_columns
    hrow = jnp.clip(own_codes // coarse_grid_cols - row_index + 1, 0, HOME - 1)
    hcol = jnp.clip(own_codes % coarse_grid_cols - col_index + 1, 0, HOME - 1)
    rel = jnp.where(kept, hrow * WIN + hcol, 4 * TRASH)
    home_rc = hcol * HOME + hrow

    def payload(p_part, rel_part):
        count = p_part.shape[0]
        flat = p_part.reshape(count * B, KP * B)
        extra = jnp.pad(rel_part.reshape(1, count * KP).astype(jnp.bfloat16),
                        ((0, 15), (0, KP * B - count * KP)))
        return jnp.concatenate([flat, extra], axis=0)

    def unpack(got, count):
        p_part = got[:count * B].reshape(count, B, KP * B)
        rel_part = got[count * B, :count * KP].astype(jnp.int32).reshape(count, KP)
        return p_part, rel_part

    hr, hc = tile_rows + 2, tile_cols + 2
    above_in, below_in = exchange(
        payload(prolong[0], rel[0]), payload(prolong[tile_rows - 1], rel[tile_rows - 1]), "row")
    above, above_rel = unpack(above_in, tile_cols)
    below, below_rel = unpack(below_in, tile_cols)
    tall = jnp.concatenate([above[None], prolong, below[None]], axis=0)
    tall_rel = jnp.concatenate([above_rel[None], rel, below_rel[None]], axis=0)
    left_in, right_in = exchange(
        payload(tall[:, 0], tall_rel[:, 0]), payload(tall[:, tile_cols - 1], tall_rel[:, tile_cols - 1]), "col")
    left_rel = unpack(left_in, hr)[1]
    right_rel = unpack(right_in, hr)[1]
    near_rel = jnp.concatenate([left_rel[:, None], tall_rel, right_rel[:, None]], axis=1)

    off_r = (jnp.arange(hr, dtype=jnp.int32) + tile_rows - 1) // tile_rows - 1
    off_c = (jnp.arange(hc, dtype=jnp.int32) + tile_cols - 1) // tile_cols - 1
    base = (off_r[:, None, None] + 1) * WIN + off_c[None, :, None] + 1
    near_slot = jnp.minimum(near_rel + base, TRASH).reshape(hr * hc * KP)

    first_row = row_index * tile_rows
    first_col = col_index * tile_cols
    targets = fine_columns
    pos = (targets // grid_cols - first_row + 1) * hc + targets % grid_cols - first_col + 1
    pos = jnp.clip(pos, 0, hr * hc - 1)
    home = jnp.where(kept, home_rc, HOME * HOME)

    smem = pltpu.MemorySpace.SMEM
    vmem = pltpu.MemorySpace.VMEM
    width = WIN * WIN * B
    parity = jnp.stack([col_index % 2, row_index % 2]).astype(jnp.int32)
    keep, first, second = pl.pallas_call(
        galerkin_kernel,
        out_shape=(
            jax.ShapeDtypeStruct((HOME, B, width), jnp.float32),
            jax.ShapeDtypeStruct((HOME, B, width), SEND),
            jax.ShapeDtypeStruct((HOME, B, width), SEND),
        ),
        in_specs=[pl.BlockSpec(memory_space=smem)] * 5 + [pl.BlockSpec(memory_space=vmem)] * 6,
        out_specs=(pl.BlockSpec(memory_space=vmem),) * 3,
        scratch_shapes=[
            pltpu.VMEM((TRASH + 1, B, B), jnp.float32),
            pltpu.VMEM((patches * B, width), jnp.bfloat16),
            pltpu.VMEM(((HOME * HOME + 1) * B, patches * B), jnp.float32),
            pltpu.VMEM((hr * hc, B, KP * B), jnp.bfloat16),
        ],
    )(
        parity,
        pos.astype(jnp.int32),
        near_slot.astype(jnp.int32),
        fine_counts.astype(jnp.int32),
        home.astype(jnp.int32),
        fine_blocks.reshape(patches, B, KA * B),
        prolong.reshape(patches, B, KP * B),
        above_in,
        below_in,
        left_in,
        right_in,
    )
    got_a, got_b = swap_rounds(first, second, "col")
    band = WIN * OUTW * B
    first2, second2 = pl.pallas_call(
        fold_cols_send_kernel,
        out_shape=(
            jax.ShapeDtypeStruct((B, band), SEND),
            jax.ShapeDtypeStruct((B, band), SEND),
        ),
        in_specs=[pl.BlockSpec(memory_space=smem)] + [pl.BlockSpec(memory_space=vmem)] * 3,
        out_specs=(pl.BlockSpec(memory_space=vmem),) * 2,
    )(parity, keep, got_a, got_b)
    keep2 = pl.pallas_call(
        fold_cols_keep_kernel,
        out_shape=jax.ShapeDtypeStruct((B, OUTW * OUTW * B), jnp.float32),
        in_specs=[pl.BlockSpec(memory_space=smem)] + [pl.BlockSpec(memory_space=vmem)] * 3,
        out_specs=pl.BlockSpec(memory_space=vmem),
    )(parity, keep, got_a, got_b)
    row_a, row_b = swap_rounds(first2, second2, "row")
    out = pl.pallas_call(
        fold_rows_kernel,
        out_shape=jax.ShapeDtypeStruct((B, OUTW * OUTW * B), jnp.bfloat16),
        in_specs=[pl.BlockSpec(memory_space=smem), pl.BlockSpec(memory_space=vmem)]
        + [pl.BlockSpec(memory_space=pltpu.MemorySpace.HBM)] * 2,
        out_specs=pl.BlockSpec(memory_space=vmem),
        scratch_shapes=[pltpu.VMEM((B, band), SEND), pltpu.VMEM((B, band), SEND)],
    )(parity, keep2, row_a, row_b)
    return out.reshape(1, 1, B, OUTW * OUTW * B)


def solution(mesh):
    in_specs = (
        P("row", "col", None, None),
        P("row", "col", None),
        P("row", "col"),
        P("row", "col", None, None),
        P("row", "col", None),
        P("row", "col"),
    )
    out_specs = P("row", "col", None, None)
    return jax.shard_map(
        per_device, mesh=mesh, in_specs=in_specs, out_specs=out_specs, check_vma=False
    )
```

```python
import jax
import jax.numpy as jnp
from jax import lax
from jax.experimental import pallas as pl
from jax.experimental.pallas import tpu as pltpu
from jax.sharding import PartitionSpec as P

B = 64
KA = 9
KP = 4
AG = 4

NEAR = 3
WIN = 5
HOME = 3
OUTW = 7
TRASH = WIN * WIN
SEND = jnp.bfloat16


def shifted(value, by_row, by_col):
    rows = lax.axis_size("row")
    cols = lax.axis_size("col")
    pairs = []
    for r in range(rows):
        for c in range(cols):
            tr, tc = r + by_row, c + by_col
            if 0 <= tr < rows and 0 <= tc < cols:
                pairs.append((r * cols + c, tr * cols + tc))
    return lax.ppermute(value, ("row", "col"), pairs)


def exchange(to_prev, to_next, axis):
    count = lax.axis_size(axis)
    even = lax.axis_index(axis) % 2 == 0
    first = [(j, j ^ 1) for j in range(count) if (j ^ 1) < count]
    second = [(j, j + 1) for j in range(1, count - 1, 2)] + [(j + 1, j) for j in range(1, count - 1, 2)]
    got_first = lax.ppermute(jnp.where(even, to_next, to_prev), axis, first)
    got_second = lax.ppermute(jnp.where(even, to_prev, to_next), axis, second)
    from_prev = jnp.where(even, got_second, got_first)
    from_next = jnp.where(even, got_first, got_second)
    return from_prev, from_next


def swap_rounds(first, second, axis):
    count = lax.axis_size(axis)
    pairs_a = [(j, j ^ 1) for j in range(count) if (j ^ 1) < count]
    pairs_b = [(j, j + 1) for j in range(1, count - 1, 2)] + [(j + 1, j) for j in range(1, count - 1, 2)]
    return lax.ppermute(first, axis, pairs_a), lax.ppermute(second, axis, pairs_b)


def galerkin_kernel(par_ref, pos_ref, nslot_ref, count_ref, home_ref, a_ref, own_ref, above_ref, below_ref,
                    left_ref, right_ref, keep_ref, first_ref, second_ref,
                    acc_ref, prod_ref, dpt_ref, p_ref):
    patches = a_ref.shape[0]
    rows, cols = AG, AG
    hc = cols + 2
    for x in range(rows):
        for y in range(cols):
            p_ref[(x + 1) * hc + y + 1] = own_ref[x * cols + y]
    for y in range(cols):
        p_ref[y + 1] = above_ref[y * B:(y + 1) * B]
        p_ref[(rows + 1) * hc + y + 1] = below_ref[y * B:(y + 1) * B]
    for x in range(rows + 2):
        p_ref[x * hc] = left_ref[x * B:(x + 1) * B]
        p_ref[x * hc + hc - 1] = right_ref[x * B:(x + 1) * B]

    def one_patch(i, carry):
        acc_ref[...] = jnp.zeros(acc_ref.shape, jnp.float32)
        x = i // AG
        y = i % AG
        count = count_ref[x, y]
        for k in range(KA):
            pos = pos_ref[x, y, k]
            a_blk = a_ref[i, :, k * B:(k + 1) * B]
            term = jnp.dot(a_blk, p_ref[pos], preferred_element_type=jnp.float32)
            for q in range(KP):
                s = jnp.where(k < count, nslot_ref[pos * KP + q], TRASH)
                acc_ref[s] = acc_ref[s] + term[:, q * B:(q + 1) * B]
        row = pl.multiple_of(i * B, B)
        for w in range(0, WIN * WIN - 1, 2):
            pair = jnp.concatenate([acc_ref[w], acc_ref[w + 1]], axis=1)
            prod_ref[pl.ds(row, B), w * B:(w + 2) * B] = pair.astype(jnp.bfloat16)
        last = WIN * WIN - 1
        prod_ref[pl.ds(row, B), last * B:(last + 1) * B] = acc_ref[last].astype(jnp.bfloat16)
        return carry

    lax.fori_loop(0, patches, one_patch, 0)

    dpt_ref[...] = jnp.zeros(dpt_ref.shape, jnp.float32)
    for i in range(patches):
        flipped = own_ref[i].astype(jnp.float32).T
        for p in range(KP):
            start = pl.multiple_of(home_ref[i // AG, i % AG, p] * B, B)
            dpt_ref[pl.ds(start, B), i * B:(i + 1) * B] += flipped[p * B:(p + 1) * B, :]

    prod = prod_ref[...]
    group = HOME * B
    odd = par_ref[0]
    for out, at in ((first_ref, 2 - 2 * odd), (keep_ref, 1), (second_ref, 2 * odd)):
        start = pl.multiple_of(at * group, group)
        terms = jnp.dot(dpt_ref[pl.ds(start, group)].astype(jnp.bfloat16), prod,
                        preferred_element_type=jnp.float32)
        out[...] = terms.reshape(out.shape).astype(out.dtype)


def fold_cols_band(keep_ref, a_ref, b_ref, even, d, out, shift=0):
    src_w = WIN * B
    dst_w = OUTW * B
    for sx in range(WIN):
        lo = (sx + shift) * dst_w
        s0 = sx * src_w
        own = keep_ref[d, :, s0:s0 + src_w]
        got_a = a_ref[d, :, s0:s0 + src_w].astype(jnp.float32)
        got_b = b_ref[d, :, s0:s0 + src_w].astype(jnp.float32)
        left = jnp.where(even, got_b, got_a)
        right = jnp.where(even, got_a, got_b)
        first = left[:, :B]
        mid = left[:, B:2 * B] + own[:, :B]
        core = left[:, 2 * B:] + own[:, B:src_w - B] + right[:, :src_w - 2 * B]
        tail = own[:, src_w - B:] + right[:, src_w - 2 * B:src_w - B]
        last = right[:, src_w - B:]
        out[:, lo:lo + B] = first.astype(out.dtype)
        out[:, lo + B:lo + 2 * B] = mid.astype(out.dtype)
        out[:, lo + 2 * B:lo + 5 * B] = core.astype(out.dtype)
        out[:, lo + 5 * B:lo + 6 * B] = tail.astype(out.dtype)
        out[:, lo + 6 * B:lo + 7 * B] = last.astype(out.dtype)


def fold_cols_send_kernel(par_ref, keep_ref, a_ref, b_ref, first_out, second_out):
    even_col = par_ref[0] == 0
    odd_row = par_ref[1]
    fold_cols_band(keep_ref, a_ref, b_ref, even_col, 2 - 2 * odd_row, first_out)
    fold_cols_band(keep_ref, a_ref, b_ref, even_col, 2 * odd_row, second_out)


def fold_cols_keep_kernel(par_ref, keep_ref, a_ref, b_ref, keep_out):
    band = OUTW * B
    keep_out[:, :band] = jnp.zeros((B, band), keep_out.dtype)
    keep_out[:, (OUTW - 1) * band:] = jnp.zeros((B, band), keep_out.dtype)
    fold_cols_band(keep_ref, a_ref, b_ref, par_ref[0] == 0, 1, keep_out, shift=1)


def fold_rows_kernel(par_ref, keep_ref, a_ref, b_ref, out_ref):
    band = OUTW * B
    even = par_ref[1] == 0
    low = 2 * band
    high = WIN * band
    from_prev_lo = jnp.where(even, b_ref[:, :low], a_ref[:, :low]).astype(jnp.float32)
    out_ref[:, :low] = (keep_ref[:, :low] + from_prev_lo).astype(out_ref.dtype)
    from_prev_mid = jnp.where(even, b_ref[:, low:high], a_ref[:, low:high]).astype(jnp.float32)
    from_next_mid = jnp.where(even, a_ref[:, :high - low], b_ref[:, :high - low]).astype(jnp.float32)
    out_ref[:, low:high] = (keep_ref[:, low:high] + from_prev_mid + from_next_mid).astype(out_ref.dtype)
    from_next_hi = jnp.where(even, a_ref[:, high - low:], b_ref[:, high - low:]).astype(jnp.float32)
    out_ref[:, high:] = (keep_ref[:, high:] + from_next_hi).astype(out_ref.dtype)


def per_device(
    fine_blocks, fine_columns, fine_counts, prolong_blocks, prolong_columns, prolong_counts
):
    tile_rows, tile_cols = fine_counts.shape
    assert tile_rows == AG and tile_cols == AG
    patches = tile_rows * tile_cols
    grid_cols = tile_cols * lax.axis_size("col")
    coarse_grid_cols = lax.axis_size("col")
    row_index = lax.axis_index("row")
    col_index = lax.axis_index("col")

    prolong = prolong_blocks
    entries = jnp.arange(KP, dtype=jnp.int32)
    kept = entries[None, None, :] < prolong_counts[:, :, None]

    own_codes = prolong_columns
    own_agg = own_codes[..., :1]
    hrow = jnp.clip(own_codes // coarse_grid_cols - own_agg // coarse_grid_cols + 1, 0, HOME - 1)
    hcol = jnp.clip(own_codes % coarse_grid_cols - own_agg % coarse_grid_cols + 1, 0, HOME - 1)
    rel = jnp.where(kept, hrow * WIN + hcol, 4 * TRASH)
    home_rc = hcol * HOME + hrow

    def payload(p_part, rel_part):
        count = p_part.shape[0]
        flat = p_part.reshape(count * B, KP * B)
        extra = jnp.pad(rel_part.reshape(1, count * KP).astype(jnp.bfloat16),
                        ((0, 15), (0, KP * B - count * KP)))
        return jnp.concatenate([flat, extra], axis=0)

    def unpack(got, count):
        p_part = got[:count * B].reshape(count, B, KP * B)
        rel_part = got[count * B, :count * KP].astype(jnp.int32).reshape(count, KP)
        return p_part, rel_part

    hr, hc = tile_rows + 2, tile_cols + 2
    above_in, below_in = exchange(
        payload(prolong[0], rel[0]), payload(prolong[tile_rows - 1], rel[tile_rows - 1]), "row")
    above, above_rel = unpack(above_in, tile_cols)
    below, below_rel = unpack(below_in, tile_cols)
    tall = jnp.concatenate([above[None], prolong, below[None]], axis=0)
    tall_rel = jnp.concatenate([above_rel[None], rel, below_rel[None]], axis=0)
    left_in, right_in = exchange(
        payload(tall[:, 0], tall_rel[:, 0]), payload(tall[:, tile_cols - 1], tall_rel[:, tile_cols - 1]), "col")
    left_rel = unpack(left_in, hr)[1]
    right_rel = unpack(right_in, hr)[1]
    near_rel = jnp.concatenate([left_rel[:, None], tall_rel, right_rel[:, None]], axis=1)

    off_r = (jnp.arange(hr, dtype=jnp.int32) + tile_rows - 1) // tile_rows - 1
    off_c = (jnp.arange(hc, dtype=jnp.int32) + tile_cols - 1) // tile_cols - 1
    base = (off_r[:, None, None] + 1) * WIN + off_c[None, :, None] + 1
    near_slot = jnp.minimum(near_rel + base, TRASH).reshape(hr * hc * KP)

    first_row = row_index * tile_rows
    first_col = col_index * tile_cols
    targets = fine_columns
    pos = (targets // grid_cols - first_row + 1) * hc + targets % grid_cols - first_col + 1
    pos = jnp.clip(pos, 0, hr * hc - 1)
    home = jnp.where(kept, home_rc, HOME * HOME)

    smem = pltpu.MemorySpace.SMEM
    vmem = pltpu.MemorySpace.VMEM
    width = WIN * WIN * B
    parity = jnp.stack([col_index % 2, row_index % 2]).astype(jnp.int32)
    keep, first, second = pl.pallas_call(
        galerkin_kernel,
        out_shape=(
            jax.ShapeDtypeStruct((HOME, B, width), jnp.float32),
            jax.ShapeDtypeStruct((HOME, B, width), SEND),
            jax.ShapeDtypeStruct((HOME, B, width), SEND),
        ),
        in_specs=[pl.BlockSpec(memory_space=smem)] * 5 + [pl.BlockSpec(memory_space=vmem)] * 6,
        out_specs=(pl.BlockSpec(memory_space=vmem),) * 3,
        scratch_shapes=[
            pltpu.VMEM((TRASH + 1, B, B), jnp.float32),
            pltpu.VMEM((patches * B, width), jnp.bfloat16),
            pltpu.VMEM(((HOME * HOME + 1) * B, patches * B), jnp.float32),
            pltpu.VMEM((hr * hc, B, KP * B), jnp.bfloat16),
        ],
    )(
        parity,
        pos.astype(jnp.int32),
        near_slot.astype(jnp.int32),
        fine_counts.astype(jnp.int32),
        home.astype(jnp.int32),
        fine_blocks.reshape(patches, B, KA * B),
        prolong.reshape(patches, B, KP * B),
        above_in,
        below_in,
        left_in,
        right_in,
    )
    got_a, got_b = swap_rounds(first, second, "col")
    band = WIN * OUTW * B
    first2, second2 = pl.pallas_call(
        fold_cols_send_kernel,
        out_shape=(
            jax.ShapeDtypeStruct((B, band), SEND),
            jax.ShapeDtypeStruct((B, band), SEND),
        ),
        in_specs=[pl.BlockSpec(memory_space=smem)] + [pl.BlockSpec(memory_space=vmem)] * 3,
        out_specs=(pl.BlockSpec(memory_space=vmem),) * 2,
    )(parity, keep, got_a, got_b)
    keep2 = pl.pallas_call(
        fold_cols_keep_kernel,
        out_shape=jax.ShapeDtypeStruct((B, OUTW * OUTW * B), jnp.float32),
        in_specs=[pl.BlockSpec(memory_space=smem)] + [pl.BlockSpec(memory_space=vmem)] * 3,
        out_specs=pl.BlockSpec(memory_space=vmem),
    )(parity, keep, got_a, got_b)
    row_a, row_b = swap_rounds(first2, second2, "row")
    out = pl.pallas_call(
        fold_rows_kernel,
        out_shape=jax.ShapeDtypeStruct((B, OUTW * OUTW * B), jnp.bfloat16),
        in_specs=[pl.BlockSpec(memory_space=smem)] + [pl.BlockSpec(memory_space=vmem)] * 3,
        out_specs=pl.BlockSpec(memory_space=vmem),
    )(parity, keep2, row_a, row_b)
    return out.reshape(1, 1, B, OUTW * OUTW * B)


def solution(mesh):
    in_specs = (
        P("row", "col", None, None),
        P("row", "col", None),
        P("row", "col"),
        P("row", "col", None, None),
        P("row", "col", None),
        P("row", "col"),
    )
    out_specs = P("row", "col", None, None)
    return jax.shard_map(
        per_device, mesh=mesh, in_specs=in_specs, out_specs=out_specs, check_vma=False
    )
```

```python
import jax
import jax.numpy as jnp
from jax import lax
from jax.experimental import pallas as pl
from jax.experimental.pallas import tpu as pltpu
from jax.sharding import PartitionSpec as P

B = 64
KA = 9
KP = 4
AG = 4

NEAR = 3
WIN = 5
HOME = 3
OUTW = 7
TRASH = WIN * WIN
SEND = jnp.bfloat16


def shifted(value, by_row, by_col):
    rows = lax.axis_size("row")
    cols = lax.axis_size("col")
    pairs = []
    for r in range(rows):
        for c in range(cols):
            tr, tc = r + by_row, c + by_col
            if 0 <= tr < rows and 0 <= tc < cols:
                pairs.append((r * cols + c, tr * cols + tc))
    return lax.ppermute(value, ("row", "col"), pairs)


def exchange(to_prev, to_next, axis):
    count = lax.axis_size(axis)
    even = lax.axis_index(axis) % 2 == 0
    first = [(j, j ^ 1) for j in range(count) if (j ^ 1) < count]
    second = [(j, j + 1) for j in range(1, count - 1, 2)] + [(j + 1, j) for j in range(1, count - 1, 2)]
    got_first = lax.ppermute(jnp.where(even, to_next, to_prev), axis, first)
    got_second = lax.ppermute(jnp.where(even, to_prev, to_next), axis, second)
    from_prev = jnp.where(even, got_second, got_first)
    from_next = jnp.where(even, got_first, got_second)
    return from_prev, from_next


def swap_rounds(first, second, axis):
    count = lax.axis_size(axis)
    pairs_a = [(j, j ^ 1) for j in range(count) if (j ^ 1) < count]
    pairs_b = [(j, j + 1) for j in range(1, count - 1, 2)] + [(j + 1, j) for j in range(1, count - 1, 2)]
    return lax.ppermute(first, axis, pairs_a), lax.ppermute(second, axis, pairs_b)


def galerkin_kernel(par_ref, pos_ref, nslot_ref, count_ref, home_ref, a_ref, own_ref, above_ref, below_ref,
                    left_ref, right_ref, keep_ref, first_ref, second_ref,
                    acc_ref, prod_ref, dpt_ref, p_ref):
    patches = a_ref.shape[0]
    rows, cols = AG, AG
    hc = cols + 2
    for x in range(rows):
        for y in range(cols):
            p_ref[(x + 1) * hc + y + 1] = own_ref[x * cols + y]
    for y in range(cols):
        p_ref[y + 1] = above_ref[y * B:(y + 1) * B]
        p_ref[(rows + 1) * hc + y + 1] = below_ref[y * B:(y + 1) * B]
    for x in range(rows + 2):
        p_ref[x * hc] = left_ref[x * B:(x + 1) * B]
        p_ref[x * hc + hc - 1] = right_ref[x * B:(x + 1) * B]

    def one_patch(i, carry):
        acc_ref[...] = jnp.zeros(acc_ref.shape, jnp.float32)
        x = i // AG
        y = i % AG
        count = count_ref[x, y]
        for k in range(KA):
            pos = pos_ref[x, y, k]
            a_blk = a_ref[i, :, k * B:(k + 1) * B]
            term = jnp.dot(a_blk, p_ref[pos], preferred_element_type=jnp.float32)
            for q in range(KP):
                s = jnp.where(k < count, nslot_ref[pos * KP + q], TRASH)
                acc_ref[s] = acc_ref[s] + term[:, q * B:(q + 1) * B]
        row = pl.multiple_of(i * B, B)
        for w in range(0, WIN * WIN - 1, 2):
            pair = jnp.concatenate([acc_ref[w], acc_ref[w + 1]], axis=1)
            prod_ref[pl.ds(row, B), w * B:(w + 2) * B] = pair.astype(jnp.bfloat16)
        last = WIN * WIN - 1
        prod_ref[pl.ds(row, B), last * B:(last + 1) * B] = acc_ref[last].astype(jnp.bfloat16)
        return carry

    lax.fori_loop(0, patches, one_patch, 0)

    dpt_ref[...] = jnp.zeros(dpt_ref.shape, jnp.float32)
    for i in range(patches):
        flipped = own_ref[i].T
        for p in range(KP):
            start = pl.multiple_of(home_ref[i // AG, i % AG, p] * B, B)
            dpt_ref[pl.ds(start, B), i * B:(i + 1) * B] += flipped[p * B:(p + 1) * B, :].astype(jnp.float32)

    prod = prod_ref[...]
    group = HOME * B
    odd = par_ref[0]
    for out, at in ((first_ref, 2 - 2 * odd), (keep_ref, 1), (second_ref, 2 * odd)):
        start = pl.multiple_of(at * group, group)
        terms = jnp.dot(dpt_ref[pl.ds(start, group)].astype(jnp.bfloat16), prod,
                        preferred_element_type=jnp.float32)
        out[...] = terms.reshape(out.shape).astype(out.dtype)


def fold_cols_band(keep_ref, a_ref, b_ref, even, d, out, shift=0):
    src_w = WIN * B
    dst_w = OUTW * B
    for sx in range(WIN):
        lo = (sx + shift) * dst_w
        s0 = sx * src_w
        own = keep_ref[d, :, s0:s0 + src_w]
        got_a = a_ref[d, :, s0:s0 + src_w].astype(jnp.float32)
        got_b = b_ref[d, :, s0:s0 + src_w].astype(jnp.float32)
        left = jnp.where(even, got_b, got_a)
        right = jnp.where(even, got_a, got_b)
        first = left[:, :B]
        mid = left[:, B:2 * B] + own[:, :B]
        core = left[:, 2 * B:] + own[:, B:src_w - B] + right[:, :src_w - 2 * B]
        tail = own[:, src_w - B:] + right[:, src_w - 2 * B:src_w - B]
        last = right[:, src_w - B:]
        out[:, lo:lo + B] = first.astype(out.dtype)
        out[:, lo + B:lo + 2 * B] = mid.astype(out.dtype)
        out[:, lo + 2 * B:lo + 5 * B] = core.astype(out.dtype)
        out[:, lo + 5 * B:lo + 6 * B] = tail.astype(out.dtype)
        out[:, lo + 6 * B:lo + 7 * B] = last.astype(out.dtype)


def fold_cols_send_kernel(par_ref, keep_ref, a_ref, b_ref, first_out, second_out):
    even_col = par_ref[0] == 0
    odd_row = par_ref[1]
    fold_cols_band(keep_ref, a_ref, b_ref, even_col, 2 - 2 * odd_row, first_out)
    fold_cols_band(keep_ref, a_ref, b_ref, even_col, 2 * odd_row, second_out)


def fold_cols_keep_kernel(par_ref, keep_ref, a_ref, b_ref, keep_out):
    band = OUTW * B
    keep_out[:, :band] = jnp.zeros((B, band), keep_out.dtype)
    keep_out[:, (OUTW - 1) * band:] = jnp.zeros((B, band), keep_out.dtype)
    fold_cols_band(keep_ref, a_ref, b_ref, par_ref[0] == 0, 1, keep_out, shift=1)


def fold_rows_kernel(par_ref, keep_ref, a_ref, b_ref, out_ref):
    band = OUTW * B
    even = par_ref[1] == 0
    low = 2 * band
    high = WIN * band
    from_prev_lo = jnp.where(even, b_ref[:, :low], a_ref[:, :low]).astype(jnp.float32)
    out_ref[:, :low] = (keep_ref[:, :low] + from_prev_lo).astype(out_ref.dtype)
    from_prev_mid = jnp.where(even, b_ref[:, low:high], a_ref[:, low:high]).astype(jnp.float32)
    from_next_mid = jnp.where(even, a_ref[:, :high - low], b_ref[:, :high - low]).astype(jnp.float32)
    out_ref[:, low:high] = (keep_ref[:, low:high] + from_prev_mid + from_next_mid).astype(out_ref.dtype)
    from_next_hi = jnp.where(even, a_ref[:, high - low:], b_ref[:, high - low:]).astype(jnp.float32)
    out_ref[:, high:] = (keep_ref[:, high:] + from_next_hi).astype(out_ref.dtype)


def per_device(
    fine_blocks, fine_columns, fine_counts, prolong_blocks, prolong_columns, prolong_counts
):
    tile_rows, tile_cols = fine_counts.shape
    assert tile_rows == AG and tile_cols == AG
    patches = tile_rows * tile_cols
    grid_cols = tile_cols * lax.axis_size("col")
    coarse_grid_cols = lax.axis_size("col")
    row_index = lax.axis_index("row")
    col_index = lax.axis_index("col")

    prolong = prolong_blocks
    entries = jnp.arange(KP, dtype=jnp.int32)
    kept = entries[None, None, :] < prolong_counts[:, :, None]

    own_codes = prolong_columns
    hrow = jnp.clip(own_codes // coarse_grid_cols - row_index + 1, 0, HOME - 1)
    hcol = jnp.clip(own_codes % coarse_grid_cols - col_index + 1, 0, HOME - 1)
    rel = jnp.where(kept, hrow * WIN + hcol, 4 * TRASH)
    home_rc = hcol * HOME + hrow

    def payload(p_part, rel_part):
        count = p_part.shape[0]
        flat = p_part.reshape(count * B, KP * B)
        extra = jnp.pad(rel_part.reshape(1, count * KP).astype(jnp.bfloat16),
                        ((0, 15), (0, KP * B - count * KP)))
        return jnp.concatenate([flat, extra], axis=0)

    def unpack(got, count):
        p_part = got[:count * B].reshape(count, B, KP * B)
        rel_part = got[count * B, :count * KP].astype(jnp.int32).reshape(count, KP)
        return p_part, rel_part

    hr, hc = tile_rows + 2, tile_cols + 2
    above_in, below_in = exchange(
        payload(prolong[0], rel[0]), payload(prolong[tile_rows - 1], rel[tile_rows - 1]), "row")
    above, above_rel = unpack(above_in, tile_cols)
    below, below_rel = unpack(below_in, tile_cols)
    tall = jnp.concatenate([above[None], prolong, below[None]], axis=0)
    tall_rel = jnp.concatenate([above_rel[None], rel, below_rel[None]], axis=0)
    left_in, right_in = exchange(
        payload(tall[:, 0], tall_rel[:, 0]), payload(tall[:, tile_cols - 1], tall_rel[:, tile_cols - 1]), "col")
    left_rel = unpack(left_in, hr)[1]
    right_rel = unpack(right_in, hr)[1]
    near_rel = jnp.concatenate([left_rel[:, None], tall_rel, right_rel[:, None]], axis=1)

    off_r = (jnp.arange(hr, dtype=jnp.int32) + tile_rows - 1) // tile_rows - 1
    off_c = (jnp.arange(hc, dtype=jnp.int32) + tile_cols - 1) // tile_cols - 1
    base = (off_r[:, None, None] + 1) * WIN + off_c[None, :, None] + 1
    near_slot = jnp.minimum(near_rel + base, TRASH).reshape(hr * hc * KP)

    first_row = row_index * tile_rows
    first_col = col_index * tile_cols
    targets = fine_columns
    pos = (targets // grid_cols - first_row + 1) * hc + targets % grid_cols - first_col + 1
    pos = jnp.clip(pos, 0, hr * hc - 1)
    home = jnp.where(kept, home_rc, HOME * HOME)

    smem = pltpu.MemorySpace.SMEM
    vmem = pltpu.MemorySpace.VMEM
    width = WIN * WIN * B
    parity = jnp.stack([col_index % 2, row_index % 2]).astype(jnp.int32)
    keep, first, second = pl.pallas_call(
        galerkin_kernel,
        out_shape=(
            jax.ShapeDtypeStruct((HOME, B, width), jnp.float32),
            jax.ShapeDtypeStruct((HOME, B, width), SEND),
            jax.ShapeDtypeStruct((HOME, B, width), SEND),
        ),
        in_specs=[pl.BlockSpec(memory_space=smem)] * 5 + [pl.BlockSpec(memory_space=vmem)] * 6,
        out_specs=(pl.BlockSpec(memory_space=vmem),) * 3,
        scratch_shapes=[
            pltpu.VMEM((TRASH + 1, B, B), jnp.float32),
            pltpu.VMEM((patches * B, width), jnp.bfloat16),
            pltpu.VMEM(((HOME * HOME + 1) * B, patches * B), jnp.float32),
            pltpu.VMEM((hr * hc, B, KP * B), jnp.bfloat16),
        ],
    )(
        parity,
        pos.astype(jnp.int32),
        near_slot.astype(jnp.int32),
        fine_counts.astype(jnp.int32),
        home.astype(jnp.int32),
        fine_blocks.reshape(patches, B, KA * B),
        prolong.reshape(patches, B, KP * B),
        above_in,
        below_in,
        left_in,
        right_in,
    )
    got_a, got_b = swap_rounds(first, second, "col")
    band = WIN * OUTW * B
    first2, second2 = pl.pallas_call(
        fold_cols_send_kernel,
        out_shape=(
            jax.ShapeDtypeStruct((B, band), SEND),
            jax.ShapeDtypeStruct((B, band), SEND),
        ),
        in_specs=[pl.BlockSpec(memory_space=smem)] + [pl.BlockSpec(memory_space=vmem)] * 3,
        out_specs=(pl.BlockSpec(memory_space=vmem),) * 2,
    )(parity, keep, got_a, got_b)
    keep2 = pl.pallas_call(
        fold_cols_keep_kernel,
        out_shape=jax.ShapeDtypeStruct((B, OUTW * OUTW * B), jnp.float32),
        in_specs=[pl.BlockSpec(memory_space=smem)] + [pl.BlockSpec(memory_space=vmem)] * 3,
        out_specs=pl.BlockSpec(memory_space=vmem),
    )(parity, keep, got_a, got_b)
    row_a, row_b = swap_rounds(first2, second2, "row")
    out = pl.pallas_call(
        fold_rows_kernel,
        out_shape=jax.ShapeDtypeStruct((B, OUTW * OUTW * B), jnp.bfloat16),
        in_specs=[pl.BlockSpec(memory_space=smem)] + [pl.BlockSpec(memory_space=vmem)] * 3,
        out_specs=pl.BlockSpec(memory_space=vmem),
    )(parity, keep2, row_a, row_b)
    return out.reshape(1, 1, B, OUTW * OUTW * B)


def solution(mesh):
    in_specs = (
        P("row", "col", None, None),
        P("row", "col", None),
        P("row", "col"),
        P("row", "col", None, None),
        P("row", "col", None),
        P("row", "col"),
    )
    out_specs = P("row", "col", None, None)
    return jax.shard_map(
        per_device, mesh=mesh, in_specs=in_specs, out_specs=out_specs, check_vma=False
    )
```

```python
import jax
import jax.numpy as jnp
from jax import lax
from jax.experimental import pallas as pl
from jax.experimental.pallas import tpu as pltpu
from jax.sharding import PartitionSpec as P

B = 64
KA = 9
KP = 4
AG = 4

NEAR = 3
WIN = 5
HOME = 3
OUTW = 7
TRASH = WIN * WIN
SEND = jnp.bfloat16


def shifted(value, by_row, by_col):
    rows = lax.axis_size("row")
    cols = lax.axis_size("col")
    pairs = []
    for r in range(rows):
        for c in range(cols):
            tr, tc = r + by_row, c + by_col
            if 0 <= tr < rows and 0 <= tc < cols:
                pairs.append((r * cols + c, tr * cols + tc))
    return lax.ppermute(value, ("row", "col"), pairs)


def exchange(to_prev, to_next, axis):
    count = lax.axis_size(axis)
    even = lax.axis_index(axis) % 2 == 0
    first = [(j, j ^ 1) for j in range(count) if (j ^ 1) < count]
    second = [(j, j + 1) for j in range(1, count - 1, 2)] + [(j + 1, j) for j in range(1, count - 1, 2)]
    got_first = lax.ppermute(jnp.where(even, to_next, to_prev), axis, first)
    got_second = lax.ppermute(jnp.where(even, to_prev, to_next), axis, second)
    from_prev = jnp.where(even, got_second, got_first)
    from_next = jnp.where(even, got_first, got_second)
    return from_prev, from_next


def swap_rounds(first, second, axis):
    count = lax.axis_size(axis)
    pairs_a = [(j, j ^ 1) for j in range(count) if (j ^ 1) < count]
    pairs_b = [(j, j + 1) for j in range(1, count - 1, 2)] + [(j + 1, j) for j in range(1, count - 1, 2)]
    return lax.ppermute(first, axis, pairs_a), lax.ppermute(second, axis, pairs_b)


def galerkin_kernel(par_ref, pos_ref, nslot_ref, count_ref, home_ref, a_ref, own_ref, above_ref, below_ref,
                    left_ref, right_ref, keep_ref, first_ref, second_ref,
                    acc_ref, prod_ref, dpt_ref, p_ref):
    patches = a_ref.shape[0]
    rows, cols = AG, AG
    hc = cols + 2
    for x in range(rows):
        for y in range(cols):
            p_ref[(x + 1) * hc + y + 1] = own_ref[x * cols + y]
    for y in range(cols):
        p_ref[y + 1] = above_ref[y * B:(y + 1) * B]
        p_ref[(rows + 1) * hc + y + 1] = below_ref[y * B:(y + 1) * B]
    for x in range(rows + 2):
        p_ref[x * hc] = left_ref[x * B:(x + 1) * B]
        p_ref[x * hc + hc - 1] = right_ref[x * B:(x + 1) * B]

    def one_patch(i, carry):
        acc_ref[:TRASH] = jnp.zeros((TRASH, B, B), jnp.float32)
        x = i // AG
        y = i % AG
        count = count_ref[x, y]
        for k in range(KA):
            pos = pos_ref[x, y, k]
            a_blk = a_ref[i, :, k * B:(k + 1) * B]
            term = jnp.dot(a_blk, p_ref[pos], preferred_element_type=jnp.float32)
            for q in range(KP):
                s = jnp.where(k < count, nslot_ref[pos * KP + q], TRASH)
                acc_ref[s] = acc_ref[s] + term[:, q * B:(q + 1) * B]
        row = pl.multiple_of(i * B, B)
        for w in range(0, WIN * WIN - 1, 2):
            pair = jnp.concatenate([acc_ref[w], acc_ref[w + 1]], axis=1)
            prod_ref[pl.ds(row, B), w * B:(w + 2) * B] = pair.astype(jnp.bfloat16)
        last = WIN * WIN - 1
        prod_ref[pl.ds(row, B), last * B:(last + 1) * B] = acc_ref[last].astype(jnp.bfloat16)
        return carry

    lax.fori_loop(0, patches, one_patch, 0)

    dpt_ref[:HOME * HOME * B] = jnp.zeros((HOME * HOME * B, dpt_ref.shape[1]), jnp.float32)
    for i in range(patches):
        flipped = own_ref[i].T
        for p in range(KP):
            start = pl.multiple_of(home_ref[i // AG, i % AG, p] * B, B)
            dpt_ref[pl.ds(start, B), i * B:(i + 1) * B] += flipped[p * B:(p + 1) * B, :].astype(jnp.float32)

    prod = prod_ref[...]
    group = HOME * B
    odd = par_ref[0]
    for out, at in ((first_ref, 2 - 2 * odd), (keep_ref, 1), (second_ref, 2 * odd)):
        start = pl.multiple_of(at * group, group)
        terms = jnp.dot(dpt_ref[pl.ds(start, group)].astype(jnp.bfloat16), prod,
                        preferred_element_type=jnp.float32)
        out[...] = terms.reshape(out.shape).astype(out.dtype)


def fold_cols_band(keep_ref, a_ref, b_ref, even, d, out, shift=0):
    src_w = WIN * B
    dst_w = OUTW * B
    for sx in range(WIN):
        lo = (sx + shift) * dst_w
        s0 = sx * src_w
        own = keep_ref[d, :, s0:s0 + src_w]
        got_a = a_ref[d, :, s0:s0 + src_w].astype(jnp.float32)
        got_b = b_ref[d, :, s0:s0 + src_w].astype(jnp.float32)
        left = jnp.where(even, got_b, got_a)
        right = jnp.where(even, got_a, got_b)
        first = left[:, :B]
        mid = left[:, B:2 * B] + own[:, :B]
        core = left[:, 2 * B:] + own[:, B:src_w - B] + right[:, :src_w - 2 * B]
        tail = own[:, src_w - B:] + right[:, src_w - 2 * B:src_w - B]
        last = right[:, src_w - B:]
        out[:, lo:lo + B] = first.astype(out.dtype)
        out[:, lo + B:lo + 2 * B] = mid.astype(out.dtype)
        out[:, lo + 2 * B:lo + 5 * B] = core.astype(out.dtype)
        out[:, lo + 5 * B:lo + 6 * B] = tail.astype(out.dtype)
        out[:, lo + 6 * B:lo + 7 * B] = last.astype(out.dtype)


def fold_cols_send_kernel(par_ref, keep_ref, a_ref, b_ref, first_out, second_out):
    even_col = par_ref[0] == 0
    odd_row = par_ref[1]
    fold_cols_band(keep_ref, a_ref, b_ref, even_col, 2 - 2 * odd_row, first_out)
    fold_cols_band(keep_ref, a_ref, b_ref, even_col, 2 * odd_row, second_out)


def fold_cols_keep_kernel(par_ref, keep_ref, a_ref, b_ref, keep_out):
    band = OUTW * B
    keep_out[:, :band] = jnp.zeros((B, band), keep_out.dtype)
    keep_out[:, (OUTW - 1) * band:] = jnp.zeros((B, band), keep_out.dtype)
    fold_cols_band(keep_ref, a_ref, b_ref, par_ref[0] == 0, 1, keep_out, shift=1)


def fold_rows_kernel(par_ref, keep_ref, a_ref, b_ref, out_ref):
    band = OUTW * B
    even = par_ref[1] == 0
    low = 2 * band
    high = WIN * band
    from_prev_lo = jnp.where(even, b_ref[:, :low], a_ref[:, :low]).astype(jnp.float32)
    out_ref[:, :low] = (keep_ref[:, :low] + from_prev_lo).astype(out_ref.dtype)
    from_prev_mid = jnp.where(even, b_ref[:, low:high], a_ref[:, low:high]).astype(jnp.float32)
    from_next_mid = jnp.where(even, a_ref[:, :high - low], b_ref[:, :high - low]).astype(jnp.float32)
    out_ref[:, low:high] = (keep_ref[:, low:high] + from_prev_mid + from_next_mid).astype(out_ref.dtype)
    from_next_hi = jnp.where(even, a_ref[:, high - low:], b_ref[:, high - low:]).astype(jnp.float32)
    out_ref[:, high:] = (keep_ref[:, high:] + from_next_hi).astype(out_ref.dtype)


def per_device(
    fine_blocks, fine_columns, fine_counts, prolong_blocks, prolong_columns, prolong_counts
):
    tile_rows, tile_cols = fine_counts.shape
    assert tile_rows == AG and tile_cols == AG
    patches = tile_rows * tile_cols
    grid_cols = tile_cols * lax.axis_size("col")
    coarse_grid_cols = lax.axis_size("col")
    row_index = lax.axis_index("row")
    col_index = lax.axis_index("col")

    prolong = prolong_blocks
    entries = jnp.arange(KP, dtype=jnp.int32)
    kept = entries[None, None, :] < prolong_counts[:, :, None]

    own_codes = prolong_columns
    hrow = jnp.clip(own_codes // coarse_grid_cols - row_index + 1, 0, HOME - 1)
    hcol = jnp.clip(own_codes % coarse_grid_cols - col_index + 1, 0, HOME - 1)
    rel = jnp.where(kept, hrow * WIN + hcol, 4 * TRASH)
    home_rc = hcol * HOME + hrow

    def payload(p_part, rel_part):
        count = p_part.shape[0]
        flat = p_part.reshape(count * B, KP * B)
        extra = jnp.pad(rel_part.reshape(1, count * KP).astype(jnp.bfloat16),
                        ((0, 15), (0, KP * B - count * KP)))
        return jnp.concatenate([flat, extra], axis=0)

    def unpack(got, count):
        p_part = got[:count * B].reshape(count, B, KP * B)
        rel_part = got[count * B, :count * KP].astype(jnp.int32).reshape(count, KP)
        return p_part, rel_part

    hr, hc = tile_rows + 2, tile_cols + 2
    above_in, below_in = exchange(
        payload(prolong[0], rel[0]), payload(prolong[tile_rows - 1], rel[tile_rows - 1]), "row")
    above, above_rel = unpack(above_in, tile_cols)
    below, below_rel = unpack(below_in, tile_cols)
    tall = jnp.concatenate([above[None], prolong, below[None]], axis=0)
    tall_rel = jnp.concatenate([above_rel[None], rel, below_rel[None]], axis=0)
    left_in, right_in = exchange(
        payload(tall[:, 0], tall_rel[:, 0]), payload(tall[:, tile_cols - 1], tall_rel[:, tile_cols - 1]), "col")
    left_rel = unpack(left_in, hr)[1]
    right_rel = unpack(right_in, hr)[1]
    near_rel = jnp.concatenate([left_rel[:, None], tall_rel, right_rel[:, None]], axis=1)

    off_r = (jnp.arange(hr, dtype=jnp.int32) + tile_rows - 1) // tile_rows - 1
    off_c = (jnp.arange(hc, dtype=jnp.int32) + tile_cols - 1) // tile_cols - 1
    base = (off_r[:, None, None] + 1) * WIN + off_c[None, :, None] + 1
    near_slot = jnp.minimum(near_rel + base, TRASH).reshape(hr * hc * KP)

    first_row = row_index * tile_rows
    first_col = col_index * tile_cols
    targets = fine_columns
    pos = (targets // grid_cols - first_row + 1) * hc + targets % grid_cols - first_col + 1
    pos = jnp.clip(pos, 0, hr * hc - 1)
    home = jnp.where(kept, home_rc, HOME * HOME)

    smem = pltpu.MemorySpace.SMEM
    vmem = pltpu.MemorySpace.VMEM
    width = WIN * WIN * B
    parity = jnp.stack([col_index % 2, row_index % 2]).astype(jnp.int32)
    keep, first, second = pl.pallas_call(
        galerkin_kernel,
        out_shape=(
            jax.ShapeDtypeStruct((HOME, B, width), jnp.float32),
            jax.ShapeDtypeStruct((HOME, B, width), SEND),
            jax.ShapeDtypeStruct((HOME, B, width), SEND),
        ),
        in_specs=[pl.BlockSpec(memory_space=smem)] * 5 + [pl.BlockSpec(memory_space=vmem)] * 6,
        out_specs=(pl.BlockSpec(memory_space=vmem),) * 3,
        scratch_shapes=[
            pltpu.VMEM((TRASH + 1, B, B), jnp.float32),
            pltpu.VMEM((patches * B, width), jnp.bfloat16),
            pltpu.VMEM(((HOME * HOME + 1) * B, patches * B), jnp.float32),
            pltpu.VMEM((hr * hc, B, KP * B), jnp.bfloat16),
        ],
    )(
        parity,
        pos.astype(jnp.int32),
        near_slot.astype(jnp.int32),
        fine_counts.astype(jnp.int32),
        home.astype(jnp.int32),
        fine_blocks.reshape(patches, B, KA * B),
        prolong.reshape(patches, B, KP * B),
        above_in,
        below_in,
        left_in,
        right_in,
    )
    got_a, got_b = swap_rounds(first, second, "col")
    band = WIN * OUTW * B
    first2, second2 = pl.pallas_call(
        fold_cols_send_kernel,
        out_shape=(
            jax.ShapeDtypeStruct((B, band), SEND),
            jax.ShapeDtypeStruct((B, band), SEND),
        ),
        in_specs=[pl.BlockSpec(memory_space=smem)] + [pl.BlockSpec(memory_space=vmem)] * 3,
        out_specs=(pl.BlockSpec(memory_space=vmem),) * 2,
    )(parity, keep, got_a, got_b)
    keep2 = pl.pallas_call(
        fold_cols_keep_kernel,
        out_shape=jax.ShapeDtypeStruct((B, OUTW * OUTW * B), jnp.float32),
        in_specs=[pl.BlockSpec(memory_space=smem)] + [pl.BlockSpec(memory_space=vmem)] * 3,
        out_specs=pl.BlockSpec(memory_space=vmem),
    )(parity, keep, got_a, got_b)
    row_a, row_b = swap_rounds(first2, second2, "row")
    out = pl.pallas_call(
        fold_rows_kernel,
        out_shape=jax.ShapeDtypeStruct((B, OUTW * OUTW * B), jnp.bfloat16),
        in_specs=[pl.BlockSpec(memory_space=smem)] + [pl.BlockSpec(memory_space=vmem)] * 3,
        out_specs=pl.BlockSpec(memory_space=vmem),
    )(parity, keep2, row_a, row_b)
    return out.reshape(1, 1, B, OUTW * OUTW * B)


def solution(mesh):
    in_specs = (
        P("row", "col", None, None),
        P("row", "col", None),
        P("row", "col"),
        P("row", "col", None, None),
        P("row", "col", None),
        P("row", "col"),
    )
    out_specs = P("row", "col", None, None)
    return jax.shard_map(
        per_device, mesh=mesh, in_specs=in_specs, out_specs=out_specs, check_vma=False
    )
```
